32 devices in a mesh: group: 2 (over x), chan: 16 (over z, y, core).
Axes of the slice: x: 2, y: 2, z: 4, core: 2. Of those that a mesh axis runs over, the one named last changes fastest.
Arguments:
- parent_state: float32 [32, 16, 16384], P('group', None, 'chan'), parts along dimension 0, may hold values from -6 to 6
- parent_conv: bfloat16 [32, 3, 16384], P('group', None, 'chan'), parts along dimension 0, may hold values from -6 to 6
- fork_map: int32 [32], P('group'), parts along dimension 0, may hold values from 0 to 15
- judge_lengths: int32 [32], P('group'), parts along dimension 0, may hold values from 1 to 16, 128 in all
- mixer_input: bfloat16 [32, 20, 16384], P('group', None, 'chan'), parts along dimension 0, may hold values from -6 to 6
- gate_input: bfloat16 [32, 20, 16384], P('group', None, 'chan'), parts along dimension 0, may hold values from -6 to 6
- conv_weight: bfloat16 [4, 16384], P(None, 'chan'), may hold values from -3 to 3
- conv_bias: float32 [16384], P('chan'), may hold values from -0.5 to 0.5
- rate_down: bfloat16 [16384, 512], P('chan'), may hold values from -0.046875 to 0.046875
- selection_weight: bfloat16 [16384, 32], P('chan'), may hold values from -0.046875 to 0.046875
- rate_up: bfloat16 [512, 16384], P(None, 'chan'), may hold values from -0.25 to 0.25
- rate_bias: float32 [16384], P('chan'), may hold values from -7 to -2.3
- decay_log: float32 [16, 16384], P(None, 'chan'), may hold values from 0 to 2.77
- skip_gain: float32 [16384], P('chan'), may hold values from 0.5 to 1.5
Outputs:
- mixer_output: bfloat16 [32, 20, 16384], P(('group', 'chan')), parts along dimension 0
- final_state: float32 [32, 16, 16384], P(('group', 'chan')), parts along dimension 0
The draws below stay inside these ranges and needn't reach their ends.
There are 2 independent parts, one for each index of `group`. The reference program is written for one: setup_inputs(seed, part) draws one part's arguments, and reference() takes and returns one part's arrays. A program takes and returns all parts, laid end to end along the dimension named above; an argument that names none is the same for every part. Nothing has to cross between parts.
Inputs may be any that keep to these rules, and one draw needn't show every extreme that they name: `fork_map`: index of the parent node a thought continues. `judge_lengths`: the lengths of one part sum to 128 and the longest is exactly 16.
All inputs are finite; a program needn't handle non-finite values.
Results may differ from the reference program's by a relative error of at most 0.0095.
Values may be sent and summed in bfloat16 or wider, within the bound.
No kernel may reach another device: no remote copies, remote signals or barrier semaphores. Data moves between devices by JAX's collectives and lax.ppermute only.
A program may use at most 128 MiB of HBM per device.

```python
import math
import jax
import jax.numpy as jnp
import numpy as np
from jax import lax

E = 16384
S = 16
R = 512
CONV = 4
PARENTS = 16
GEN = 4
JUDGE = 16
THOUGHTS = 16
TOK = 20


def touch_ends(values, key, low, top_value):
    longest = values.shape.index(max(values.shape))
    spots = []
    for shift in (0, 1):
        where = [jax.random.randint(jax.random.fold_in(key, axis), (), 0, length) for axis, length in enumerate(values.shape)]
        where[longest] = (where[longest] + shift) % values.shape[longest]
        spots.append(tuple(where))
    return values.at[spots[0]].set(low).at[spots[1]].set(top_value)


def shard_levels(rng, extent, cuts, least, largest):
    loudness, own = 1.0, jax.random.fold_in(rng, 6)
    for dim, parts in cuts:
        heights = jnp.exp(jax.random.uniform(jax.random.fold_in(own, dim), (parts,), jnp.float32, least / len(cuts), largest / len(cuts)))
        loudness = loudness * jnp.repeat(heights, extent[dim] // parts).reshape([-1 if axis == dim else 1 for axis in range(len(extent))])
    return loudness


def rank_table(count, lean):
    portions = [(1 << 20) // math.isqrt(grade ** lean) + 1 for grade in range(1, count + 1)]
    spread = 1 + sum(portions) // (1 << 30)
    return np.cumsum(np.array([max(1, weight // spread) for weight in portions]))


def skewed_ids(key, dims, number_of, slope):
    table = rank_table(number_of, slope)
    pick = jax.random.randint(jax.random.fold_in(key, 1), dims, 0, int(table[number_of - 1]))
    grade = jnp.searchsorted(jnp.asarray(table, jnp.int32), pick, side="right")
    return jax.random.permutation(jax.random.fold_in(key, 2), number_of)[grade].astype(jnp.int32)


def profile(amount, total, most, skew):
    loads = [(1 << 20) // math.isqrt(grade ** skew) + 1 for grade in range(2, amount + 1)]
    spare, counts = total - most - (amount - 1), [1] * (amount - 1)
    while spare > 0:
        candidates = [i for i in range(amount - 1) if counts[i] < most]
        pool, left = sum([loads[i] for i in candidates]), spare
        for i in candidates:
            more = min(most - counts[i], max(1, left * loads[i] // pool), spare)
            counts[i] = counts[i] + more
            spare = spare - more
    return np.array([most] + counts)


def uneven_parts(rng, number_of, total, reach, skew):
    if number_of == 2:
        one = jax.random.randint(rng, (), max(1, total - reach), min(reach, total - 1) + 1)
        return jnp.stack([one, total - one])
    lengths = jnp.asarray(profile(number_of, total, reach, skew), jnp.int32)
    couples = (number_of - 1) // 2
    giver, receiver = lengths[1:1 + 2 * couples:2], lengths[2:2 + 2 * couples:2]
    slack = jnp.minimum(giver - 1, reach - receiver)
    passed = jax.random.randint(jax.random.fold_in(rng, 1), (couples,), 0, 1 << 20) % (slack + 1)
    lengths = lengths.at[1:1 + 2 * couples:2].set(giver - passed).at[2:2 + 2 * couples:2].set(receiver + passed)
    return lengths[jax.random.permutation(jax.random.fold_in(rng, 2), number_of)]


def normal_values(key, dims, deviation, bound, split=(), kind=jnp.bfloat16):
    entries = deviation * jax.random.normal(key, dims, jnp.float32)
    if split:
        entries = entries * shard_levels(key, dims, split, -0.22, 0.18)
    return jnp.clip(entries, -bound, bound).astype(kind)


def setup_inputs(seed: int = 0, part: int = 0) -> dict:
    key_of = jax.random.split(jax.random.key(seed), 15)
    part_splits = jax.random.split(jax.random.fold_in(key_of[14], part), 15)
    return {
        "parent_state": normal_values(part_splits[0], (PARENTS, S, E), 1.0, 6.0, ((2, 16),), jnp.float32),
        "parent_conv": normal_values(part_splits[1], (PARENTS, CONV - 1, E), 1.0, 6.0, ((2, 16),)),
        "fork_map": touch_ends(skewed_ids(part_splits[2], (THOUGHTS,), PARENTS, 2), jax.random.fold_in(part_splits[2], 3), 0, PARENTS - 1).astype(jnp.int32),
        "judge_lengths": uneven_parts(part_splits[3], THOUGHTS, THOUGHTS * JUDGE // 2, JUDGE, 2).astype(jnp.int32),
        "mixer_input": normal_values(part_splits[4], (THOUGHTS, TOK, E), 1.0, 6.0, ((2, 16),)),
        "gate_input": normal_values(part_splits[5], (THOUGHTS, TOK, E), 1.0, 6.0, ((2, 16),)),
        "conv_weight": normal_values(key_of[6], (CONV, E), CONV ** -0.5, 3.0, ((1, 16),)),
        "conv_bias": jnp.clip(jax.random.uniform(key_of[7], (E,), jnp.float32, -0.5, 0.5) * shard_levels(key_of[7], (E,), ((0, 16),), -0.4, 0.0), -0.5, 0.5),
        "rate_down": normal_values(key_of[8], (E, R), E ** -0.5, 0.046875, ((0, 16),)),
        "selection_weight": normal_values(key_of[9], (E, 2 * S), E ** -0.5, 0.046875, ((0, 16),)),
        "rate_up": normal_values(key_of[10], (R, E), R ** -0.5, 0.25, ((1, 16),)),
        "rate_bias": jnp.clip(-7.0 + 4.7 * jax.random.uniform(key_of[11], (E,), jnp.float32) ** shard_levels(key_of[11], (E,), ((0, 16),), -0.2, 0.2), -7.0, -2.3),
        "decay_log": jnp.clip(2.77 * jax.random.uniform(key_of[12], (S, E), jnp.float32) ** shard_levels(key_of[12], (S, E), ((1, 16),), -0.2, 0.2), 0.0, 2.77),
        "skip_gain": jnp.clip(0.5 + 1.0 * jax.random.uniform(key_of[13], (E,), jnp.float32) ** shard_levels(key_of[13], (E,), ((0, 16),), -0.2, 0.2), 0.5, 1.5),
    }


def reference(parent_state, parent_conv, fork_map, judge_lengths, mixer_input, gate_input, conv_weight, conv_bias, rate_down, selection_weight, rate_up, rate_bias, decay_log, skip_gain):
    thought_count, positions, width_all = mixer_input.shape
    start_conv = jnp.take(parent_conv, fork_map, axis=0)
    padded = jnp.concatenate([start_conv, mixer_input], axis=1).astype(jnp.float32)
    tap_weights = conv_weight.astype(jnp.float32)
    summed = conv_bias[None, None, :] + tap_weights[0][None, None, :] * padded[:, 0:positions, :]
    for offset in range(1, CONV):
        summed = summed + tap_weights[offset][None, None, :] * padded[:, offset:offset + positions, :]
    driven = jax.nn.silu(summed).astype(jnp.bfloat16)
    token_rows = driven.reshape(thought_count * positions, width_all)
    rate_low = jnp.dot(token_rows, rate_down, preferred_element_type=jnp.float32).astype(jnp.bfloat16)
    selection = jnp.dot(token_rows, selection_weight, preferred_element_type=jnp.float32)
    step_rate = jax.nn.softplus(jnp.dot(rate_low, rate_up, preferred_element_type=jnp.float32) + rate_bias[None, :])
    position = lax.broadcasted_iota(jnp.int32, (thought_count, positions), 1)
    live_mask = position < (GEN + judge_lengths)[:, None]
    step_rate = step_rate.reshape(thought_count, positions, width_all) * live_mask[:, :, None].astype(jnp.float32)
    selection = selection.reshape(thought_count, positions, 2 * S)
    decay_rate = -jnp.exp(decay_log)
    start_state = jnp.take(parent_state, fork_map, axis=0)

    def advance(carried, pieces):
        drive_rows, gate_rows, rate_rows, select_rows, alive_rows = pieces
        inflow = drive_rows.astype(jnp.float32)
        factor = jnp.exp(rate_rows[:, None, :] * decay_rate[None, :, :])
        push_term = (rate_rows * inflow)[:, None, :] * select_rows[:, :S, None]
        carried = factor * carried + push_term
        readout = jnp.sum(select_rows[:, S:, None] * carried, axis=1)
        result = (readout + skip_gain[None, :] * inflow) * jax.nn.silu(gate_rows.astype(jnp.float32))
        result = jnp.where(alive_rows[:, None], result, 0.0).astype(jnp.bfloat16)
        return carried, result

    final_state, outputs = lax.scan(advance, start_state, (jnp.swapaxes(driven, 0, 1), jnp.swapaxes(gate_input, 0, 1), jnp.swapaxes(step_rate, 0, 1), jnp.swapaxes(selection, 0, 1), jnp.swapaxes(live_mask, 0, 1)))
    return jnp.swapaxes(outputs, 0, 1), final_state
```

```python
import functools

import jax
import jax.numpy as jnp
from jax import lax
from jax.experimental import pallas as pl
from jax.experimental.pallas import tpu as pltpu
from jax.sharding import PartitionSpec as P

GEN = 4


def convolve(parent_conv, fork_map, mixer_input, conv_weight, conv_bias):
    positions = mixer_input.shape[1]
    start_conv = jnp.take(parent_conv, fork_map, axis=0)
    padded = jnp.concatenate([start_conv, mixer_input], axis=1).astype(jnp.float32)
    tap_weights = conv_weight.astype(jnp.float32)
    summed = conv_bias[None, None, :] + tap_weights[0][None, None, :] * padded[:, 0:positions, :]
    for offset in range(1, conv_weight.shape[0]):
        summed = (
            summed + tap_weights[offset][None, None, :] * padded[:, offset : offset + positions, :]
        )
    return jax.nn.silu(summed).astype(jnp.bfloat16)


def scan_kernel(
    lens_ref, fmap_ref, rate_ref, drive_ref, gate_ref, b_ref, c_ref, h0_ref, a_ref, skip_ref,
    out_ref, hT_ref, u_scr, y_scr, *, width
):
    t = pl.program_id(0)
    positions = rate_ref.shape[1]
    state_size, width_local = h0_ref.shape[1], h0_ref.shape[2]
    live = jnp.clip(lens_ref[t] + GEN, 0, positions)
    inflow = drive_ref[0].astype(jnp.float32)
    u_scr[...] = rate_ref[0] * inflow
    b_all = b_ref[0]
    c_all = c_ref[0]
    lane = lax.broadcasted_iota(jnp.int32, b_all.shape, 1)
    for chunk in range(width_local // width):
        cols = pl.ds(chunk * width, width)
        decay = a_ref[:, cols]

        def step(p, h):
            pick = lane == p
            b_col = jnp.sum(jnp.where(pick, b_all, 0.0), axis=1, keepdims=True)
            c_col = jnp.sum(jnp.where(pick, c_all, 0.0), axis=1, keepdims=True)
            rate_row = rate_ref[0, pl.ds(p, 1), cols]
            push_row = u_scr[pl.ds(p, 1), cols]
            h = jnp.exp(rate_row * decay) * h + push_row * b_col
            y_scr[pl.ds(p, 1), cols] = jnp.sum(c_col * h, axis=0, keepdims=True)
            return h

        h = lax.fori_loop(0, live, step, h0_ref[0, :, cols])
        hT_ref[0, :, cols] = h
    gate = gate_ref[0].astype(jnp.float32)
    result = (y_scr[...] + skip_ref[...] * inflow) * jax.nn.silu(gate)
    row = lax.broadcasted_iota(jnp.int32, result.shape, 0)
    out_ref[0] = jnp.where(row < live, result, 0.0).astype(out_ref.dtype)


def run_scan(judge_lengths, fork_map, step_rate, driven, gate_input, b_t, c_t, parent_state,
             decay_rate, skip_gain):
    thought_count, positions, width_local = driven.shape
    state_size = parent_state.shape[1]
    width = min(512, width_local)
    kernel = functools.partial(scan_kernel, width=width)
    row_block = lambda t, lens, fmap: (t, 0, 0)
    grid_spec = pltpu.PrefetchScalarGridSpec(
        num_scalar_prefetch=2,
        grid=(thought_count,),
        in_specs=[
            pl.BlockSpec((1, positions, width_local), row_block),
            pl.BlockSpec((1, positions, width_local), row_block),
            pl.BlockSpec((1, positions, width_local), row_block),
            pl.BlockSpec((1, state_size, positions), row_block),
            pl.BlockSpec((1, state_size, positions), row_block),
            pl.BlockSpec((1, state_size, width_local), lambda t, lens, fmap: (fmap[t], 0, 0)),
            pl.BlockSpec((state_size, width_local), lambda t, lens, fmap: (0, 0)),
            pl.BlockSpec((1, width_local), lambda t, lens, fmap: (0, 0)),
        ],
        out_specs=[
            pl.BlockSpec((1, positions, width_local), row_block),
            pl.BlockSpec((1, state_size, width_local), row_block),
        ],
        scratch_shapes=[
            pltpu.VMEM((positions, width_local), jnp.float32),
            pltpu.VMEM((positions, width_local), jnp.float32),
        ],
    )
    return pl.pallas_call(
        kernel,
        grid_spec=grid_spec,
        out_shape=(
            jax.ShapeDtypeStruct((thought_count, positions, width_local), jnp.bfloat16),
            jax.ShapeDtypeStruct((thought_count, state_size, width_local), jnp.float32),
        ),
        compiler_params=pltpu.CompilerParams(dimension_semantics=("arbitrary",)),
    )(judge_lengths, fork_map, step_rate, driven, gate_input, b_t, c_t, parent_state,
      decay_rate, skip_gain.reshape(1, width_local))


def body(
    parent_state,
    parent_conv,
    fork_map,
    judge_lengths,
    mixer_input,
    gate_input,
    conv_weight,
    conv_bias,
    rate_down,
    selection_weight,
    rate_up,
    rate_bias,
    decay_log,
    skip_gain,
):
    thought_count, positions, width_local = mixer_input.shape
    state_size = parent_state.shape[1]
    rank = rate_down.shape[1]
    driven = convolve(parent_conv, fork_map, mixer_input, conv_weight, conv_bias)
    token_rows = driven.reshape(thought_count * positions, width_local)
    low_part = jnp.dot(token_rows, rate_down, preferred_element_type=jnp.float32)
    select_part = jnp.dot(token_rows, selection_weight, preferred_element_type=jnp.float32)
    summed = lax.psum(jnp.concatenate([low_part, select_part], axis=1), "chan")
    rate_low = summed[:, :rank].astype(jnp.bfloat16)
    selection = summed[:, rank:].reshape(thought_count, positions, 2 * state_size)
    step_rate = jax.nn.softplus(
        jnp.dot(rate_low, rate_up, preferred_element_type=jnp.float32) + rate_bias[None, :]
    ).reshape(thought_count, positions, width_local)
    b_t = jnp.swapaxes(selection[:, :, :state_size], 1, 2)
    c_t = jnp.swapaxes(selection[:, :, state_size:], 1, 2)
    decay_rate = -jnp.exp(decay_log)
    out_local, state_local = run_scan(
        judge_lengths, fork_map, step_rate, driven, gate_input, b_t, c_t, parent_state,
        decay_rate, skip_gain,
    )
    mixer_output = lax.all_to_all(out_local, "chan", split_axis=0, concat_axis=2, tiled=True)
    final_state = lax.all_to_all(state_local, "chan", split_axis=0, concat_axis=2, tiled=True)
    return (mixer_output, final_state)


def solution(mesh):
    placed = (
        P("group", None, "chan"),
        P("group", None, "chan"),
        P("group"),
        P("group"),
        P("group", None, "chan"),
        P("group", None, "chan"),
        P(None, "chan"),
        P("chan"),
        P("chan", None),
        P("chan", None),
        P(None, "chan"),
        P("chan"),
        P(None, "chan"),
        P("chan"),
    )
    return jax.shard_map(
        body,
        mesh=mesh,
        in_specs=placed,
        out_specs=(P(("group", "chan"), None, None), P(("group", "chan"), None, None)),
        check_vma=False,
    )
```

```python
import functools

import jax
import jax.numpy as jnp
from jax import lax
from jax.experimental import pallas as pl
from jax.experimental.pallas import tpu as pltpu
from jax.sharding import PartitionSpec as P

GEN = 4


def convolve(parent_conv, fork_map, mixer_input, conv_weight, conv_bias):
    positions = mixer_input.shape[1]
    start_conv = jnp.take(parent_conv, fork_map, axis=0)
    padded = jnp.concatenate([start_conv, mixer_input], axis=1).astype(jnp.float32)
    tap_weights = conv_weight.astype(jnp.float32)
    summed = conv_bias[None, None, :] + tap_weights[0][None, None, :] * padded[:, 0:positions, :]
    for offset in range(1, conv_weight.shape[0]):
        summed = (
            summed + tap_weights[offset][None, None, :] * padded[:, offset : offset + positions, :]
        )
    return jax.nn.silu(summed).astype(jnp.bfloat16)


def scan_kernel(
    lens_ref, fmap_ref, rate_ref, drive_ref, gate_ref, b_ref, c_ref, h0_ref, a_ref, skip_ref,
    out_ref, hT_ref, u_scr, y_scr, *, width
):
    t = pl.program_id(0)
    positions = rate_ref.shape[1]
    state_size, width_local = h0_ref.shape[1], h0_ref.shape[2]
    live = jnp.clip(lens_ref[t] + GEN, 0, positions)
    inflow = drive_ref[0].astype(jnp.float32)
    u_scr[...] = rate_ref[0] * inflow
    b_all = b_ref[0]
    c_all = c_ref[0]
    lane = lax.broadcasted_iota(jnp.int32, b_all.shape, 1)
    for chunk in range(width_local // width):
        cols = pl.ds(chunk * width, width)
        decay = a_ref[:, cols]

        def step(p, h):
            pick = lane == p
            b_col = jnp.sum(jnp.where(pick, b_all, 0.0), axis=1, keepdims=True)
            c_col = jnp.sum(jnp.where(pick, c_all, 0.0), axis=1, keepdims=True)
            rate_row = rate_ref[0, pl.ds(p, 1), cols]
            push_row = u_scr[pl.ds(p, 1), cols]
            h = jnp.exp(rate_row * decay) * h + push_row * b_col
            y_scr[pl.ds(p, 1), cols] = jnp.sum(c_col * h, axis=0, keepdims=True)
            return h

        h = lax.fori_loop(0, live, step, h0_ref[0, :, cols])
        hT_ref[0, :, cols] = h
    gate = gate_ref[0].astype(jnp.float32)
    result = (y_scr[...] + skip_ref[...] * inflow) * jax.nn.silu(gate)
    row = lax.broadcasted_iota(jnp.int32, result.shape, 0)
    out_ref[0] = jnp.where(row < live, result, 0.0).astype(out_ref.dtype)


def run_scan(judge_lengths, fork_map, step_rate, driven, gate_input, b_t, c_t, parent_state,
             decay_rate, skip_gain):
    thought_count, positions, width_local = driven.shape
    state_size = parent_state.shape[1]
    width = min(512, width_local)
    kernel = functools.partial(scan_kernel, width=width)
    row_block = lambda t, lens, fmap: (t, 0, 0)
    grid_spec = pltpu.PrefetchScalarGridSpec(
        num_scalar_prefetch=2,
        grid=(thought_count,),
        in_specs=[
            pl.BlockSpec((1, positions, width_local), row_block),
            pl.BlockSpec((1, positions, width_local), row_block),
            pl.BlockSpec((1, positions, width_local), row_block),
            pl.BlockSpec((1, state_size, positions), row_block),
            pl.BlockSpec((1, state_size, positions), row_block),
            pl.BlockSpec((1, state_size, width_local), lambda t, lens, fmap: (fmap[t], 0, 0)),
            pl.BlockSpec((state_size, width_local), lambda t, lens, fmap: (0, 0)),
            pl.BlockSpec((1, width_local), lambda t, lens, fmap: (0, 0)),
        ],
        out_specs=[
            pl.BlockSpec((1, positions, width_local), row_block),
            pl.BlockSpec((1, state_size, width_local), row_block),
        ],
        scratch_shapes=[
            pltpu.VMEM((positions, width_local), jnp.float32),
            pltpu.VMEM((positions, width_local), jnp.float32),
        ],
    )
    return pl.pallas_call(
        kernel,
        grid_spec=grid_spec,
        out_shape=(
            jax.ShapeDtypeStruct((thought_count, positions, width_local), jnp.bfloat16),
            jax.ShapeDtypeStruct((thought_count, state_size, width_local), jnp.float32),
        ),
        compiler_params=pltpu.CompilerParams(dimension_semantics=("arbitrary",)),
    )(judge_lengths, fork_map, step_rate, driven, gate_input, b_t, c_t, parent_state,
      decay_rate, skip_gain.reshape(1, width_local))


def body(
    parent_state,
    parent_conv,
    fork_map,
    judge_lengths,
    mixer_input,
    gate_input,
    conv_weight,
    conv_bias,
    rate_down,
    selection_weight,
    rate_up,
    rate_bias,
    decay_log,
    skip_gain,
):
    thought_count, positions, width_local = mixer_input.shape
    state_size = parent_state.shape[1]
    rank = rate_down.shape[1]
    driven = convolve(parent_conv, fork_map, mixer_input, conv_weight, conv_bias)
    token_rows = driven.reshape(thought_count * positions, width_local)
    low_part = jnp.dot(token_rows, rate_down, preferred_element_type=jnp.float32)
    select_part = jnp.dot(token_rows, selection_weight, preferred_element_type=jnp.float32)
    partial = jnp.concatenate([low_part, select_part], axis=1)
    devices = lax.axis_size("chan")
    pieces = lax.all_to_all(
        partial.reshape(devices, -1, partial.shape[1]), "chan", 0, 0, tiled=True
    )
    summed = lax.all_gather(jnp.sum(pieces, axis=0), "chan", axis=0, tiled=True)
    rate_low = summed[:, :rank].astype(jnp.bfloat16)
    selection = summed[:, rank:].reshape(thought_count, positions, 2 * state_size)
    step_rate = jax.nn.softplus(
        jnp.dot(rate_low, rate_up, preferred_element_type=jnp.float32) + rate_bias[None, :]
    ).reshape(thought_count, positions, width_local)
    b_t = jnp.swapaxes(selection[:, :, :state_size], 1, 2)
    c_t = jnp.swapaxes(selection[:, :, state_size:], 1, 2)
    decay_rate = -jnp.exp(decay_log)
    out_local, state_local = run_scan(
        judge_lengths, fork_map, step_rate, driven, gate_input, b_t, c_t, parent_state,
        decay_rate, skip_gain,
    )
    mixer_output = lax.all_to_all(out_local, "chan", split_axis=0, concat_axis=2, tiled=True)
    final_state = lax.all_to_all(state_local, "chan", split_axis=0, concat_axis=2, tiled=True)
    return (mixer_output, final_state)


def solution(mesh):
    placed = (
        P("group", None, "chan"),
        P("group", None, "chan"),
        P("group"),
        P("group"),
        P("group", None, "chan"),
        P("group", None, "chan"),
        P(None, "chan"),
        P("chan"),
        P("chan", None),
        P("chan", None),
        P(None, "chan"),
        P("chan"),
        P(None, "chan"),
        P("chan"),
    )
    return jax.shard_map(
        body,
        mesh=mesh,
        in_specs=placed,
        out_specs=(P(("group", "chan"), None, None), P(("group", "chan"), None, None)),
        check_vma=False,
    )
```

```python
import functools

import jax
import jax.numpy as jnp
from jax import lax
from jax.experimental import pallas as pl
from jax.experimental.pallas import tpu as pltpu
from jax.sharding import PartitionSpec as P

GEN = 4


def convolve(parent_conv, fork_map, mixer_input, conv_weight, conv_bias):
    positions = mixer_input.shape[1]
    start_conv = jnp.take(parent_conv, fork_map, axis=0)
    padded = jnp.concatenate([start_conv, mixer_input], axis=1).astype(jnp.float32)
    tap_weights = conv_weight.astype(jnp.float32)
    summed = conv_bias[None, None, :] + tap_weights[0][None, None, :] * padded[:, 0:positions, :]
    for offset in range(1, conv_weight.shape[0]):
        summed = (
            summed + tap_weights[offset][None, None, :] * padded[:, offset : offset + positions, :]
        )
    return jax.nn.silu(summed).astype(jnp.bfloat16)


def scan_kernel(
    lens_ref, fmap_ref, rate_ref, drive_ref, gate_ref, b_ref, c_ref, h0_ref, a_ref, skip_ref,
    packed_ref, u_scr, y_scr, *, width
):
    t = pl.program_id(0)
    positions = rate_ref.shape[1]
    state_size, width_local = h0_ref.shape[1], h0_ref.shape[2]
    live = jnp.clip(lens_ref[t] + GEN, 0, positions)
    inflow = drive_ref[0].astype(jnp.float32)
    u_scr[...] = rate_ref[0] * inflow
    b_all = b_ref[0]
    c_all = c_ref[0]
    lane = lax.broadcasted_iota(jnp.int32, b_all.shape, 1)
    for chunk in range(width_local // width):
        cols = pl.ds(chunk * width, width)
        decay = a_ref[:, cols]

        def step(p, h):
            pick = lane == p
            b_col = jnp.sum(jnp.where(pick, b_all, 0.0), axis=1, keepdims=True)
            c_col = jnp.sum(jnp.where(pick, c_all, 0.0), axis=1, keepdims=True)
            rate_row = rate_ref[0, pl.ds(p, 1), cols]
            push_row = u_scr[pl.ds(p, 1), cols]
            h = jnp.exp(rate_row * decay) * h + push_row * b_col
            y_scr[pl.ds(p, 1), cols] = jnp.sum(c_col * h, axis=0, keepdims=True)
            return h

        h = lax.fori_loop(0, live, step, h0_ref[0, :, cols])
        packed_ref[0, :state_size, cols] = h.astype(packed_ref.dtype)
    gate = gate_ref[0].astype(jnp.float32)
    result = (y_scr[...] + skip_ref[...] * inflow) * jax.nn.silu(gate)
    row = lax.broadcasted_iota(jnp.int32, result.shape, 0)
    packed_ref[0, state_size:, :] = jnp.where(row < live, result, 0.0).astype(packed_ref.dtype)


def run_scan(judge_lengths, fork_map, step_rate, driven, gate_input, b_t, c_t, parent_state,
             decay_rate, skip_gain):
    thought_count, positions, width_local = driven.shape
    state_size = parent_state.shape[1]
    width = min(512, width_local)
    kernel = functools.partial(scan_kernel, width=width)
    row_block = lambda t, lens, fmap: (t, 0, 0)
    grid_spec = pltpu.PrefetchScalarGridSpec(
        num_scalar_prefetch=2,
        grid=(thought_count,),
        in_specs=[
            pl.BlockSpec((1, positions, width_local), row_block),
            pl.BlockSpec((1, positions, width_local), row_block),
            pl.BlockSpec((1, positions, width_local), row_block),
            pl.BlockSpec((1, state_size, positions), row_block),
            pl.BlockSpec((1, state_size, positions), row_block),
            pl.BlockSpec((1, state_size, width_local), lambda t, lens, fmap: (fmap[t], 0, 0)),
            pl.BlockSpec((state_size, width_local), lambda t, lens, fmap: (0, 0)),
            pl.BlockSpec((1, width_local), lambda t, lens, fmap: (0, 0)),
        ],
        out_specs=pl.BlockSpec((1, state_size + positions, width_local), row_block),
        scratch_shapes=[
            pltpu.VMEM((positions, width_local), jnp.float32),
            pltpu.VMEM((positions, width_local), jnp.float32),
        ],
    )
    return pl.pallas_call(
        kernel,
        grid_spec=grid_spec,
        out_shape=jax.ShapeDtypeStruct(
            (thought_count, state_size + positions, width_local), jnp.bfloat16
        ),
        compiler_params=pltpu.CompilerParams(dimension_semantics=("arbitrary",)),
    )(judge_lengths, fork_map, step_rate, driven, gate_input, b_t, c_t, parent_state,
      decay_rate, skip_gain.reshape(1, width_local))


def body(
    parent_state,
    parent_conv,
    fork_map,
    judge_lengths,
    mixer_input,
    gate_input,
    conv_weight,
    conv_bias,
    rate_down,
    selection_weight,
    rate_up,
    rate_bias,
    decay_log,
    skip_gain,
):
    thought_count, positions, width_local = mixer_input.shape
    state_size = parent_state.shape[1]
    rank = rate_down.shape[1]
    driven = convolve(parent_conv, fork_map, mixer_input, conv_weight, conv_bias)
    token_rows = driven.reshape(thought_count * positions, width_local)
    low_part = jnp.dot(token_rows, rate_down, preferred_element_type=jnp.float32)
    select_part = jnp.dot(token_rows, selection_weight, preferred_element_type=jnp.float32)
    partial = jnp.concatenate([low_part, select_part], axis=1)
    devices = lax.axis_size("chan")
    pieces = lax.all_to_all(
        partial.reshape(devices, -1, partial.shape[1]), "chan", 0, 0, tiled=True
    )
    reduced = jnp.sum(pieces, axis=0)
    low_mine = reduced[:, :rank].astype(jnp.bfloat16)
    select_high = reduced[:, rank:].astype(jnp.bfloat16)
    select_low = (reduced[:, rank:] - select_high.astype(jnp.float32)).astype(jnp.bfloat16)
    gathered = lax.all_gather(
        jnp.concatenate([low_mine, select_high, select_low], axis=1), "chan", axis=0, tiled=True
    )
    rate_low = gathered[:, :rank]
    selection = (
        gathered[:, rank : rank + 2 * state_size].astype(jnp.float32)
        + gathered[:, rank + 2 * state_size :].astype(jnp.float32)
    ).reshape(thought_count, positions, 2 * state_size)
    step_rate = jax.nn.softplus(
        jnp.dot(rate_low, rate_up, preferred_element_type=jnp.float32) + rate_bias[None, :]
    ).reshape(thought_count, positions, width_local)
    b_t = jnp.swapaxes(selection[:, :, :state_size], 1, 2)
    c_t = jnp.swapaxes(selection[:, :, state_size:], 1, 2)
    decay_rate = -jnp.exp(decay_log)
    packed_local = run_scan(
        judge_lengths, fork_map, step_rate, driven, gate_input, b_t, c_t, parent_state,
        decay_rate, skip_gain,
    )
    packed = lax.all_to_all(packed_local, "chan", split_axis=0, concat_axis=2, tiled=True)
    final_state = packed[:, :state_size].astype(jnp.float32)
    mixer_output = packed[:, state_size:]
    return (mixer_output, final_state)


def solution(mesh):
    placed = (
        P("group", None, "chan"),
        P("group", None, "chan"),
        P("group"),
        P("group"),
        P("group", None, "chan"),
        P("group", None, "chan"),
        P(None, "chan"),
        P("chan"),
        P("chan", None),
        P("chan", None),
        P(None, "chan"),
        P("chan"),
        P(None, "chan"),
        P("chan"),
    )
    return jax.shard_map(
        body,
        mesh=mesh,
        in_specs=placed,
        out_specs=(P(("group", "chan"), None, None), P(("group", "chan"), None, None)),
        check_vma=False,
    )
```

```python
import jax
import jax.numpy as jnp
from jax import lax
from jax.experimental import pallas as pl
from jax.experimental.pallas import tpu as pltpu
from jax.sharding import PartitionSpec as P

GEN = 4


def convolve(parent_conv, fork_map, mixer_input, conv_weight, conv_bias):
    positions = mixer_input.shape[1]
    start_conv = jnp.take(parent_conv, fork_map, axis=0)
    padded = jnp.concatenate([start_conv, mixer_input], axis=1).astype(jnp.float32)
    tap_weights = conv_weight.astype(jnp.float32)
    summed = conv_bias[None, None, :] + tap_weights[0][None, None, :] * padded[:, 0:positions, :]
    for offset in range(1, conv_weight.shape[0]):
        summed = (
            summed + tap_weights[offset][None, None, :] * padded[:, offset : offset + positions, :]
        )
    return jax.nn.silu(summed).astype(jnp.bfloat16)


def scan_kernel(
    lens_ref, fmap_ref, rate_ref, drive_ref, gate_ref, b_ref, c_ref, h0_ref, a_ref, skip_ref,
    packed_ref, r_scr, u_scr, y_scr
):
    t = pl.program_id(0)
    positions = rate_ref.shape[1]
    state_size = h0_ref.shape[1]
    live = jnp.clip(lens_ref[t] + GEN, 0, positions)
    inflow = drive_ref[0].astype(jnp.float32)
    alive = lax.broadcasted_iota(jnp.int32, inflow.shape, 0) < live
    rate = jnp.where(alive, rate_ref[0], 0.0)
    r_scr[...] = rate
    u_scr[...] = rate * inflow
    b_all = b_ref[0]
    c_all = c_ref[0]
    decay = a_ref[...]
    h = h0_ref[0]
    for p in range(positions):
        h = jnp.exp(r_scr[p : p + 1, :] * decay) * h + u_scr[p : p + 1, :] * b_all[:, p : p + 1]
        y_scr[p : p + 1, :] = jnp.sum(c_all[:, p : p + 1] * h, axis=0, keepdims=True)
    packed_ref[0, :state_size, :] = h.astype(packed_ref.dtype)
    gate = gate_ref[0].astype(jnp.float32)
    result = (y_scr[...] + skip_ref[...] * inflow) * jax.nn.silu(gate)
    packed_ref[0, state_size:, :] = jnp.where(alive, result, 0.0).astype(packed_ref.dtype)


def run_scan(judge_lengths, fork_map, step_rate, driven, gate_input, b_t, c_t, parent_state,
             decay_rate, skip_gain):
    thought_count, positions, width_local = driven.shape
    state_size = parent_state.shape[1]
    kernel = scan_kernel
    row_block = lambda t, lens, fmap: (t, 0, 0)
    grid_spec = pltpu.PrefetchScalarGridSpec(
        num_scalar_prefetch=2,
        grid=(thought_count,),
        in_specs=[
            pl.BlockSpec((1, positions, width_local), row_block),
            pl.BlockSpec((1, positions, width_local), row_block),
            pl.BlockSpec((1, positions, width_local), row_block),
            pl.BlockSpec((1, state_size, positions), row_block),
            pl.BlockSpec((1, state_size, positions), row_block),
            pl.BlockSpec((1, state_size, width_local), lambda t, lens, fmap: (fmap[t], 0, 0)),
            pl.BlockSpec((state_size, width_local), lambda t, lens, fmap: (0, 0)),
            pl.BlockSpec((1, width_local), lambda t, lens, fmap: (0, 0)),
        ],
        out_specs=pl.BlockSpec((1, state_size + positions, width_local), row_block),
        scratch_shapes=[pltpu.VMEM((positions, width_local), jnp.float32)] * 3,
    )
    return pl.pallas_call(
        kernel,
        grid_spec=grid_spec,
        out_shape=jax.ShapeDtypeStruct(
            (thought_count, state_size + positions, width_local), jnp.bfloat16
        ),
        compiler_params=pltpu.CompilerParams(dimension_semantics=("arbitrary",)),
    )(judge_lengths, fork_map, step_rate, driven, gate_input, b_t, c_t, parent_state,
      decay_rate, skip_gain.reshape(1, width_local))


def body(
    parent_state,
    parent_conv,
    fork_map,
    judge_lengths,
    mixer_input,
    gate_input,
    conv_weight,
    conv_bias,
    rate_down,
    selection_weight,
    rate_up,
    rate_bias,
    decay_log,
    skip_gain,
):
    thought_count, positions, width_local = mixer_input.shape
    state_size = parent_state.shape[1]
    rank = rate_down.shape[1]
    driven = convolve(parent_conv, fork_map, mixer_input, conv_weight, conv_bias)
    token_rows = driven.reshape(thought_count * positions, width_local)
    low_part = jnp.dot(token_rows, rate_down, preferred_element_type=jnp.float32)
    select_part = jnp.dot(token_rows, selection_weight, preferred_element_type=jnp.float32)
    partial = jnp.concatenate([low_part, select_part], axis=1)
    devices = lax.axis_size("chan")
    pieces = lax.all_to_all(
        partial.reshape(devices, -1, partial.shape[1]), "chan", 0, 0, tiled=True
    )
    reduced = jnp.sum(pieces, axis=0)
    low_mine = reduced[:, :rank].astype(jnp.bfloat16)
    select_high = reduced[:, rank:].astype(jnp.bfloat16)
    select_low = (reduced[:, rank:] - select_high.astype(jnp.float32)).astype(jnp.bfloat16)
    gathered = lax.all_gather(
        jnp.concatenate([low_mine, select_high, select_low], axis=1), "chan", axis=0, tiled=True
    )
    rate_low = gathered[:, :rank]
    selection = (
        gathered[:, rank : rank + 2 * state_size].astype(jnp.float32)
        + gathered[:, rank + 2 * state_size :].astype(jnp.float32)
    ).reshape(thought_count, positions, 2 * state_size)
    step_rate = jax.nn.softplus(
        jnp.dot(rate_low, rate_up, preferred_element_type=jnp.float32) + rate_bias[None, :]
    ).reshape(thought_count, positions, width_local)
    b_t = jnp.swapaxes(selection[:, :, :state_size], 1, 2)
    c_t = jnp.swapaxes(selection[:, :, state_size:], 1, 2)
    decay_rate = -jnp.exp(decay_log)
    packed_local = run_scan(
        judge_lengths, fork_map, step_rate, driven, gate_input, b_t, c_t, parent_state,
        decay_rate, skip_gain,
    )
    packed = lax.all_to_all(packed_local, "chan", split_axis=0, concat_axis=2, tiled=True)
    final_state = packed[:, :state_size].astype(jnp.float32)
    mixer_output = packed[:, state_size:]
    return (mixer_output, final_state)


def solution(mesh):
    placed = (
        P("group", None, "chan"),
        P("group", None, "chan"),
        P("group"),
        P("group"),
        P("group", None, "chan"),
        P("group", None, "chan"),
        P(None, "chan"),
        P("chan"),
        P("chan", None),
        P("chan", None),
        P(None, "chan"),
        P("chan"),
        P(None, "chan"),
        P("chan"),
    )
    return jax.shard_map(
        body,
        mesh=mesh,
        in_specs=placed,
        out_specs=(P(("group", "chan"), None, None), P(("group", "chan"), None, None)),
        check_vma=False,
    )
```

```python
import jax
import jax.numpy as jnp
from jax import lax
from jax.experimental import pallas as pl
from jax.experimental.pallas import tpu as pltpu
from jax.sharding import PartitionSpec as P

GEN = 4


def convolve(parent_conv, fork_map, mixer_input, conv_weight, conv_bias):
    positions = mixer_input.shape[1]
    start_conv = jnp.take(parent_conv, fork_map, axis=0)
    padded = jnp.concatenate([start_conv, mixer_input], axis=1).astype(jnp.float32)
    tap_weights = conv_weight.astype(jnp.float32)
    summed = conv_bias[None, None, :] + tap_weights[0][None, None, :] * padded[:, 0:positions, :]
    for offset in range(1, conv_weight.shape[0]):
        summed = (
            summed + tap_weights[offset][None, None, :] * padded[:, offset : offset + positions, :]
        )
    return jax.nn.silu(summed).astype(jnp.bfloat16)


def scan_kernel(
    lens_ref, fmap_ref, rate_ref, drive_ref, gate_ref, b_ref, c_ref, h0_ref, a_ref, skip_ref,
    packed_ref, r_scr, u_scr, y_scr
):
    t = pl.program_id(0)
    positions = rate_ref.shape[1]
    state_size = h0_ref.shape[1]
    live = jnp.clip(lens_ref[t] + GEN, 0, positions)
    inflow = drive_ref[0].astype(jnp.float32)
    alive = lax.broadcasted_iota(jnp.int32, inflow.shape, 0) < live
    rate = jnp.where(alive, rate_ref[0], 0.0)
    r_scr[...] = rate
    u_scr[...] = rate * inflow
    b_all = b_ref[0]
    c_all = c_ref[0]
    decay = a_ref[...]
    h = h0_ref[0]
    for p in range(positions):
        h = jnp.exp(r_scr[p : p + 1, :] * decay) * h + u_scr[p : p + 1, :] * b_all[:, p : p + 1]
        y_scr[p : p + 1, :] = jnp.sum(c_all[:, p : p + 1] * h, axis=0, keepdims=True)
    packed_ref[0, :state_size, :] = h.astype(packed_ref.dtype)
    gate = gate_ref[0].astype(jnp.float32)
    result = (y_scr[...] + skip_ref[...] * inflow) * jax.nn.silu(gate)
    packed_ref[0, state_size:, :] = jnp.where(alive, result, 0.0).astype(packed_ref.dtype)


def run_scan(judge_lengths, fork_map, step_rate, driven, gate_input, b_t, c_t, parent_state,
             decay_rate, skip_gain):
    thought_count, positions, width_local = driven.shape
    state_size = parent_state.shape[1]
    kernel = scan_kernel
    row_block = lambda t, lens, fmap: (t, 0, 0)
    grid_spec = pltpu.PrefetchScalarGridSpec(
        num_scalar_prefetch=2,
        grid=(thought_count,),
        in_specs=[
            pl.BlockSpec((1, positions, width_local), row_block),
            pl.BlockSpec((1, positions, width_local), row_block),
            pl.BlockSpec((1, positions, width_local), row_block),
            pl.BlockSpec((1, state_size, positions), row_block),
            pl.BlockSpec((1, state_size, positions), row_block),
            pl.BlockSpec((1, state_size, width_local), lambda t, lens, fmap: (fmap[t], 0, 0)),
            pl.BlockSpec((state_size, width_local), lambda t, lens, fmap: (0, 0)),
            pl.BlockSpec((1, width_local), lambda t, lens, fmap: (0, 0)),
        ],
        out_specs=pl.BlockSpec((1, state_size + positions, width_local), row_block),
        scratch_shapes=[pltpu.VMEM((positions, width_local), jnp.float32)] * 3,
    )
    return pl.pallas_call(
        kernel,
        grid_spec=grid_spec,
        out_shape=jax.ShapeDtypeStruct(
            (thought_count, state_size + positions, width_local), jnp.bfloat16
        ),
        compiler_params=pltpu.CompilerParams(dimension_semantics=("arbitrary",)),
    )(judge_lengths, fork_map, step_rate, driven, gate_input, b_t, c_t, parent_state,
      decay_rate, skip_gain.reshape(1, width_local))


def body(
    parent_state,
    parent_conv,
    fork_map,
    judge_lengths,
    mixer_input,
    gate_input,
    conv_weight,
    conv_bias,
    rate_down,
    selection_weight,
    rate_up,
    rate_bias,
    decay_log,
    skip_gain,
):
    thought_count, positions, width_local = mixer_input.shape
    state_size = parent_state.shape[1]
    rank = rate_down.shape[1]
    driven = convolve(parent_conv, fork_map, mixer_input, conv_weight, conv_bias)
    token_rows = driven.reshape(thought_count * positions, width_local)
    low_part = jnp.dot(token_rows, rate_down, preferred_element_type=jnp.float32)
    select_part = jnp.dot(token_rows, selection_weight, preferred_element_type=jnp.float32)
    select_high = select_part.astype(jnp.bfloat16)
    select_low = (select_part - select_high.astype(jnp.float32)).astype(jnp.bfloat16)
    partial = jnp.concatenate([low_part.astype(jnp.bfloat16), select_high, select_low], axis=1)
    devices = lax.axis_size("chan")
    pieces = lax.all_to_all(
        partial.reshape(devices, -1, partial.shape[1]), "chan", 0, 0, tiled=True
    ).astype(jnp.float32)
    reduced = jnp.sum(pieces, axis=0)
    low_mine = reduced[:, :rank].astype(jnp.bfloat16)
    select_sum = reduced[:, rank : rank + 2 * state_size] + reduced[:, rank + 2 * state_size :]
    select_high = select_sum.astype(jnp.bfloat16)
    select_low = (select_sum - select_high.astype(jnp.float32)).astype(jnp.bfloat16)
    mine = jnp.concatenate([low_mine, select_high, select_low], axis=1)
    gathered = lax.all_to_all(
        jnp.broadcast_to(mine[None], (devices,) + mine.shape), "chan", 0, 0, tiled=True
    ).reshape(-1, mine.shape[1])
    rate_low = gathered[:, :rank]
    selection = (
        gathered[:, rank : rank + 2 * state_size].astype(jnp.float32)
        + gathered[:, rank + 2 * state_size :].astype(jnp.float32)
    ).reshape(thought_count, positions, 2 * state_size)
    step_rate = jax.nn.softplus(
        jnp.dot(rate_low, rate_up, preferred_element_type=jnp.float32) + rate_bias[None, :]
    ).reshape(thought_count, positions, width_local)
    b_t = jnp.swapaxes(selection[:, :, :state_size], 1, 2)
    c_t = jnp.swapaxes(selection[:, :, state_size:], 1, 2)
    decay_rate = -jnp.exp(decay_log)
    packed_local = run_scan(
        judge_lengths, fork_map, step_rate, driven, gate_input, b_t, c_t, parent_state,
        decay_rate, skip_gain,
    )
    packed = lax.all_to_all(packed_local, "chan", split_axis=0, concat_axis=2, tiled=True)
    final_state = packed[:, :state_size].astype(jnp.float32)
    mixer_output = packed[:, state_size:]
    return (mixer_output, final_state)


def solution(mesh):
    placed = (
        P("group", None, "chan"),
        P("group", None, "chan"),
        P("group"),
        P("group"),
        P("group", None, "chan"),
        P("group", None, "chan"),
        P(None, "chan"),
        P("chan"),
        P("chan", None),
        P("chan", None),
        P(None, "chan"),
        P("chan"),
        P(None, "chan"),
        P("chan"),
    )
    return jax.shard_map(
        body,
        mesh=mesh,
        in_specs=placed,
        out_specs=(P(("group", "chan"), None, None), P(("group", "chan"), None, None)),
        check_vma=False,
    )
```

```python
import jax
import jax.numpy as jnp
from jax import lax
from jax.experimental import pallas as pl
from jax.experimental.pallas import tpu as pltpu
from jax.sharding import PartitionSpec as P

GEN = 4


def convolve(parent_conv, fork_map, mixer_input, conv_weight, conv_bias):
    positions = mixer_input.shape[1]
    start_conv = jnp.take(parent_conv, fork_map, axis=0)
    padded = jnp.concatenate([start_conv, mixer_input], axis=1).astype(jnp.float32)
    tap_weights = conv_weight.astype(jnp.float32)
    summed = conv_bias[None, None, :] + tap_weights[0][None, None, :] * padded[:, 0:positions, :]
    for offset in range(1, conv_weight.shape[0]):
        summed = (
            summed + tap_weights[offset][None, None, :] * padded[:, offset : offset + positions, :]
        )
    return jax.nn.silu(summed).astype(jnp.bfloat16)


def scan_kernel(
    lens_ref, fmap_ref, gathered_ref, up_ref, bias_ref, drive_ref, gate_ref, b_ref, h0_ref,
    a_ref, skip_ref, packed_ref, r_scr, u_scr, y_scr
):
    t = pl.program_id(0)
    positions = drive_ref.shape[1]
    state_size = h0_ref.shape[1]
    rank = up_ref.shape[0]
    live = jnp.clip(lens_ref[t] + GEN, 0, positions)
    row_all = gathered_ref[0]
    pre = (
        jnp.dot(row_all[:, :rank], up_ref[...], preferred_element_type=jnp.float32)
        + bias_ref[...]
    )
    rate = jnp.maximum(pre, 0.0) + jnp.log1p(jnp.exp(-jnp.abs(pre)))
    readout_rows = (
        row_all[:, rank + state_size : rank + 2 * state_size].astype(jnp.float32)
        + row_all[:, rank + 3 * state_size :].astype(jnp.float32)
    )
    inflow = drive_ref[0].astype(jnp.float32)
    alive = lax.broadcasted_iota(jnp.int32, inflow.shape, 0) < live
    rate = jnp.where(alive, rate, 0.0)
    r_scr[...] = rate
    u_scr[...] = rate * inflow
    b_all = b_ref[0]
    decay = a_ref[...]
    h = h0_ref[0]
    for p in range(positions):
        h = jnp.exp(r_scr[p : p + 1, :] * decay) * h + u_scr[p : p + 1, :] * b_all[:, p : p + 1]
        y_scr[p : p + 1, :] = jnp.dot(
            readout_rows[p : p + 1, :], h,
            precision=lax.Precision.HIGHEST, preferred_element_type=jnp.float32,
        )
    packed_ref[0, :state_size, :] = h.astype(packed_ref.dtype)
    gate = gate_ref[0].astype(jnp.float32)
    result = (y_scr[...] + skip_ref[...] * inflow) * jax.nn.silu(gate)
    packed_ref[0, state_size:, :] = jnp.where(alive, result, 0.0).astype(packed_ref.dtype)


def run_scan(judge_lengths, fork_map, gathered, rate_up, rate_bias, driven, gate_input, b_t,
             parent_state, decay_rate, skip_gain):
    thought_count, positions, width_local = driven.shape
    state_size = parent_state.shape[1]
    rank, columns = rate_up.shape[0], gathered.shape[2]
    row_block = lambda t, lens, fmap: (t, 0, 0)
    whole = lambda t, lens, fmap: (0, 0)
    grid_spec = pltpu.PrefetchScalarGridSpec(
        num_scalar_prefetch=2,
        grid=(thought_count,),
        in_specs=[
            pl.BlockSpec((1, positions, columns), row_block),
            pl.BlockSpec((rank, width_local), whole),
            pl.BlockSpec((1, width_local), whole),
            pl.BlockSpec((1, positions, width_local), row_block),
            pl.BlockSpec((1, positions, width_local), row_block),
            pl.BlockSpec((1, state_size, positions), row_block),
            pl.BlockSpec((1, state_size, width_local), lambda t, lens, fmap: (fmap[t], 0, 0)),
            pl.BlockSpec((state_size, width_local), whole),
            pl.BlockSpec((1, width_local), whole),
        ],
        out_specs=pl.BlockSpec((1, state_size + positions, width_local), row_block),
        scratch_shapes=[pltpu.VMEM((positions, width_local), jnp.float32)] * 3,
    )
    return pl.pallas_call(
        scan_kernel,
        grid_spec=grid_spec,
        out_shape=jax.ShapeDtypeStruct(
            (thought_count, state_size + positions, width_local), jnp.bfloat16
        ),
        compiler_params=pltpu.CompilerParams(dimension_semantics=("arbitrary",)),
    )(judge_lengths, fork_map, gathered, rate_up, rate_bias.reshape(1, width_local), driven,
      gate_input, b_t, parent_state, decay_rate, skip_gain.reshape(1, width_local))


def body(
    parent_state,
    parent_conv,
    fork_map,
    judge_lengths,
    mixer_input,
    gate_input,
    conv_weight,
    conv_bias,
    rate_down,
    selection_weight,
    rate_up,
    rate_bias,
    decay_log,
    skip_gain,
):
    thought_count, positions, width_local = mixer_input.shape
    state_size = parent_state.shape[1]
    rank = rate_down.shape[1]
    driven = convolve(parent_conv, fork_map, mixer_input, conv_weight, conv_bias)
    token_rows = driven.reshape(thought_count * positions, width_local)
    low_part = jnp.dot(token_rows, rate_down, preferred_element_type=jnp.float32)
    select_part = jnp.dot(token_rows, selection_weight, preferred_element_type=jnp.float32)
    select_high = select_part.astype(jnp.bfloat16)
    select_low = (select_part - select_high.astype(jnp.float32)).astype(jnp.bfloat16)
    partial = jnp.concatenate([low_part.astype(jnp.bfloat16), select_high, select_low], axis=1)
    devices = lax.axis_size("chan")
    pieces = lax.all_to_all(
        partial.reshape(devices, -1, partial.shape[1]), "chan", 0, 0, tiled=True
    ).astype(jnp.float32)
    reduced = jnp.sum(pieces, axis=0)
    low_mine = reduced[:, :rank].astype(jnp.bfloat16)
    select_sum = reduced[:, rank : rank + 2 * state_size] + reduced[:, rank + 2 * state_size :]
    select_high = select_sum.astype(jnp.bfloat16)
    select_low = (select_sum - select_high.astype(jnp.float32)).astype(jnp.bfloat16)
    mine = jnp.concatenate([low_mine, select_high, select_low], axis=1)
    gathered = lax.all_to_all(
        jnp.broadcast_to(mine[None], (devices,) + mine.shape), "chan", 0, 0, tiled=True
    )
    b_t = jnp.swapaxes(
        gathered[:, :, rank : rank + state_size].astype(jnp.float32)
        + gathered[:, :, rank + 2 * state_size : rank + 3 * state_size].astype(jnp.float32),
        1, 2,
    )
    decay_rate = -jnp.exp(decay_log)
    packed_local = run_scan(
        judge_lengths, fork_map, gathered, rate_up, rate_bias, driven, gate_input, b_t,
        parent_state, decay_rate, skip_gain,
    )
    packed = lax.all_to_all(packed_local, "chan", split_axis=0, concat_axis=2, tiled=True)
    final_state = packed[:, :state_size].astype(jnp.float32)
    mixer_output = packed[:, state_size:]
    return (mixer_output, final_state)


def solution(mesh):
    placed = (
        P("group", None, "chan"),
        P("group", None, "chan"),
        P("group"),
        P("group"),
        P("group", None, "chan"),
        P("group", None, "chan"),
        P(None, "chan"),
        P("chan"),
        P("chan", None),
        P("chan", None),
        P(None, "chan"),
        P("chan"),
        P(None, "chan"),
        P("chan"),
    )
    return jax.shard_map(
        body,
        mesh=mesh,
        in_specs=placed,
        out_specs=(P(("group", "chan"), None, None), P(("group", "chan"), None, None)),
        check_vma=False,
    )
```

```python
import jax
import jax.numpy as jnp
from jax import lax
from jax.experimental import pallas as pl
from jax.experimental.pallas import tpu as pltpu
from jax.sharding import PartitionSpec as P

GEN = 4


def convolve(parent_conv, fork_map, mixer_input, conv_weight, conv_bias):
    positions = mixer_input.shape[1]
    start_conv = jnp.take(parent_conv, fork_map, axis=0, mode="clip")
    padded = jnp.concatenate([start_conv, mixer_input], axis=1).astype(jnp.float32)
    tap_weights = conv_weight.astype(jnp.float32)
    summed = conv_bias[None, None, :] + tap_weights[0][None, None, :] * padded[:, 0:positions, :]
    for offset in range(1, conv_weight.shape[0]):
        summed = (
            summed + tap_weights[offset][None, None, :] * padded[:, offset : offset + positions, :]
        )
    return jax.nn.silu(summed).astype(jnp.bfloat16)


def scan_kernel(
    lens_ref, fmap_ref, rate_ref, drive_ref, gate_ref, b_ref, c_ref, *rest
):
    pair = len(rest) - 6
    h0_refs, (a_ref, skip_ref, packed_ref, r_scr, u_scr, y_scr) = rest[:pair], rest[pair:]
    positions = rate_ref.shape[1]
    state_size = h0_refs[0].shape[1]
    decay = a_ref[...]
    states, lives = [], []
    for k in range(pair):
        live = jnp.clip(lens_ref[pl.program_id(0) * pair + k] + GEN, 0, positions)
        inflow = drive_ref[k].astype(jnp.float32)
        alive = lax.broadcasted_iota(jnp.int32, inflow.shape, 0) < live
        rate = jnp.where(alive, rate_ref[k], 0.0)
        r_scr[k] = rate
        u_scr[k] = rate * inflow
        states.append(h0_refs[k][0])
        lives.append(alive)
    for p in range(positions):
        for k in range(pair):
            b_col = b_ref[k][:, p : p + 1]
            c_col = c_ref[k][:, p : p + 1]
            h = states[k]
            h = jnp.exp(r_scr[k, p : p + 1, :] * decay) * h + u_scr[k, p : p + 1, :] * b_col
            y_scr[k, p : p + 1, :] = jnp.sum(c_col * h, axis=0, keepdims=True)
            states[k] = h
    for k in range(pair):
        packed_ref[k, :state_size, :] = states[k].astype(packed_ref.dtype)
        inflow = drive_ref[k].astype(jnp.float32)
        gate = gate_ref[k].astype(jnp.float32)
        result = (y_scr[k] + skip_ref[...] * inflow) * jax.nn.silu(gate)
        packed_ref[k, state_size:, :] = jnp.where(lives[k], result, 0.0).astype(packed_ref.dtype)


def run_scan(judge_lengths, fork_map, step_rate, driven, gate_input, b_t, c_t, parent_state,
             decay_rate, skip_gain):
    thought_count, positions, width_local = driven.shape
    state_size = parent_state.shape[1]
    pair = 2 if thought_count % 2 == 0 else 1
    row_block = lambda t, lens, fmap: (t, 0, 0)
    whole = lambda t, lens, fmap: (0, 0)

    def state_block(k):
        return pl.BlockSpec(
            (1, state_size, width_local), lambda t, lens, fmap: (fmap[t * pair + k], 0, 0)
        )

    grid_spec = pltpu.PrefetchScalarGridSpec(
        num_scalar_prefetch=2,
        grid=(thought_count // pair,),
        in_specs=[
            pl.BlockSpec((pair, positions, width_local), row_block),
            pl.BlockSpec((pair, positions, width_local), row_block),
            pl.BlockSpec((pair, positions, width_local), row_block),
            pl.BlockSpec((pair, state_size, positions), row_block),
            pl.BlockSpec((pair, state_size, positions), row_block),
        ]
        + [state_block(k) for k in range(pair)]
        + [
            pl.BlockSpec((state_size, width_local), whole),
            pl.BlockSpec((1, width_local), whole),
        ],
        out_specs=pl.BlockSpec((pair, state_size + positions, width_local), row_block),
        scratch_shapes=[pltpu.VMEM((pair, positions, width_local), jnp.float32)] * 3,
    )
    return pl.pallas_call(
        scan_kernel,
        grid_spec=grid_spec,
        out_shape=jax.ShapeDtypeStruct(
            (thought_count, state_size + positions, width_local), jnp.bfloat16
        ),
        compiler_params=pltpu.CompilerParams(dimension_semantics=("arbitrary",)),
    )(judge_lengths, fork_map, step_rate, driven, gate_input, b_t, c_t,
      *([parent_state] * pair), decay_rate, skip_gain.reshape(1, width_local))


def body(
    parent_state,
    parent_conv,
    fork_map,
    judge_lengths,
    mixer_input,
    gate_input,
    conv_weight,
    conv_bias,
    rate_down,
    selection_weight,
    rate_up,
    rate_bias,
    decay_log,
    skip_gain,
):
    thought_count, positions, width_local = mixer_input.shape
    state_size = parent_state.shape[1]
    rank = rate_down.shape[1]
    driven = convolve(parent_conv, fork_map, mixer_input, conv_weight, conv_bias)
    token_rows = driven.reshape(thought_count * positions, width_local)
    low_part = jnp.dot(token_rows, rate_down, preferred_element_type=jnp.float32)
    select_part = jnp.dot(token_rows, selection_weight, preferred_element_type=jnp.float32)
    select_high = select_part.astype(jnp.bfloat16)
    select_low = (select_part - select_high.astype(jnp.float32)).astype(jnp.bfloat16)
    partial = jnp.concatenate([low_part.astype(jnp.bfloat16), select_high, select_low], axis=1)
    devices = lax.axis_size("chan")
    pieces = lax.all_to_all(
        partial.reshape(devices, -1, partial.shape[1]), "chan", 0, 0, tiled=True
    ).astype(jnp.float32)
    reduced = jnp.sum(pieces, axis=0)
    low_mine = reduced[:, :rank].astype(jnp.bfloat16)
    select_sum = reduced[:, rank : rank + 2 * state_size] + reduced[:, rank + 2 * state_size :]
    select_high = select_sum.astype(jnp.bfloat16)
    select_low = (select_sum - select_high.astype(jnp.float32)).astype(jnp.bfloat16)
    mine = jnp.concatenate([low_mine, select_high, select_low], axis=1)
    gathered = lax.all_to_all(
        jnp.broadcast_to(mine[None], (devices,) + mine.shape), "chan", 0, 0, tiled=True
    ).reshape(-1, mine.shape[1])
    rate_low = gathered[:, :rank]
    selection = (
        gathered[:, rank : rank + 2 * state_size].astype(jnp.float32)
        + gathered[:, rank + 2 * state_size :].astype(jnp.float32)
    ).reshape(thought_count, positions, 2 * state_size)
    step_rate = jax.nn.softplus(
        jnp.dot(rate_low, rate_up, preferred_element_type=jnp.float32) + rate_bias[None, :]
    ).reshape(thought_count, positions, width_local)
    b_t = jnp.swapaxes(selection[:, :, :state_size], 1, 2)
    c_t = jnp.swapaxes(selection[:, :, state_size:], 1, 2)
    decay_rate = -jnp.exp(decay_log)
    packed_local = run_scan(
        judge_lengths, fork_map, step_rate, driven, gate_input, b_t, c_t, parent_state,
        decay_rate, skip_gain,
    )
    packed = lax.all_to_all(packed_local, "chan", split_axis=0, concat_axis=2, tiled=True)
    final_state = packed[:, :state_size].astype(jnp.float32)
    mixer_output = packed[:, state_size:]
    return (mixer_output, final_state)


def solution(mesh):
    placed = (
        P("group", None, "chan"),
        P("group", None, "chan"),
        P("group"),
        P("group"),
        P("group", None, "chan"),
        P("group", None, "chan"),
        P(None, "chan"),
        P("chan"),
        P("chan", None),
        P("chan", None),
        P(None, "chan"),
        P("chan"),
        P(None, "chan"),
        P("chan"),
    )
    return jax.shard_map(
        body,
        mesh=mesh,
        in_specs=placed,
        out_specs=(P(("group", "chan"), None, None), P(("group", "chan"), None, None)),
        check_vma=False,
    )
```

```python
import jax
import jax.numpy as jnp
from jax import lax
from jax.experimental import pallas as pl
from jax.experimental.pallas import tpu as pltpu
from jax.sharding import PartitionSpec as P

GEN = 4


def convolve(parent_conv, fork_map, mixer_input, conv_weight, conv_bias):
    positions = mixer_input.shape[1]
    start_conv = jnp.take(parent_conv, fork_map, axis=0, mode="clip")
    padded = jnp.concatenate([start_conv, mixer_input], axis=1).astype(jnp.float32)
    tap_weights = conv_weight.astype(jnp.float32)
    summed = conv_bias[None, None, :] + tap_weights[0][None, None, :] * padded[:, 0:positions, :]
    for offset in range(1, conv_weight.shape[0]):
        summed = (
            summed + tap_weights[offset][None, None, :] * padded[:, offset : offset + positions, :]
        )
    return jax.nn.silu(summed).astype(jnp.bfloat16)


def scan_kernel(
    lens_ref, fmap_ref, rate_ref, drive_ref, gate_ref, b_ref, c_ref, *rest
):
    pair = len(rest) - 6
    h0_refs, (a_ref, skip_ref, packed_ref, r_scr, u_scr, y_scr) = rest[:pair], rest[pair:]
    positions = rate_ref.shape[1]
    state_size = h0_refs[0].shape[1]
    decay = a_ref[...]
    states, lives = [], []
    for k in range(pair):
        live = jnp.clip(lens_ref[pl.program_id(0) * pair + k] + GEN, 0, positions)
        inflow = drive_ref[k].astype(jnp.float32)
        alive = lax.broadcasted_iota(jnp.int32, inflow.shape, 0) < live
        rate = jnp.where(alive, rate_ref[k], 0.0)
        r_scr[k] = rate
        u_scr[k] = rate * inflow
        states.append(h0_refs[k][0])
        lives.append(alive)
    for p in range(positions):
        for k in range(pair):
            b_col = b_ref[k][:, p : p + 1]
            c_col = c_ref[k][:, p : p + 1]
            h = states[k]
            h = jnp.exp(r_scr[k, p : p + 1, :] * decay) * h + u_scr[k, p : p + 1, :] * b_col
            y_scr[k, p : p + 1, :] = jnp.sum(c_col * h, axis=0, keepdims=True)
            states[k] = h
    for k in range(pair):
        packed_ref[k, :state_size, :] = states[k].astype(packed_ref.dtype)
        inflow = drive_ref[k].astype(jnp.float32)
        gate = gate_ref[k].astype(jnp.float32)
        result = (y_scr[k] + skip_ref[...] * inflow) * jax.nn.silu(gate)
        packed_ref[k, state_size:, :] = jnp.where(lives[k], result, 0.0).astype(packed_ref.dtype)


def run_scan(judge_lengths, fork_map, step_rate, driven, gate_input, b_t, c_t, parent_state,
             decay_rate, skip_gain):
    thought_count, positions, width_local = driven.shape
    state_size = parent_state.shape[1]
    pair = 4 if thought_count % 4 == 0 else 1
    row_block = lambda t, lens, fmap: (t, 0, 0)
    whole = lambda t, lens, fmap: (0, 0)

    def state_block(k):
        return pl.BlockSpec(
            (1, state_size, width_local), lambda t, lens, fmap: (fmap[t * pair + k], 0, 0)
        )

    grid_spec = pltpu.PrefetchScalarGridSpec(
        num_scalar_prefetch=2,
        grid=(thought_count // pair,),
        in_specs=[
            pl.BlockSpec((pair, positions, width_local), row_block),
            pl.BlockSpec((pair, positions, width_local), row_block),
            pl.BlockSpec((pair, positions, width_local), row_block),
            pl.BlockSpec((pair, state_size, positions), row_block),
            pl.BlockSpec((pair, state_size, positions), row_block),
        ]
        + [state_block(k) for k in range(pair)]
        + [
            pl.BlockSpec((state_size, width_local), whole),
            pl.BlockSpec((1, width_local), whole),
        ],
        out_specs=pl.BlockSpec((pair, state_size + positions, width_local), row_block),
        scratch_shapes=[pltpu.VMEM((pair, positions, width_local), jnp.float32)] * 3,
    )
    return pl.pallas_call(
        scan_kernel,
        grid_spec=grid_spec,
        out_shape=jax.ShapeDtypeStruct(
            (thought_count, state_size + positions, width_local), jnp.bfloat16
        ),
        compiler_params=pltpu.CompilerParams(dimension_semantics=("arbitrary",)),
    )(judge_lengths, fork_map, step_rate, driven, gate_input, b_t, c_t,
      *([parent_state] * pair), decay_rate, skip_gain.reshape(1, width_local))


def body(
    parent_state,
    parent_conv,
    fork_map,
    judge_lengths,
    mixer_input,
    gate_input,
    conv_weight,
    conv_bias,
    rate_down,
    selection_weight,
    rate_up,
    rate_bias,
    decay_log,
    skip_gain,
):
    thought_count, positions, width_local = mixer_input.shape
    state_size = parent_state.shape[1]
    rank = rate_down.shape[1]
    driven = convolve(parent_conv, fork_map, mixer_input, conv_weight, conv_bias)
    token_rows = driven.reshape(thought_count * positions, width_local)
    low_part = jnp.dot(token_rows, rate_down, preferred_element_type=jnp.float32)
    select_part = jnp.dot(token_rows, selection_weight, preferred_element_type=jnp.float32)
    select_high = select_part.astype(jnp.bfloat16)
    select_low = (select_part - select_high.astype(jnp.float32)).astype(jnp.bfloat16)
    partial = jnp.concatenate([low_part.astype(jnp.bfloat16), select_high, select_low], axis=1)
    devices = lax.axis_size("chan")
    pieces = lax.all_to_all(
        partial.reshape(devices, -1, partial.shape[1]), "chan", 0, 0, tiled=True
    ).astype(jnp.float32)
    reduced = jnp.sum(pieces, axis=0)
    low_mine = reduced[:, :rank].astype(jnp.bfloat16)
    select_sum = reduced[:, rank : rank + 2 * state_size] + reduced[:, rank + 2 * state_size :]
    select_high = select_sum.astype(jnp.bfloat16)
    select_low = (select_sum - select_high.astype(jnp.float32)).astype(jnp.bfloat16)
    mine = jnp.concatenate([low_mine, select_high, select_low], axis=1)
    gathered = lax.all_to_all(
        jnp.broadcast_to(mine[None], (devices,) + mine.shape), "chan", 0, 0, tiled=True
    ).reshape(-1, mine.shape[1])
    rate_low = gathered[:, :rank]
    selection = (
        gathered[:, rank : rank + 2 * state_size].astype(jnp.float32)
        + gathered[:, rank + 2 * state_size :].astype(jnp.float32)
    ).reshape(thought_count, positions, 2 * state_size)
    step_rate = jax.nn.softplus(
        jnp.dot(rate_low, rate_up, preferred_element_type=jnp.float32) + rate_bias[None, :]
    ).reshape(thought_count, positions, width_local)
    b_t = jnp.swapaxes(selection[:, :, :state_size], 1, 2)
    c_t = jnp.swapaxes(selection[:, :, state_size:], 1, 2)
    decay_rate = -jnp.exp(decay_log)
    packed_local = run_scan(
        judge_lengths, fork_map, step_rate, driven, gate_input, b_t, c_t, parent_state,
        decay_rate, skip_gain,
    )
    packed = lax.all_to_all(packed_local, "chan", split_axis=0, concat_axis=2, tiled=True)
    final_state = packed[:, :state_size].astype(jnp.float32)
    mixer_output = packed[:, state_size:]
    return (mixer_output, final_state)


def solution(mesh):
    placed = (
        P("group", None, "chan"),
        P("group", None, "chan"),
        P("group"),
        P("group"),
        P("group", None, "chan"),
        P("group", None, "chan"),
        P(None, "chan"),
        P("chan"),
        P("chan", None),
        P("chan", None),
        P(None, "chan"),
        P("chan"),
        P(None, "chan"),
        P("chan"),
    )
    return jax.shard_map(
        body,
        mesh=mesh,
        in_specs=placed,
        out_specs=(P(("group", "chan"), None, None), P(("group", "chan"), None, None)),
        check_vma=False,
    )
```

```python
import jax
import jax.numpy as jnp
from jax import lax
from jax.experimental import pallas as pl
from jax.experimental.pallas import tpu as pltpu
from jax.sharding import PartitionSpec as P

GEN = 4


def convolve(parent_conv, fork_map, mixer_input, conv_weight, conv_bias):
    positions = mixer_input.shape[1]
    start_conv = jnp.take(parent_conv, fork_map, axis=0, mode="clip")
    padded = jnp.concatenate([start_conv, mixer_input], axis=1).astype(jnp.float32)
    tap_weights = conv_weight.astype(jnp.float32)
    summed = conv_bias[None, None, :] + tap_weights[0][None, None, :] * padded[:, 0:positions, :]
    for offset in range(1, conv_weight.shape[0]):
        summed = (
            summed + tap_weights[offset][None, None, :] * padded[:, offset : offset + positions, :]
        )
    return jax.nn.silu(summed).astype(jnp.bfloat16)


def scan_kernel(
    lens_ref, fmap_ref, rate_ref, drive_ref, gate_ref, b_ref, c_ref, *rest
):
    pair = len(rest) - 8
    h0_refs = rest[:pair]
    a_ref, skip_ref, packed_ref, r_scr, u_scr, y_scr, bb_scr, cb_scr = rest[pair:]
    positions = rate_ref.shape[1]
    state_size, width_local = h0_refs[0].shape[1], h0_refs[0].shape[2]
    lanes = bb_scr.shape[-1]
    block = 4 if positions % 4 == 0 else 1
    states, lives, longest = [], [], 0
    for k in range(pair):
        live = jnp.clip(lens_ref[pl.program_id(0) * pair + k] + GEN, 0, positions)
        inflow = drive_ref[k].astype(jnp.float32)
        alive = lax.broadcasted_iota(jnp.int32, inflow.shape, 0) < live
        rate = jnp.where(alive, rate_ref[k], 0.0)
        r_scr[k] = rate
        u_scr[k] = rate * inflow
        b_all = b_ref[k]
        c_all = c_ref[k]
        for p in range(positions):
            bb_scr[k, p] = jnp.broadcast_to(b_all[:, p : p + 1], (state_size, lanes))
            cb_scr[k, p] = jnp.broadcast_to(c_all[:, p : p + 1], (state_size, lanes))
        states.append(h0_refs[k][0])
        lives.append(alive)
        longest = jnp.maximum(longest, live)
    decay = a_ref[...]
    tiles = width_local // lanes

    def advance(blk, carried):
        carried = list(carried)
        for i in range(block):
            p = blk * block + i
            for k in range(pair):
                b_col = jnp.tile(bb_scr[k, p], (1, tiles))
                c_col = jnp.tile(cb_scr[k, p], (1, tiles))
                h = carried[k]
                h = (
                    jnp.exp(r_scr[k, pl.ds(p, 1), :] * decay) * h
                    + u_scr[k, pl.ds(p, 1), :] * b_col
                )
                y_scr[k, pl.ds(p, 1), :] = jnp.sum(c_col * h, axis=0, keepdims=True)
                carried[k] = h
        return tuple(carried)

    states = lax.fori_loop(0, (longest + block - 1) // block, advance, tuple(states))
    for k in range(pair):
        packed_ref[k, :state_size, :] = states[k].astype(packed_ref.dtype)
        inflow = drive_ref[k].astype(jnp.float32)
        gate = gate_ref[k].astype(jnp.float32)
        result = (y_scr[k] + skip_ref[...] * inflow) * jax.nn.silu(gate)
        packed_ref[k, state_size:, :] = jnp.where(lives[k], result, 0.0).astype(packed_ref.dtype)


def run_scan(judge_lengths, fork_map, step_rate, driven, gate_input, b_t, c_t, parent_state,
             decay_rate, skip_gain):
    thought_count, positions, width_local = driven.shape
    state_size = parent_state.shape[1]
    pair = 2 if thought_count % 2 == 0 else 1
    row_block = lambda t, lens, fmap: (t, 0, 0)
    whole = lambda t, lens, fmap: (0, 0)

    def state_block(k):
        return pl.BlockSpec(
            (1, state_size, width_local), lambda t, lens, fmap: (fmap[t * pair + k], 0, 0)
        )

    grid_spec = pltpu.PrefetchScalarGridSpec(
        num_scalar_prefetch=2,
        grid=(thought_count // pair,),
        in_specs=[
            pl.BlockSpec((pair, positions, width_local), row_block),
            pl.BlockSpec((pair, positions, width_local), row_block),
            pl.BlockSpec((pair, positions, width_local), row_block),
            pl.BlockSpec((pair, state_size, positions), row_block),
            pl.BlockSpec((pair, state_size, positions), row_block),
        ]
        + [state_block(k) for k in range(pair)]
        + [
            pl.BlockSpec((state_size, width_local), whole),
            pl.BlockSpec((1, width_local), whole),
        ],
        out_specs=pl.BlockSpec((pair, state_size + positions, width_local), row_block),
        scratch_shapes=[pltpu.VMEM((pair, positions, width_local), jnp.float32)] * 3
        + [pltpu.VMEM((pair, positions, state_size, min(128, width_local)), jnp.float32)] * 2,
    )
    return pl.pallas_call(
        scan_kernel,
        grid_spec=grid_spec,
        out_shape=jax.ShapeDtypeStruct(
            (thought_count, state_size + positions, width_local), jnp.bfloat16
        ),
        compiler_params=pltpu.CompilerParams(dimension_semantics=("arbitrary",)),
    )(judge_lengths, fork_map, step_rate, driven, gate_input, b_t, c_t,
      *([parent_state] * pair), decay_rate, skip_gain.reshape(1, width_local))


def body(
    parent_state,
    parent_conv,
    fork_map,
    judge_lengths,
    mixer_input,
    gate_input,
    conv_weight,
    conv_bias,
    rate_down,
    selection_weight,
    rate_up,
    rate_bias,
    decay_log,
    skip_gain,
):
    thought_count, positions, width_local = mixer_input.shape
    state_size = parent_state.shape[1]
    rank = rate_down.shape[1]
    driven = convolve(parent_conv, fork_map, mixer_input, conv_weight, conv_bias)
    token_rows = driven.reshape(thought_count * positions, width_local)
    low_part = jnp.dot(token_rows, rate_down, preferred_element_type=jnp.float32)
    select_part = jnp.dot(token_rows, selection_weight, preferred_element_type=jnp.float32)
    select_high = select_part.astype(jnp.bfloat16)
    select_low = (select_part - select_high.astype(jnp.float32)).astype(jnp.bfloat16)
    partial = jnp.concatenate([low_part.astype(jnp.bfloat16), select_high, select_low], axis=1)
    devices = lax.axis_size("chan")
    pieces = lax.all_to_all(
        partial.reshape(devices, -1, partial.shape[1]), "chan", 0, 0, tiled=True
    ).astype(jnp.float32)
    reduced = jnp.sum(pieces, axis=0)
    low_mine = reduced[:, :rank].astype(jnp.bfloat16)
    select_sum = reduced[:, rank : rank + 2 * state_size] + reduced[:, rank + 2 * state_size :]
    select_high = select_sum.astype(jnp.bfloat16)
    select_low = (select_sum - select_high.astype(jnp.float32)).astype(jnp.bfloat16)
    mine = jnp.concatenate([low_mine, select_high, select_low], axis=1)
    gathered = lax.all_to_all(
        jnp.broadcast_to(mine[None], (devices,) + mine.shape), "chan", 0, 0, tiled=True
    ).reshape(-1, mine.shape[1])
    rate_low = gathered[:, :rank]
    selection = (
        gathered[:, rank : rank + 2 * state_size].astype(jnp.float32)
        + gathered[:, rank + 2 * state_size :].astype(jnp.float32)
    ).reshape(thought_count, positions, 2 * state_size)
    step_rate = jax.nn.softplus(
        jnp.dot(rate_low, rate_up, preferred_element_type=jnp.float32) + rate_bias[None, :]
    ).reshape(thought_count, positions, width_local)
    b_t = jnp.swapaxes(selection[:, :, :state_size], 1, 2)
    c_t = jnp.swapaxes(selection[:, :, state_size:], 1, 2)
    decay_rate = -jnp.exp(decay_log)
    packed_local = run_scan(
        judge_lengths, fork_map, step_rate, driven, gate_input, b_t, c_t, parent_state,
        decay_rate, skip_gain,
    )
    packed = lax.all_to_all(packed_local, "chan", split_axis=0, concat_axis=2, tiled=True)
    final_state = packed[:, :state_size].astype(jnp.float32)
    mixer_output = packed[:, state_size:]
    return (mixer_output, final_state)


def solution(mesh):
    placed = (
        P("group", None, "chan"),
        P("group", None, "chan"),
        P("group"),
        P("group"),
        P("group", None, "chan"),
        P("group", None, "chan"),
        P(None, "chan"),
        P("chan"),
        P("chan", None),
        P("chan", None),
        P(None, "chan"),
        P("chan"),
        P(None, "chan"),
        P("chan"),
    )
    return jax.shard_map(
        body,
        mesh=mesh,
        in_specs=placed,
        out_specs=(P(("group", "chan"), None, None), P(("group", "chan"), None, None)),
        check_vma=False,
    )
```

```python
import jax
import jax.numpy as jnp
from jax import lax
from jax.experimental import pallas as pl
from jax.experimental.pallas import tpu as pltpu
from jax.sharding import PartitionSpec as P

GEN = 4


def convolve(parent_conv, fork_map, mixer_input, conv_weight, conv_bias):
    positions = mixer_input.shape[1]
    start_conv = jnp.take(parent_conv, fork_map, axis=0, mode="clip")
    padded = jnp.concatenate([start_conv, mixer_input], axis=1).astype(jnp.float32)
    tap_weights = conv_weight.astype(jnp.float32)
    summed = conv_bias[None, None, :] + tap_weights[0][None, None, :] * padded[:, 0:positions, :]
    for offset in range(1, conv_weight.shape[0]):
        summed = (
            summed + tap_weights[offset][None, None, :] * padded[:, offset : offset + positions, :]
        )
    return jax.nn.silu(summed).astype(jnp.bfloat16)


def scan_kernel(
    lens_ref, fmap_ref, rate_ref, drive_ref, gate_ref, b_ref, c_ref, *rest
):
    pair = len(rest) - 6
    h0_refs, (a_ref, skip_ref, packed_ref, r_scr, u_scr, y_scr) = rest[:pair], rest[pair:]
    positions = rate_ref.shape[1]
    state_size = h0_refs[0].shape[1]
    decay = a_ref[...]
    states, lives = [], []
    for k in range(pair):
        live = jnp.clip(lens_ref[pl.program_id(0) * pair + k] + GEN, 0, positions)
        inflow = drive_ref[k].astype(jnp.float32)
        alive = lax.broadcasted_iota(jnp.int32, inflow.shape, 0) < live
        rate = jnp.where(alive, rate_ref[k], 0.0)
        r_scr[k] = rate
        u_scr[k] = rate * inflow
        states.append(h0_refs[k][0])
        lives.append(alive)
    for p in range(positions):
        for k in range(pair):
            b_col = b_ref[k][:, p : p + 1]
            c_col = c_ref[k][:, p : p + 1]
            h = states[k]
            rate_rows = r_scr[k, pl.ds(p, state_size, stride=0), :]
            push_rows = u_scr[k, pl.ds(p, state_size, stride=0), :]
            h = jnp.exp2(rate_rows * decay) * h + push_rows * b_col
            y_scr[k, p : p + 1, :] = jnp.sum(c_col * h, axis=0, keepdims=True)
            states[k] = h
    for k in range(pair):
        packed_ref[k, :state_size, :] = states[k].astype(packed_ref.dtype)
        inflow = drive_ref[k].astype(jnp.float32)
        gate = gate_ref[k].astype(jnp.float32)
        result = (y_scr[k] + skip_ref[...] * inflow) * jax.nn.silu(gate)
        packed_ref[k, state_size:, :] = jnp.where(lives[k], result, 0.0).astype(packed_ref.dtype)


def run_scan(judge_lengths, fork_map, step_rate, driven, gate_input, b_t, c_t, parent_state,
             decay_rate, skip_gain):
    thought_count, positions, width_local = driven.shape
    state_size = parent_state.shape[1]
    pair = 2 if thought_count % 2 == 0 else 1
    row_block = lambda t, lens, fmap: (t, 0, 0)
    whole = lambda t, lens, fmap: (0, 0)

    def state_block(k):
        return pl.BlockSpec(
            (1, state_size, width_local), lambda t, lens, fmap: (fmap[t * pair + k], 0, 0)
        )

    grid_spec = pltpu.PrefetchScalarGridSpec(
        num_scalar_prefetch=2,
        grid=(thought_count // pair,),
        in_specs=[
            pl.BlockSpec((pair, positions, width_local), row_block),
            pl.BlockSpec((pair, positions, width_local), row_block),
            pl.BlockSpec((pair, positions, width_local), row_block),
            pl.BlockSpec((pair, state_size, positions), row_block),
            pl.BlockSpec((pair, state_size, positions), row_block),
        ]
        + [state_block(k) for k in range(pair)]
        + [
            pl.BlockSpec((state_size, width_local), whole),
            pl.BlockSpec((1, width_local), whole),
        ],
        out_specs=pl.BlockSpec((pair, state_size + positions, width_local), row_block),
        scratch_shapes=[pltpu.VMEM((pair, positions, width_local), jnp.float32)] * 3,
    )
    return pl.pallas_call(
        scan_kernel,
        grid_spec=grid_spec,
        out_shape=jax.ShapeDtypeStruct(
            (thought_count, state_size + positions, width_local), jnp.bfloat16
        ),
        compiler_params=pltpu.CompilerParams(dimension_semantics=("arbitrary",)),
    )(judge_lengths, fork_map, step_rate, driven, gate_input, b_t, c_t,
      *([parent_state] * pair), decay_rate, skip_gain.reshape(1, width_local))


def body(
    parent_state,
    parent_conv,
    fork_map,
    judge_lengths,
    mixer_input,
    gate_input,
    conv_weight,
    conv_bias,
    rate_down,
    selection_weight,
    rate_up,
    rate_bias,
    decay_log,
    skip_gain,
):
    thought_count, positions, width_local = mixer_input.shape
    state_size = parent_state.shape[1]
    rank = rate_down.shape[1]
    driven = convolve(parent_conv, fork_map, mixer_input, conv_weight, conv_bias)
    token_rows = driven.reshape(thought_count * positions, width_local)
    low_part = jnp.dot(token_rows, rate_down, preferred_element_type=jnp.float32)
    select_part = jnp.dot(token_rows, selection_weight, preferred_element_type=jnp.float32)
    select_high = select_part.astype(jnp.bfloat16)
    select_low = (select_part - select_high.astype(jnp.float32)).astype(jnp.bfloat16)
    partial = jnp.concatenate([low_part.astype(jnp.bfloat16), select_high, select_low], axis=1)
    devices = lax.axis_size("chan")
    pieces = lax.all_to_all(
        partial.reshape(devices, -1, partial.shape[1]), "chan", 0, 0, tiled=True
    ).astype(jnp.float32)
    reduced = jnp.sum(pieces, axis=0)
    low_mine = reduced[:, :rank].astype(jnp.bfloat16)
    select_sum = reduced[:, rank : rank + 2 * state_size] + reduced[:, rank + 2 * state_size :]
    select_high = select_sum.astype(jnp.bfloat16)
    select_low = (select_sum - select_high.astype(jnp.float32)).astype(jnp.bfloat16)
    mine = jnp.concatenate([low_mine, select_high, select_low], axis=1)
    gathered = lax.all_to_all(
        jnp.broadcast_to(mine[None], (devices,) + mine.shape), "chan", 0, 0, tiled=True
    ).reshape(-1, mine.shape[1])
    rate_low = gathered[:, :rank]
    selection = (
        gathered[:, rank : rank + 2 * state_size].astype(jnp.float32)
        + gathered[:, rank + 2 * state_size :].astype(jnp.float32)
    ).reshape(thought_count, positions, 2 * state_size)
    step_rate = jax.nn.softplus(
        jnp.dot(rate_low, rate_up, preferred_element_type=jnp.float32) + rate_bias[None, :]
    ).reshape(thought_count, positions, width_local)
    b_t = jnp.swapaxes(selection[:, :, :state_size], 1, 2)
    c_t = jnp.swapaxes(selection[:, :, state_size:], 1, 2)
    decay_rate = -jnp.exp(decay_log) * 1.4426950408889634
    packed_local = run_scan(
        judge_lengths, fork_map, step_rate, driven, gate_input, b_t, c_t, parent_state,
        decay_rate, skip_gain,
    )
    packed = lax.all_to_all(packed_local, "chan", split_axis=0, concat_axis=2, tiled=True)
    final_state = packed[:, :state_size].astype(jnp.float32)
    mixer_output = packed[:, state_size:]
    return (mixer_output, final_state)


def solution(mesh):
    placed = (
        P("group", None, "chan"),
        P("group", None, "chan"),
        P("group"),
        P("group"),
        P("group", None, "chan"),
        P("group", None, "chan"),
        P(None, "chan"),
        P("chan"),
        P("chan", None),
        P("chan", None),
        P(None, "chan"),
        P("chan"),
        P(None, "chan"),
        P("chan"),
    )
    return jax.shard_map(
        body,
        mesh=mesh,
        in_specs=placed,
        out_specs=(P(("group", "chan"), None, None), P(("group", "chan"), None, None)),
        check_vma=False,
    )
```

```python
import jax
import jax.numpy as jnp
from jax import lax
from jax.experimental import pallas as pl
from jax.experimental.pallas import tpu as pltpu
from jax.sharding import PartitionSpec as P

GEN = 4


def project_kernel(
    fmap_ref, conv_ref, input_ref, weight_ref, bias_ref, down_ref, select_ref,
    driven_ref, partial_ref, pad_scr, rows_scr, out_scr
):
    thought_count, positions, _ = input_ref.shape
    taps = weight_ref.shape[0]
    rank = down_ref.shape[1]
    state_twice = select_ref.shape[1]
    tap_weights = weight_ref[...].astype(jnp.float32)
    for t in range(thought_count):
        pad_scr[0 : taps - 1, :] = conv_ref[fmap_ref[t]].astype(jnp.float32)
        pad_scr[taps - 1 : taps - 1 + positions, :] = input_ref[t].astype(jnp.float32)
        summed = bias_ref[...] + tap_weights[0:1, :] * pad_scr[0:positions, :]
        for offset in range(1, taps):
            summed = summed + tap_weights[offset : offset + 1, :] * pad_scr[
                offset : offset + positions, :
            ]
        driven = jax.nn.silu(summed).astype(jnp.bfloat16)
        driven_ref[t] = driven
        rows_scr[t * positions : (t + 1) * positions, :] = driven.astype(jnp.float32)
    token_rows = rows_scr[...].astype(jnp.bfloat16)
    out_scr[:, :rank] = jnp.dot(token_rows, down_ref[...], preferred_element_type=jnp.float32)
    out_scr[:, rank:] = jnp.dot(token_rows, select_ref[...], preferred_element_type=jnp.float32)
    for t in range(thought_count):
        block = out_scr[t * positions : (t + 1) * positions, :]
        select_part = block[:, rank:]
        select_high = select_part.astype(jnp.bfloat16)
        select_low = (select_part - select_high.astype(jnp.float32)).astype(jnp.bfloat16)
        partial_ref[t, :, :rank] = block[:, :rank].astype(jnp.bfloat16)
        partial_ref[t, :, rank : rank + state_twice] = select_high
        partial_ref[t, :, rank + state_twice :] = select_low


def project(parent_conv, fork_map, mixer_input, conv_weight, conv_bias, rate_down,
            selection_weight):
    thought_count, positions, width_local = mixer_input.shape
    taps = conv_weight.shape[0]
    rank, state_twice = rate_down.shape[1], selection_weight.shape[1]
    full = lambda shape: pl.BlockSpec(shape, lambda i, fmap: (0,) * len(shape))
    grid_spec = pltpu.PrefetchScalarGridSpec(
        num_scalar_prefetch=1,
        grid=(1,),
        in_specs=[
            full(parent_conv.shape),
            full(mixer_input.shape),
            full(conv_weight.shape),
            full((1, width_local)),
            full(rate_down.shape),
            full(selection_weight.shape),
        ],
        out_specs=[
            full(mixer_input.shape),
            full((thought_count, positions, rank + 2 * state_twice)),
        ],
        scratch_shapes=[
            pltpu.VMEM((taps - 1 + positions, width_local), jnp.float32),
            pltpu.VMEM((thought_count * positions, width_local), jnp.float32),
            pltpu.VMEM((thought_count * positions, rank + state_twice), jnp.float32),
        ],
    )
    return pl.pallas_call(
        project_kernel,
        grid_spec=grid_spec,
        out_shape=(
            jax.ShapeDtypeStruct(mixer_input.shape, jnp.bfloat16),
            jax.ShapeDtypeStruct((thought_count, positions, rank + 2 * state_twice), jnp.bfloat16),
        ),
    )(fork_map, parent_conv, mixer_input, conv_weight, conv_bias.reshape(1, width_local),
      rate_down, selection_weight)


def scan_kernel(
    lens_ref, fmap_ref, rate_ref, drive_ref, gate_ref, b_ref, c_ref, *rest
):
    pair = len(rest) - 6
    h0_refs, (a_ref, skip_ref, packed_ref, r_scr, u_scr, y_scr) = rest[:pair], rest[pair:]
    positions = rate_ref.shape[1]
    state_size = h0_refs[0].shape[1]
    decay = a_ref[...]
    states, lives = [], []
    for k in range(pair):
        live = jnp.clip(lens_ref[pl.program_id(0) * pair + k] + GEN, 0, positions)
        inflow = drive_ref[k].astype(jnp.float32)
        alive = lax.broadcasted_iota(jnp.int32, inflow.shape, 0) < live
        rate = jnp.where(alive, rate_ref[k], 0.0)
        r_scr[k] = rate
        u_scr[k] = rate * inflow
        states.append(h0_refs[k][0])
        lives.append(alive)
    for p in range(positions):
        for k in range(pair):
            b_col = b_ref[k][:, p : p + 1]
            c_col = c_ref[k][:, p : p + 1]
            h = states[k]
            rate_rows = r_scr[k, pl.ds(p, state_size, stride=0), :]
            push_rows = u_scr[k, pl.ds(p, state_size, stride=0), :]
            h = jnp.exp2(rate_rows * decay) * h + push_rows * b_col
            y_scr[k, p : p + 1, :] = jnp.sum(c_col * h, axis=0, keepdims=True)
            states[k] = h
    for k in range(pair):
        packed_ref[k, :state_size, :] = states[k].astype(packed_ref.dtype)
        inflow = drive_ref[k].astype(jnp.float32)
        gate = gate_ref[k].astype(jnp.float32)
        result = (y_scr[k] + skip_ref[...] * inflow) * jax.nn.silu(gate)
        packed_ref[k, state_size:, :] = jnp.where(lives[k], result, 0.0).astype(packed_ref.dtype)


def run_scan(judge_lengths, fork_map, step_rate, driven, gate_input, b_t, c_t, parent_state,
             decay_rate, skip_gain):
    thought_count, positions, width_local = driven.shape
    state_size = parent_state.shape[1]
    pair = 2 if thought_count % 2 == 0 else 1
    row_block = lambda t, lens, fmap: (t, 0, 0)
    whole = lambda t, lens, fmap: (0, 0)

    def state_block(k):
        return pl.BlockSpec(
            (1, state_size, width_local), lambda t, lens, fmap: (fmap[t * pair + k], 0, 0)
        )

    grid_spec = pltpu.PrefetchScalarGridSpec(
        num_scalar_prefetch=2,
        grid=(thought_count // pair,),
        in_specs=[
            pl.BlockSpec((pair, positions, width_local), row_block),
            pl.BlockSpec((pair, positions, width_local), row_block),
            pl.BlockSpec((pair, positions, width_local), row_block),
            pl.BlockSpec((pair, state_size, positions), row_block),
            pl.BlockSpec((pair, state_size, positions), row_block),
        ]
        + [state_block(k) for k in range(pair)]
        + [
            pl.BlockSpec((state_size, width_local), whole),
            pl.BlockSpec((1, width_local), whole),
        ],
        out_specs=pl.BlockSpec((pair, state_size + positions, width_local), row_block),
        scratch_shapes=[pltpu.VMEM((pair, positions, width_local), jnp.float32)] * 3,
    )
    return pl.pallas_call(
        scan_kernel,
        grid_spec=grid_spec,
        out_shape=jax.ShapeDtypeStruct(
            (thought_count, state_size + positions, width_local), jnp.bfloat16
        ),
        compiler_params=pltpu.CompilerParams(dimension_semantics=("arbitrary",)),
    )(judge_lengths, fork_map, step_rate, driven, gate_input, b_t, c_t,
      *([parent_state] * pair), decay_rate, skip_gain.reshape(1, width_local))


def body(
    parent_state,
    parent_conv,
    fork_map,
    judge_lengths,
    mixer_input,
    gate_input,
    conv_weight,
    conv_bias,
    rate_down,
    selection_weight,
    rate_up,
    rate_bias,
    decay_log,
    skip_gain,
):
    thought_count, positions, width_local = mixer_input.shape
    state_size = parent_state.shape[1]
    rank = rate_down.shape[1]
    driven, partial = project(
        parent_conv, fork_map, mixer_input, conv_weight, conv_bias, rate_down, selection_weight
    )
    devices = lax.axis_size("chan")
    pieces = lax.all_to_all(
        partial.reshape(devices, -1, partial.shape[2]), "chan", 0, 0, tiled=True
    ).astype(jnp.float32)
    reduced = jnp.sum(pieces, axis=0)
    low_mine = reduced[:, :rank].astype(jnp.bfloat16)
    select_sum = reduced[:, rank : rank + 2 * state_size] + reduced[:, rank + 2 * state_size :]
    select_high = select_sum.astype(jnp.bfloat16)
    select_low = (select_sum - select_high.astype(jnp.float32)).astype(jnp.bfloat16)
    mine = jnp.concatenate([low_mine, select_high, select_low], axis=1)
    gathered = lax.all_to_all(
        jnp.broadcast_to(mine[None], (devices,) + mine.shape), "chan", 0, 0, tiled=True
    ).reshape(-1, mine.shape[1])
    rate_low = gathered[:, :rank]
    selection = (
        gathered[:, rank : rank + 2 * state_size].astype(jnp.float32)
        + gathered[:, rank + 2 * state_size :].astype(jnp.float32)
    ).reshape(thought_count, positions, 2 * state_size)
    step_rate = jax.nn.softplus(
        jnp.dot(rate_low, rate_up, preferred_element_type=jnp.float32) + rate_bias[None, :]
    ).reshape(thought_count, positions, width_local)
    b_t = jnp.swapaxes(selection[:, :, :state_size], 1, 2)
    c_t = jnp.swapaxes(selection[:, :, state_size:], 1, 2)
    decay_rate = -jnp.exp(decay_log) * 1.4426950408889634
    packed_local = run_scan(
        judge_lengths, fork_map, step_rate, driven, gate_input, b_t, c_t, parent_state,
        decay_rate, skip_gain,
    )
    packed = lax.all_to_all(packed_local, "chan", split_axis=0, concat_axis=2, tiled=True)
    final_state = packed[:, :state_size].astype(jnp.float32)
    mixer_output = packed[:, state_size:]
    return (mixer_output, final_state)


def solution(mesh):
    placed = (
        P("group", None, "chan"),
        P("group", None, "chan"),
        P("group"),
        P("group"),
        P("group", None, "chan"),
        P("group", None, "chan"),
        P(None, "chan"),
        P("chan"),
        P("chan", None),
        P("chan", None),
        P(None, "chan"),
        P("chan"),
        P(None, "chan"),
        P("chan"),
    )
    return jax.shard_map(
        body,
        mesh=mesh,
        in_specs=placed,
        out_specs=(P(("group", "chan"), None, None), P(("group", "chan"), None, None)),
        check_vma=False,
    )
```

```python
import jax
import jax.numpy as jnp
from jax import lax
from jax.experimental import pallas as pl
from jax.experimental.pallas import tpu as pltpu
from jax.sharding import PartitionSpec as P

GEN = 4


def project_kernel(
    fmap_ref, conv_ref, input_ref, weight_ref, bias_ref, down_ref, select_ref,
    driven_ref, partial_ref, pad_scr, rows_scr, out_scr
):
    positions, thought_count, _ = input_ref.shape
    taps = weight_ref.shape[0]
    rank = down_ref.shape[1]
    state_twice = select_ref.shape[0]
    tap_weights = weight_ref[...].astype(jnp.float32)
    for t in range(thought_count):
        for tap in range(taps - 1):
            pad_scr[tap : tap + 1, :] = conv_ref[tap, pl.ds(fmap_ref[t], 1), :].astype(
                jnp.float32
            )
        pad_scr[taps - 1 : taps - 1 + positions, :] = input_ref[:, t, :].astype(jnp.float32)
        summed = bias_ref[...] + tap_weights[0:1, :] * pad_scr[0:positions, :]
        for offset in range(1, taps):
            summed = summed + tap_weights[offset : offset + 1, :] * pad_scr[
                offset : offset + positions, :
            ]
        driven = jax.nn.silu(summed).astype(jnp.bfloat16)
        driven_ref[t] = driven
        rows_scr[t * positions : (t + 1) * positions, :] = driven.astype(jnp.float32)
    token_rows = rows_scr[...].astype(jnp.bfloat16)
    out_scr[:, :rank] = jnp.dot(token_rows, down_ref[...], preferred_element_type=jnp.float32)
    out_scr[:, rank:] = lax.dot_general(
        token_rows, select_ref[...], (((1,), (1,)), ((), ())),
        preferred_element_type=jnp.float32,
    )
    for t in range(thought_count):
        block = out_scr[t * positions : (t + 1) * positions, :]
        select_part = block[:, rank:]
        select_high = select_part.astype(jnp.bfloat16)
        select_low = (select_part - select_high.astype(jnp.float32)).astype(jnp.bfloat16)
        partial_ref[t, :, :rank] = block[:, :rank].astype(jnp.bfloat16)
        partial_ref[t, :, rank : rank + state_twice] = select_high
        partial_ref[t, :, rank + state_twice :] = select_low


def project(parent_conv, fork_map, mixer_input, conv_weight, conv_bias, rate_down,
            selection_weight):
    thought_count, positions, width_local = mixer_input.shape
    taps = conv_weight.shape[0]
    rank, state_twice = rate_down.shape[1], selection_weight.shape[1]
    conv_view = jnp.transpose(parent_conv, (1, 0, 2)).astype(jnp.float32)
    input_view = jnp.transpose(mixer_input, (1, 0, 2))
    select_view = jnp.transpose(selection_weight)
    full = lambda shape: pl.BlockSpec(shape, lambda i, fmap: (0,) * len(shape))
    grid_spec = pltpu.PrefetchScalarGridSpec(
        num_scalar_prefetch=1,
        grid=(1,),
        in_specs=[
            full(conv_view.shape),
            full(input_view.shape),
            full(conv_weight.shape),
            full((1, width_local)),
            full(rate_down.shape),
            full(select_view.shape),
        ],
        out_specs=[
            full(mixer_input.shape),
            full((thought_count, positions, rank + 2 * state_twice)),
        ],
        scratch_shapes=[
            pltpu.VMEM((taps - 1 + positions, width_local), jnp.float32),
            pltpu.VMEM((thought_count * positions, width_local), jnp.float32),
            pltpu.VMEM((thought_count * positions, rank + state_twice), jnp.float32),
        ],
    )
    return pl.pallas_call(
        project_kernel,
        grid_spec=grid_spec,
        out_shape=(
            jax.ShapeDtypeStruct(mixer_input.shape, jnp.bfloat16),
            jax.ShapeDtypeStruct((thought_count, positions, rank + 2 * state_twice), jnp.bfloat16),
        ),
    )(fork_map, conv_view, input_view, conv_weight, conv_bias.reshape(1, width_local),
      rate_down, select_view)


def scan_kernel(
    lens_ref, fmap_ref, rate_ref, drive_ref, gate_ref, b_ref, c_ref, *rest
):
    pair = len(rest) - 6
    h0_refs, (a_ref, skip_ref, packed_ref, r_scr, u_scr, y_scr) = rest[:pair], rest[pair:]
    positions = rate_ref.shape[1]
    state_size = h0_refs[0].shape[1]
    decay = a_ref[...]
    states, lives = [], []
    for k in range(pair):
        live = jnp.clip(lens_ref[pl.program_id(0) * pair + k] + GEN, 0, positions)
        inflow = drive_ref[k].astype(jnp.float32)
        alive = lax.broadcasted_iota(jnp.int32, inflow.shape, 0) < live
        rate = jnp.where(alive, rate_ref[k], 0.0)
        r_scr[k] = rate
        u_scr[k] = rate * inflow
        states.append(h0_refs[k][0])
        lives.append(alive)
    for p in range(positions):
        for k in range(pair):
            b_col = b_ref[k][:, p : p + 1]
            c_col = c_ref[k][:, p : p + 1]
            h = states[k]
            rate_rows = r_scr[k, pl.ds(p, state_size, stride=0), :]
            push_rows = u_scr[k, pl.ds(p, state_size, stride=0), :]
            h = jnp.exp2(rate_rows * decay) * h + push_rows * b_col
            y_scr[k, p : p + 1, :] = jnp.sum(c_col * h, axis=0, keepdims=True)
            states[k] = h
    for k in range(pair):
        packed_ref[k, :state_size, :] = states[k].astype(packed_ref.dtype)
        inflow = drive_ref[k].astype(jnp.float32)
        gate = gate_ref[k].astype(jnp.float32)
        result = (y_scr[k] + skip_ref[...] * inflow) * jax.nn.silu(gate)
        packed_ref[k, state_size:, :] = jnp.where(lives[k], result, 0.0).astype(packed_ref.dtype)


def run_scan(judge_lengths, fork_map, step_rate, driven, gate_input, b_t, c_t, parent_state,
             decay_rate, skip_gain):
    thought_count, positions, width_local = driven.shape
    state_size = parent_state.shape[1]
    pair = 2 if thought_count % 2 == 0 else 1
    row_block = lambda t, lens, fmap: (t, 0, 0)
    whole = lambda t, lens, fmap: (0, 0)

    def state_block(k):
        return pl.BlockSpec(
            (1, state_size, width_local), lambda t, lens, fmap: (fmap[t * pair + k], 0, 0)
        )

    grid_spec = pltpu.PrefetchScalarGridSpec(
        num_scalar_prefetch=2,
        grid=(thought_count // pair,),
        in_specs=[
            pl.BlockSpec((pair, positions, width_local), row_block),
            pl.BlockSpec((pair, positions, width_local), row_block),
            pl.BlockSpec((pair, positions, width_local), row_block),
            pl.BlockSpec((pair, state_size, positions), row_block),
            pl.BlockSpec((pair, state_size, positions), row_block),
        ]
        + [state_block(k) for k in range(pair)]
        + [
            pl.BlockSpec((state_size, width_local), whole),
            pl.BlockSpec((1, width_local), whole),
        ],
        out_specs=pl.BlockSpec((pair, state_size + positions, width_local), row_block),
        scratch_shapes=[pltpu.VMEM((pair, positions, width_local), jnp.float32)] * 3,
    )
    return pl.pallas_call(
        scan_kernel,
        grid_spec=grid_spec,
        out_shape=jax.ShapeDtypeStruct(
            (thought_count, state_size + positions, width_local), jnp.bfloat16
        ),
        compiler_params=pltpu.CompilerParams(dimension_semantics=("arbitrary",)),
    )(judge_lengths, fork_map, step_rate, driven, gate_input, b_t, c_t,
      *([parent_state] * pair), decay_rate, skip_gain.reshape(1, width_local))


def body(
    parent_state,
    parent_conv,
    fork_map,
    judge_lengths,
    mixer_input,
    gate_input,
    conv_weight,
    conv_bias,
    rate_down,
    selection_weight,
    rate_up,
    rate_bias,
    decay_log,
    skip_gain,
):
    thought_count, positions, width_local = mixer_input.shape
    state_size = parent_state.shape[1]
    rank = rate_down.shape[1]
    driven, partial = project(
        parent_conv, fork_map, mixer_input, conv_weight, conv_bias, rate_down, selection_weight
    )
    devices = lax.axis_size("chan")
    pieces = lax.all_to_all(
        partial.reshape(devices, -1, partial.shape[2]), "chan", 0, 0, tiled=True
    ).astype(jnp.float32)
    reduced = jnp.sum(pieces, axis=0)
    low_mine = reduced[:, :rank].astype(jnp.bfloat16)
    select_sum = reduced[:, rank : rank + 2 * state_size] + reduced[:, rank + 2 * state_size :]
    select_high = select_sum.astype(jnp.bfloat16)
    select_low = (select_sum - select_high.astype(jnp.float32)).astype(jnp.bfloat16)
    mine = jnp.concatenate([low_mine, select_high, select_low], axis=1)
    gathered = lax.all_to_all(
        jnp.broadcast_to(mine[None], (devices,) + mine.shape), "chan", 0, 0, tiled=True
    ).reshape(-1, mine.shape[1])
    rate_low = gathered[:, :rank]
    selection = (
        gathered[:, rank : rank + 2 * state_size].astype(jnp.float32)
        + gathered[:, rank + 2 * state_size :].astype(jnp.float32)
    ).reshape(thought_count, positions, 2 * state_size)
    step_rate = jax.nn.softplus(
        jnp.dot(rate_low, rate_up, preferred_element_type=jnp.float32) + rate_bias[None, :]
    ).reshape(thought_count, positions, width_local)
    b_t = jnp.swapaxes(selection[:, :, :state_size], 1, 2)
    c_t = jnp.swapaxes(selection[:, :, state_size:], 1, 2)
    decay_rate = -jnp.exp(decay_log) * 1.4426950408889634
    packed_local = run_scan(
        judge_lengths, fork_map, step_rate, driven, gate_input, b_t, c_t, parent_state,
        decay_rate, skip_gain,
    )
    packed = lax.all_to_all(packed_local, "chan", split_axis=0, concat_axis=2, tiled=True)
    final_state = packed[:, :state_size].astype(jnp.float32)
    mixer_output = packed[:, state_size:]
    return (mixer_output, final_state)


def solution(mesh):
    placed = (
        P("group", None, "chan"),
        P("group", None, "chan"),
        P("group"),
        P("group"),
        P("group", None, "chan"),
        P("group", None, "chan"),
        P(None, "chan"),
        P("chan"),
        P("chan", None),
        P("chan", None),
        P(None, "chan"),
        P("chan"),
        P(None, "chan"),
        P("chan"),
    )
    return jax.shard_map(
        body,
        mesh=mesh,
        in_specs=placed,
        out_specs=(P(("group", "chan"), None, None), P(("group", "chan"), None, None)),
        check_vma=False,
    )
```

```python
import jax
import jax.numpy as jnp
from jax import lax
from jax.experimental import pallas as pl
from jax.experimental.pallas import tpu as pltpu
from jax.sharding import PartitionSpec as P

GEN = 4


def project_kernel(
    fmap_ref, conv_ref, input_ref, weight_ref, bias_ref, down_ref, select_ref,
    driven_ref, partial_ref, pad_scr, rows_scr, out_scr
):
    positions, thought_count, _ = input_ref.shape
    taps = weight_ref.shape[0]
    rank = down_ref.shape[1]
    state_twice = select_ref.shape[0]
    tap_weights = weight_ref[...].astype(jnp.float32)
    parents = conv_ref.shape[1]
    row = lax.broadcasted_iota(jnp.int32, (thought_count, parents), 0)
    col = lax.broadcasted_iota(jnp.int32, (thought_count, parents), 1)
    pick = jnp.zeros((thought_count, parents), jnp.float32)
    for t in range(thought_count):
        pick = jnp.where((row == t) & (col == fmap_ref[t]), 1.0, pick)
    pick = pick.astype(jnp.bfloat16)
    starts = [
        jnp.dot(pick, conv_ref[tap], preferred_element_type=jnp.float32)
        for tap in range(taps - 1)
    ]
    for t in range(thought_count):
        for tap in range(taps - 1):
            pad_scr[tap : tap + 1, :] = starts[tap][t : t + 1, :]
        pad_scr[taps - 1 : taps - 1 + positions, :] = input_ref[:, t, :].astype(jnp.float32)
        summed = bias_ref[...] + tap_weights[0:1, :] * pad_scr[0:positions, :]
        for offset in range(1, taps):
            summed = summed + tap_weights[offset : offset + 1, :] * pad_scr[
                offset : offset + positions, :
            ]
        driven = jax.nn.silu(summed).astype(jnp.bfloat16)
        driven_ref[t] = driven
        rows_scr[t * positions : (t + 1) * positions, :] = driven.astype(jnp.float32)
    token_rows = rows_scr[...].astype(jnp.bfloat16)
    out_scr[:, :rank] = jnp.dot(token_rows, down_ref[...], preferred_element_type=jnp.float32)
    out_scr[:, rank:] = lax.dot_general(
        token_rows, select_ref[...], (((1,), (1,)), ((), ())),
        preferred_element_type=jnp.float32,
    )
    for t in range(thought_count):
        block = out_scr[t * positions : (t + 1) * positions, :]
        select_part = block[:, rank:]
        select_high = select_part.astype(jnp.bfloat16)
        select_low = (select_part - select_high.astype(jnp.float32)).astype(jnp.bfloat16)
        partial_ref[t, :, :rank] = block[:, :rank].astype(jnp.bfloat16)
        partial_ref[t, :, rank : rank + state_twice] = select_high
        partial_ref[t, :, rank + state_twice :] = select_low


def project(parent_conv, fork_map, mixer_input, conv_weight, conv_bias, rate_down,
            selection_weight):
    thought_count, positions, width_local = mixer_input.shape
    taps = conv_weight.shape[0]
    rank, state_twice = rate_down.shape[1], selection_weight.shape[1]
    conv_view = jnp.transpose(parent_conv, (1, 0, 2))
    input_view = jnp.transpose(mixer_input, (1, 0, 2))
    select_view = jnp.transpose(selection_weight)
    full = lambda shape: pl.BlockSpec(shape, lambda i, fmap: (0,) * len(shape))
    grid_spec = pltpu.PrefetchScalarGridSpec(
        num_scalar_prefetch=1,
        grid=(1,),
        in_specs=[
            full(conv_view.shape),
            full(input_view.shape),
            full(conv_weight.shape),
            full((1, width_local)),
            full(rate_down.shape),
            full(select_view.shape),
        ],
        out_specs=[
            full(mixer_input.shape),
            full((thought_count, positions, rank + 2 * state_twice)),
        ],
        scratch_shapes=[
            pltpu.VMEM((taps - 1 + positions, width_local), jnp.float32),
            pltpu.VMEM((thought_count * positions, width_local), jnp.float32),
            pltpu.VMEM((thought_count * positions, rank + state_twice), jnp.float32),
        ],
    )
    return pl.pallas_call(
        project_kernel,
        grid_spec=grid_spec,
        out_shape=(
            jax.ShapeDtypeStruct(mixer_input.shape, jnp.bfloat16),
            jax.ShapeDtypeStruct((thought_count, positions, rank + 2 * state_twice), jnp.bfloat16),
        ),
    )(fork_map, conv_view, input_view, conv_weight, conv_bias.reshape(1, width_local),
      rate_down, select_view)


def scan_kernel(
    lens_ref, fmap_ref, rate_ref, drive_ref, gate_ref, b_ref, c_ref, *rest
):
    pair = len(rest) - 6
    h0_refs, (a_ref, skip_ref, packed_ref, r_scr, u_scr, y_scr) = rest[:pair], rest[pair:]
    positions = rate_ref.shape[1]
    state_size = h0_refs[0].shape[1]
    decay = a_ref[...]
    states, lives = [], []
    for k in range(pair):
        live = jnp.clip(lens_ref[pl.program_id(0) * pair + k] + GEN, 0, positions)
        inflow = drive_ref[k].astype(jnp.float32)
        alive = lax.broadcasted_iota(jnp.int32, inflow.shape, 0) < live
        rate = jnp.where(alive, rate_ref[k], 0.0)
        r_scr[k] = rate
        u_scr[k] = rate * inflow
        states.append(h0_refs[k][0])
        lives.append(alive)
    for p in range(positions):
        for k in range(pair):
            b_col = b_ref[k][:, p : p + 1]
            c_col = c_ref[k][:, p : p + 1]
            h = states[k]
            rate_rows = r_scr[k, pl.ds(p, state_size, stride=0), :]
            push_rows = u_scr[k, pl.ds(p, state_size, stride=0), :]
            h = jnp.exp2(rate_rows * decay) * h + push_rows * b_col
            y_scr[k, p : p + 1, :] = jnp.sum(c_col * h, axis=0, keepdims=True)
            states[k] = h
    for k in range(pair):
        packed_ref[k, :state_size, :] = states[k].astype(packed_ref.dtype)
        inflow = drive_ref[k].astype(jnp.float32)
        gate = gate_ref[k].astype(jnp.float32)
        result = (y_scr[k] + skip_ref[...] * inflow) * jax.nn.silu(gate)
        packed_ref[k, state_size:, :] = jnp.where(lives[k], result, 0.0).astype(packed_ref.dtype)


def run_scan(judge_lengths, fork_map, step_rate, driven, gate_input, b_t, c_t, parent_state,
             decay_rate, skip_gain):
    thought_count, positions, width_local = driven.shape
    state_size = parent_state.shape[1]
    pair = 2 if thought_count % 2 == 0 else 1
    row_block = lambda t, lens, fmap: (t, 0, 0)
    whole = lambda t, lens, fmap: (0, 0)

    def state_block(k):
        return pl.BlockSpec(
            (1, state_size, width_local), lambda t, lens, fmap: (fmap[t * pair + k], 0, 0)
        )

    grid_spec = pltpu.PrefetchScalarGridSpec(
        num_scalar_prefetch=2,
        grid=(thought_count // pair,),
        in_specs=[
            pl.BlockSpec((pair, positions, width_local), row_block),
            pl.BlockSpec((pair, positions, width_local), row_block),
            pl.BlockSpec((pair, positions, width_local), row_block),
            pl.BlockSpec((pair, state_size, positions), row_block),
            pl.BlockSpec((pair, state_size, positions), row_block),
        ]
        + [state_block(k) for k in range(pair)]
        + [
            pl.BlockSpec((state_size, width_local), whole),
            pl.BlockSpec((1, width_local), whole),
        ],
        out_specs=pl.BlockSpec((pair, state_size + positions, width_local), row_block),
        scratch_shapes=[pltpu.VMEM((pair, positions, width_local), jnp.float32)] * 3,
    )
    return pl.pallas_call(
        scan_kernel,
        grid_spec=grid_spec,
        out_shape=jax.ShapeDtypeStruct(
            (thought_count, state_size + positions, width_local), jnp.bfloat16
        ),
        compiler_params=pltpu.CompilerParams(dimension_semantics=("arbitrary",)),
    )(judge_lengths, fork_map, step_rate, driven, gate_input, b_t, c_t,
      *([parent_state] * pair), decay_rate, skip_gain.reshape(1, width_local))


def body(
    parent_state,
    parent_conv,
    fork_map,
    judge_lengths,
    mixer_input,
    gate_input,
    conv_weight,
    conv_bias,
    rate_down,
    selection_weight,
    rate_up,
    rate_bias,
    decay_log,
    skip_gain,
):
    thought_count, positions, width_local = mixer_input.shape
    state_size = parent_state.shape[1]
    rank = rate_down.shape[1]
    driven, partial = project(
        parent_conv, fork_map, mixer_input, conv_weight, conv_bias, rate_down, selection_weight
    )
    devices = lax.axis_size("chan")
    pieces = lax.all_to_all(
        partial.reshape(devices, -1, partial.shape[2]), "chan", 0, 0, tiled=True
    ).astype(jnp.float32)
    reduced = jnp.sum(pieces, axis=0)
    low_mine = reduced[:, :rank].astype(jnp.bfloat16)
    select_sum = reduced[:, rank : rank + 2 * state_size] + reduced[:, rank + 2 * state_size :]
    select_high = select_sum.astype(jnp.bfloat16)
    select_low = (select_sum - select_high.astype(jnp.float32)).astype(jnp.bfloat16)
    mine = jnp.concatenate([low_mine, select_high, select_low], axis=1)
    gathered = lax.all_to_all(
        jnp.broadcast_to(mine[None], (devices,) + mine.shape), "chan", 0, 0, tiled=True
    ).reshape(-1, mine.shape[1])
    rate_low = gathered[:, :rank]
    selection = (
        gathered[:, rank : rank + 2 * state_size].astype(jnp.float32)
        + gathered[:, rank + 2 * state_size :].astype(jnp.float32)
    ).reshape(thought_count, positions, 2 * state_size)
    step_rate = jax.nn.softplus(
        jnp.dot(rate_low, rate_up, preferred_element_type=jnp.float32) + rate_bias[None, :]
    ).reshape(thought_count, positions, width_local)
    b_t = jnp.swapaxes(selection[:, :, :state_size], 1, 2)
    c_t = jnp.swapaxes(selection[:, :, state_size:], 1, 2)
    decay_rate = -jnp.exp(decay_log) * 1.4426950408889634
    packed_local = run_scan(
        judge_lengths, fork_map, step_rate, driven, gate_input, b_t, c_t, parent_state,
        decay_rate, skip_gain,
    )
    packed = lax.all_to_all(packed_local, "chan", split_axis=0, concat_axis=2, tiled=True)
    final_state = packed[:, :state_size].astype(jnp.float32)
    mixer_output = packed[:, state_size:]
    return (mixer_output, final_state)


def solution(mesh):
    placed = (
        P("group", None, "chan"),
        P("group", None, "chan"),
        P("group"),
        P("group"),
        P("group", None, "chan"),
        P("group", None, "chan"),
        P(None, "chan"),
        P("chan"),
        P("chan", None),
        P("chan", None),
        P(None, "chan"),
        P("chan"),
        P(None, "chan"),
        P("chan"),
    )
    return jax.shard_map(
        body,
        mesh=mesh,
        in_specs=placed,
        out_specs=(P(("group", "chan"), None, None), P(("group", "chan"), None, None)),
        check_vma=False,
    )
```

```python
import jax
import jax.numpy as jnp
from jax import lax
from jax.experimental import pallas as pl
from jax.experimental.pallas import tpu as pltpu
from jax.sharding import PartitionSpec as P

GEN = 4


def project_kernel(
    fmap_ref, conv_ref, input_ref, weight_ref, bias_ref, down_ref, select_ref,
    driven_ref, partial_ref, pad_scr, rows_scr, out_scr
):
    positions, thought_count, _ = input_ref.shape
    taps = weight_ref.shape[0]
    rank = down_ref.shape[1]
    state_twice = select_ref.shape[0]
    tap_weights = weight_ref[...].astype(jnp.float32)
    parents = conv_ref.shape[1]
    row = lax.broadcasted_iota(jnp.int32, (thought_count, parents), 0)
    col = lax.broadcasted_iota(jnp.int32, (thought_count, parents), 1)
    pick = jnp.zeros((thought_count, parents), jnp.float32)
    for t in range(thought_count):
        pick = jnp.where((row == t) & (col == fmap_ref[t]), 1.0, pick)
    pick = pick.astype(jnp.bfloat16)
    starts = [
        jnp.dot(pick, conv_ref[tap], preferred_element_type=jnp.float32)
        for tap in range(taps - 1)
    ]
    for t in range(thought_count):
        for tap in range(taps - 1):
            pad_scr[tap : tap + 1, :] = starts[tap][t : t + 1, :]
        pad_scr[taps - 1 : taps - 1 + positions, :] = input_ref[:, t, :].astype(jnp.float32)
        summed = bias_ref[...] + tap_weights[0:1, :] * pad_scr[0:positions, :]
        for offset in range(1, taps):
            summed = summed + tap_weights[offset : offset + 1, :] * pad_scr[
                offset : offset + positions, :
            ]
        driven = jax.nn.silu(summed).astype(jnp.bfloat16)
        driven_ref[t] = driven
        rows_scr[t * positions : (t + 1) * positions, :] = driven.astype(jnp.float32)
    token_rows = rows_scr[...].astype(jnp.bfloat16)
    out_scr[:, :rank] = jnp.dot(token_rows, down_ref[...], preferred_element_type=jnp.float32)
    out_scr[:, rank:] = lax.dot_general(
        token_rows, select_ref[...], (((1,), (1,)), ((), ())),
        preferred_element_type=jnp.float32,
    )
    for t in range(thought_count):
        block = out_scr[t * positions : (t + 1) * positions, :]
        select_part = block[:, rank:]
        select_high = select_part.astype(jnp.bfloat16)
        select_low = (select_part - select_high.astype(jnp.float32)).astype(jnp.bfloat16)
        partial_ref[t, :, :rank] = block[:, :rank].astype(jnp.bfloat16)
        partial_ref[t, :, rank : rank + state_twice] = select_high
        partial_ref[t, :, rank + state_twice :] = select_low


def project(parent_conv, fork_map, mixer_input, conv_weight, conv_bias, rate_down,
            selection_weight):
    thought_count, positions, width_local = mixer_input.shape
    taps = conv_weight.shape[0]
    rank, state_twice = rate_down.shape[1], selection_weight.shape[1]
    conv_view = jnp.transpose(parent_conv, (1, 0, 2))
    input_view = jnp.transpose(mixer_input, (1, 0, 2))
    select_view = jnp.transpose(selection_weight)
    full = lambda shape: pl.BlockSpec(shape, lambda i, fmap: (0,) * len(shape))
    grid_spec = pltpu.PrefetchScalarGridSpec(
        num_scalar_prefetch=1,
        grid=(1,),
        in_specs=[
            full(conv_view.shape),
            full(input_view.shape),
            full(conv_weight.shape),
            full((1, width_local)),
            full(rate_down.shape),
            full(select_view.shape),
        ],
        out_specs=[
            full(mixer_input.shape),
            full((thought_count, positions, rank + 2 * state_twice)),
        ],
        scratch_shapes=[
            pltpu.VMEM((taps - 1 + positions, width_local), jnp.float32),
            pltpu.VMEM((thought_count * positions, width_local), jnp.float32),
            pltpu.VMEM((thought_count * positions, rank + state_twice), jnp.float32),
        ],
    )
    return pl.pallas_call(
        project_kernel,
        grid_spec=grid_spec,
        out_shape=(
            jax.ShapeDtypeStruct(mixer_input.shape, jnp.bfloat16),
            jax.ShapeDtypeStruct((thought_count, positions, rank + 2 * state_twice), jnp.bfloat16),
        ),
    )(fork_map, conv_view, input_view, conv_weight, conv_bias.reshape(1, width_local),
      rate_down, select_view)


def scan_kernel(
    lens_ref, fmap_ref, rate_ref, drive_ref, gate_ref, b_ref, c_ref, *rest
):
    pair = len(rest) - 6
    h0_refs, (a_ref, skip_ref, packed_ref, r_scr, u_scr, y_scr) = rest[:pair], rest[pair:]
    positions = drive_ref.shape[1]
    state_size = h0_refs[0].shape[1]
    decay = a_ref[...]
    states, lives = [], []
    for k in range(pair):
        live = jnp.clip(lens_ref[pl.program_id(0) * pair + k] + GEN, 0, positions)
        inflow = drive_ref[k].astype(jnp.float32)
        alive = lax.broadcasted_iota(jnp.int32, inflow.shape, 0) < live
        rate = jnp.where(alive, rate_ref[k * positions : (k + 1) * positions, :], 0.0)
        r_scr[k] = rate
        u_scr[k] = rate * inflow
        states.append(h0_refs[k][0])
        lives.append(alive)
    for p in range(positions):
        for k in range(pair):
            b_col = b_ref[k][:, p : p + 1]
            c_col = c_ref[k][:, p : p + 1]
            h = states[k]
            rate_rows = r_scr[k, pl.ds(p, state_size, stride=0), :]
            push_rows = u_scr[k, pl.ds(p, state_size, stride=0), :]
            h = jnp.exp2(rate_rows * decay) * h + push_rows * b_col
            y_scr[k, p : p + 1, :] = jnp.sum(c_col * h, axis=0, keepdims=True)
            states[k] = h
    for k in range(pair):
        packed_ref[k, :state_size, :] = states[k].astype(packed_ref.dtype)
        inflow = drive_ref[k].astype(jnp.float32)
        gate = gate_ref[k].astype(jnp.float32)
        result = (y_scr[k] + skip_ref[...] * inflow) * jax.nn.silu(gate)
        packed_ref[k, state_size:, :] = jnp.where(lives[k], result, 0.0).astype(packed_ref.dtype)


def run_scan(judge_lengths, fork_map, step_rate, driven, gate_input, b_t, c_t, parent_state,
             decay_rate, skip_gain):
    thought_count, positions, width_local = driven.shape
    state_size = parent_state.shape[1]
    pair = 2 if thought_count % 2 == 0 else 1
    row_block = lambda t, lens, fmap: (t, 0, 0)
    whole = lambda t, lens, fmap: (0, 0)

    def state_block(k):
        return pl.BlockSpec(
            (1, state_size, width_local), lambda t, lens, fmap: (fmap[t * pair + k], 0, 0)
        )

    grid_spec = pltpu.PrefetchScalarGridSpec(
        num_scalar_prefetch=2,
        grid=(thought_count // pair,),
        in_specs=[
            pl.BlockSpec((pair * positions, width_local), lambda t, lens, fmap: (t, 0)),
            pl.BlockSpec((pair, positions, width_local), row_block),
            pl.BlockSpec((pair, positions, width_local), row_block),
            pl.BlockSpec((pair, state_size, positions), row_block),
            pl.BlockSpec((pair, state_size, positions), row_block),
        ]
        + [state_block(k) for k in range(pair)]
        + [
            pl.BlockSpec((state_size, width_local), whole),
            pl.BlockSpec((1, width_local), whole),
        ],
        out_specs=pl.BlockSpec((pair, state_size + positions, width_local), row_block),
        scratch_shapes=[pltpu.VMEM((pair, positions, width_local), jnp.float32)] * 3,
    )
    return pl.pallas_call(
        scan_kernel,
        grid_spec=grid_spec,
        out_shape=jax.ShapeDtypeStruct(
            (thought_count, state_size + positions, width_local), jnp.bfloat16
        ),
        compiler_params=pltpu.CompilerParams(dimension_semantics=("arbitrary",)),
    )(judge_lengths, fork_map, step_rate, driven, gate_input, b_t, c_t,
      *([parent_state] * pair), decay_rate, skip_gain.reshape(1, width_local))


def body(
    parent_state,
    parent_conv,
    fork_map,
    judge_lengths,
    mixer_input,
    gate_input,
    conv_weight,
    conv_bias,
    rate_down,
    selection_weight,
    rate_up,
    rate_bias,
    decay_log,
    skip_gain,
):
    thought_count, positions, width_local = mixer_input.shape
    state_size = parent_state.shape[1]
    rank = rate_down.shape[1]
    driven, partial = project(
        parent_conv, fork_map, mixer_input, conv_weight, conv_bias, rate_down, selection_weight
    )
    devices = lax.axis_size("chan")
    pieces = lax.all_to_all(
        partial.reshape(devices, -1, partial.shape[2]), "chan", 0, 0, tiled=True
    ).astype(jnp.float32)
    reduced = jnp.sum(pieces, axis=0)
    low_mine = reduced[:, :rank].astype(jnp.bfloat16)
    select_sum = reduced[:, rank : rank + 2 * state_size] + reduced[:, rank + 2 * state_size :]
    select_high = select_sum.astype(jnp.bfloat16)
    select_low = (select_sum - select_high.astype(jnp.float32)).astype(jnp.bfloat16)
    mine = jnp.concatenate([low_mine, select_high, select_low], axis=1)
    gathered = lax.all_to_all(
        jnp.broadcast_to(mine[None], (devices,) + mine.shape), "chan", 0, 0, tiled=True
    ).reshape(-1, mine.shape[1])
    rate_low = gathered[:, :rank]
    selection = (
        gathered[:, rank : rank + 2 * state_size].astype(jnp.float32)
        + gathered[:, rank + 2 * state_size :].astype(jnp.float32)
    ).reshape(thought_count, positions, 2 * state_size)
    step_rate = jax.nn.softplus(
        jnp.dot(rate_low, rate_up, preferred_element_type=jnp.float32) + rate_bias[None, :]
    )
    b_t = jnp.swapaxes(selection[:, :, :state_size], 1, 2)
    c_t = jnp.swapaxes(selection[:, :, state_size:], 1, 2)
    decay_rate = -jnp.exp(decay_log) * 1.4426950408889634
    packed_local = run_scan(
        judge_lengths, fork_map, step_rate, driven, gate_input, b_t, c_t, parent_state,
        decay_rate, skip_gain,
    )
    packed = lax.all_to_all(packed_local, "chan", split_axis=0, concat_axis=2, tiled=True)
    final_state = packed[:, :state_size].astype(jnp.float32)
    mixer_output = packed[:, state_size:]
    return (mixer_output, final_state)


def solution(mesh):
    placed = (
        P("group", None, "chan"),
        P("group", None, "chan"),
        P("group"),
        P("group"),
        P("group", None, "chan"),
        P("group", None, "chan"),
        P(None, "chan"),
        P("chan"),
        P("chan", None),
        P("chan", None),
        P(None, "chan"),
        P("chan"),
        P(None, "chan"),
        P("chan"),
    )
    return jax.shard_map(
        body,
        mesh=mesh,
        in_specs=placed,
        out_specs=(P(("group", "chan"), None, None), P(("group", "chan"), None, None)),
        check_vma=False,
    )
```

```python
import jax
import jax.numpy as jnp
from jax import lax
from jax.experimental import pallas as pl
from jax.experimental.pallas import tpu as pltpu
from jax.sharding import PartitionSpec as P

GEN = 4


def project_kernel(
    fmap_ref, conv_ref, input_ref, weight_ref, bias_ref, down_ref, select_ref,
    driven_ref, partial_ref, pad_scr, rows_scr, out_scr
):
    positions, thought_count, _ = input_ref.shape
    taps = weight_ref.shape[0]
    rank = down_ref.shape[1]
    state_twice = select_ref.shape[0]
    step = pl.program_id(0)
    tap_weights = weight_ref[...].astype(jnp.float32)
    parents = conv_ref.shape[1]
    row = lax.broadcasted_iota(jnp.int32, (thought_count, parents), 0)
    col = lax.broadcasted_iota(jnp.int32, (thought_count, parents), 1)
    pick = jnp.zeros((thought_count, parents), jnp.float32)
    for t in range(thought_count):
        pick = jnp.where((row == t) & (col == fmap_ref[t]), 1.0, pick)
    pick = pick.astype(jnp.bfloat16)
    starts = [
        jnp.dot(pick, conv_ref[tap], preferred_element_type=jnp.float32)
        for tap in range(taps - 1)
    ]
    for t in range(thought_count):
        for tap in range(taps - 1):
            pad_scr[tap : tap + 1, :] = starts[tap][t : t + 1, :]
        pad_scr[taps - 1 : taps - 1 + positions, :] = input_ref[:, t, :].astype(jnp.float32)
        summed = bias_ref[...] + tap_weights[0:1, :] * pad_scr[0:positions, :]
        for offset in range(1, taps):
            summed = summed + tap_weights[offset : offset + 1, :] * pad_scr[
                offset : offset + positions, :
            ]
        driven = jax.nn.silu(summed).astype(jnp.bfloat16)
        driven_ref[t] = driven
        rows_scr[t * positions : (t + 1) * positions, :] = driven.astype(jnp.float32)
    token_rows = rows_scr[...].astype(jnp.bfloat16)
    low = jnp.dot(token_rows, down_ref[...], preferred_element_type=jnp.float32)
    chosen = lax.dot_general(
        token_rows, select_ref[...], (((1,), (1,)), ((), ())),
        preferred_element_type=jnp.float32,
    )

    @pl.when(step == 0)
    def _():
        out_scr[:, :rank] = low
        out_scr[:, rank:] = chosen

    @pl.when(step > 0)
    def _():
        out_scr[:, :rank] += low
        out_scr[:, rank:] += chosen

    @pl.when(step == pl.num_programs(0) - 1)
    def _():
        for t in range(thought_count):
            block = out_scr[t * positions : (t + 1) * positions, :]
            select_part = block[:, rank:]
            select_high = select_part.astype(jnp.bfloat16)
            select_low = (select_part - select_high.astype(jnp.float32)).astype(jnp.bfloat16)
            partial_ref[t, :, :rank] = block[:, :rank].astype(jnp.bfloat16)
            partial_ref[t, :, rank : rank + state_twice] = select_high
            partial_ref[t, :, rank + state_twice :] = select_low


def project(parent_conv, fork_map, mixer_input, conv_weight, conv_bias, rate_down,
            selection_weight):
    thought_count, positions, width_local = mixer_input.shape
    taps = conv_weight.shape[0]
    rank, state_twice = rate_down.shape[1], selection_weight.shape[1]
    conv_view = jnp.transpose(parent_conv, (1, 0, 2))
    input_view = jnp.transpose(mixer_input, (1, 0, 2))
    select_view = jnp.transpose(selection_weight)
    steps = 2 if width_local % 256 == 0 else 1
    width = width_local // steps
    parents = conv_view.shape[1]
    grid_spec = pltpu.PrefetchScalarGridSpec(
        num_scalar_prefetch=1,
        grid=(steps,),
        in_specs=[
            pl.BlockSpec((taps - 1, parents, width), lambda i, fmap: (0, 0, i)),
            pl.BlockSpec((positions, thought_count, width), lambda i, fmap: (0, 0, i)),
            pl.BlockSpec((taps, width), lambda i, fmap: (0, i)),
            pl.BlockSpec((1, width), lambda i, fmap: (0, i)),
            pl.BlockSpec((width, rank), lambda i, fmap: (i, 0)),
            pl.BlockSpec((state_twice, width), lambda i, fmap: (0, i)),
        ],
        out_specs=[
            pl.BlockSpec((thought_count, positions, width), lambda i, fmap: (0, 0, i)),
            pl.BlockSpec(
                (thought_count, positions, rank + 2 * state_twice), lambda i, fmap: (0, 0, 0)
            ),
        ],
        scratch_shapes=[
            pltpu.VMEM((taps - 1 + positions, width), jnp.float32),
            pltpu.VMEM((thought_count * positions, width), jnp.float32),
            pltpu.VMEM((thought_count * positions, rank + state_twice), jnp.float32),
        ],
    )
    return pl.pallas_call(
        project_kernel,
        grid_spec=grid_spec,
        out_shape=(
            jax.ShapeDtypeStruct(mixer_input.shape, jnp.bfloat16),
            jax.ShapeDtypeStruct((thought_count, positions, rank + 2 * state_twice), jnp.bfloat16),
        ),
        compiler_params=pltpu.CompilerParams(dimension_semantics=("arbitrary",)),
    )(fork_map, conv_view, input_view, conv_weight, conv_bias.reshape(1, width_local),
      rate_down, select_view)


def scan_kernel(
    lens_ref, fmap_ref, rate_ref, drive_ref, gate_ref, b_ref, c_ref, *rest
):
    pair = len(rest) - 6
    h0_refs, (a_ref, skip_ref, packed_ref, r_scr, u_scr, y_scr) = rest[:pair], rest[pair:]
    positions = drive_ref.shape[1]
    state_size = h0_refs[0].shape[1]
    decay = a_ref[...]
    states, lives = [], []
    for k in range(pair):
        live = jnp.clip(lens_ref[pl.program_id(0) * pair + k] + GEN, 0, positions)
        inflow = drive_ref[k].astype(jnp.float32)
        alive = lax.broadcasted_iota(jnp.int32, inflow.shape, 0) < live
        rate = jnp.where(alive, rate_ref[k * positions : (k + 1) * positions, :], 0.0)
        r_scr[k] = rate
        u_scr[k] = rate * inflow
        states.append(h0_refs[k][0])
        lives.append(alive)
    for p in range(positions):
        for k in range(pair):
            b_col = b_ref[k][:, p : p + 1]
            c_col = c_ref[k][:, p : p + 1]
            h = states[k]
            rate_rows = r_scr[k, pl.ds(p, state_size, stride=0), :]
            push_rows = u_scr[k, pl.ds(p, state_size, stride=0), :]
            h = jnp.exp2(rate_rows * decay) * h + push_rows * b_col
            y_scr[k, p : p + 1, :] = jnp.sum(c_col * h, axis=0, keepdims=True)
            states[k] = h
    for k in range(pair):
        packed_ref[k, :state_size, :] = states[k].astype(packed_ref.dtype)
        inflow = drive_ref[k].astype(jnp.float32)
        gate = gate_ref[k].astype(jnp.float32)
        result = (y_scr[k] + skip_ref[...] * inflow) * jax.nn.silu(gate)
        packed_ref[k, state_size:, :] = jnp.where(lives[k], result, 0.0).astype(packed_ref.dtype)


def run_scan(judge_lengths, fork_map, step_rate, driven, gate_input, b_t, c_t, parent_state,
             decay_rate, skip_gain):
    thought_count, positions, width_local = driven.shape
    state_size = parent_state.shape[1]
    pair = 2 if thought_count % 2 == 0 else 1
    row_block = lambda t, lens, fmap: (t, 0, 0)
    whole = lambda t, lens, fmap: (0, 0)

    def state_block(k):
        return pl.BlockSpec(
            (1, state_size, width_local), lambda t, lens, fmap: (fmap[t * pair + k], 0, 0)
        )

    grid_spec = pltpu.PrefetchScalarGridSpec(
        num_scalar_prefetch=2,
        grid=(thought_count // pair,),
        in_specs=[
            pl.BlockSpec((pair * positions, width_local), lambda t, lens, fmap: (t, 0)),
            pl.BlockSpec((pair, positions, width_local), row_block),
            pl.BlockSpec((pair, positions, width_local), row_block),
            pl.BlockSpec((pair, state_size, positions), row_block),
            pl.BlockSpec((pair, state_size, positions), row_block),
        ]
        + [state_block(k) for k in range(pair)]
        + [
            pl.BlockSpec((state_size, width_local), whole),
            pl.BlockSpec((1, width_local), whole),
        ],
        out_specs=pl.BlockSpec((pair, state_size + positions, width_local), row_block),
        scratch_shapes=[pltpu.VMEM((pair, positions, width_local), jnp.float32)] * 3,
    )
    return pl.pallas_call(
        scan_kernel,
        grid_spec=grid_spec,
        out_shape=jax.ShapeDtypeStruct(
            (thought_count, state_size + positions, width_local), jnp.bfloat16
        ),
        compiler_params=pltpu.CompilerParams(dimension_semantics=("arbitrary",)),
    )(judge_lengths, fork_map, step_rate, driven, gate_input, b_t, c_t,
      *([parent_state] * pair), decay_rate, skip_gain.reshape(1, width_local))


def body(
    parent_state,
    parent_conv,
    fork_map,
    judge_lengths,
    mixer_input,
    gate_input,
    conv_weight,
    conv_bias,
    rate_down,
    selection_weight,
    rate_up,
    rate_bias,
    decay_log,
    skip_gain,
):
    thought_count, positions, width_local = mixer_input.shape
    state_size = parent_state.shape[1]
    rank = rate_down.shape[1]
    driven, partial = project(
        parent_conv, fork_map, mixer_input, conv_weight, conv_bias, rate_down, selection_weight
    )
    devices = lax.axis_size("chan")
    pieces = lax.all_to_all(
        partial.reshape(devices, -1, partial.shape[2]), "chan", 0, 0, tiled=True
    ).astype(jnp.float32)
    reduced = jnp.sum(pieces, axis=0)
    low_mine = reduced[:, :rank].astype(jnp.bfloat16)
    select_sum = reduced[:, rank : rank + 2 * state_size] + reduced[:, rank + 2 * state_size :]
    select_high = select_sum.astype(jnp.bfloat16)
    select_low = (select_sum - select_high.astype(jnp.float32)).astype(jnp.bfloat16)
    mine = jnp.concatenate([low_mine, select_high, select_low], axis=1)
    gathered = lax.all_to_all(
        jnp.broadcast_to(mine[None], (devices,) + mine.shape), "chan", 0, 0, tiled=True
    ).reshape(-1, mine.shape[1])
    rate_low = gathered[:, :rank]
    selection = (
        gathered[:, rank : rank + 2 * state_size].astype(jnp.float32)
        + gathered[:, rank + 2 * state_size :].astype(jnp.float32)
    ).reshape(thought_count, positions, 2 * state_size)
    step_rate = jax.nn.softplus(
        jnp.dot(rate_low, rate_up, preferred_element_type=jnp.float32) + rate_bias[None, :]
    )
    b_t = jnp.swapaxes(selection[:, :, :state_size], 1, 2)
    c_t = jnp.swapaxes(selection[:, :, state_size:], 1, 2)
    decay_rate = -jnp.exp(decay_log) * 1.4426950408889634
    packed_local = run_scan(
        judge_lengths, fork_map, step_rate, driven, gate_input, b_t, c_t, parent_state,
        decay_rate, skip_gain,
    )
    packed = lax.all_to_all(packed_local, "chan", split_axis=0, concat_axis=2, tiled=True)
    final_state = packed[:, :state_size].astype(jnp.float32)
    mixer_output = packed[:, state_size:]
    return (mixer_output, final_state)


def solution(mesh):
    placed = (
        P("group", None, "chan"),
        P("group", None, "chan"),
        P("group"),
        P("group"),
        P("group", None, "chan"),
        P("group", None, "chan"),
        P(None, "chan"),
        P("chan"),
        P("chan", None),
        P("chan", None),
        P(None, "chan"),
        P("chan"),
        P(None, "chan"),
        P("chan"),
    )
    return jax.shard_map(
        body,
        mesh=mesh,
        in_specs=placed,
        out_specs=(P(("group", "chan"), None, None), P(("group", "chan"), None, None)),
        check_vma=False,
    )
```

```python
import jax
import jax.numpy as jnp
from jax import lax
from jax.experimental import pallas as pl
from jax.experimental.pallas import tpu as pltpu
from jax.sharding import PartitionSpec as P

GEN = 4


def project_kernel(
    fmap_ref, conv_ref, input_ref, weight_ref, bias_ref, down_ref, select_ref,
    driven_ref, partial_ref, pad_scr, rows_scr, out_scr
):
    positions, thought_count, _ = input_ref.shape
    taps = weight_ref.shape[0]
    rank = down_ref.shape[1]
    state_twice = select_ref.shape[0]
    tap_weights = weight_ref[...].astype(jnp.float32)
    parents = conv_ref.shape[1]
    row = lax.broadcasted_iota(jnp.int32, (thought_count, parents), 0)
    col = lax.broadcasted_iota(jnp.int32, (thought_count, parents), 1)
    pick = jnp.zeros((thought_count, parents), jnp.float32)
    for t in range(thought_count):
        pick = jnp.where((row == t) & (col == fmap_ref[t]), 1.0, pick)
    pick = pick.astype(jnp.bfloat16)
    starts = [
        jnp.dot(pick, conv_ref[tap], preferred_element_type=jnp.float32)
        for tap in range(taps - 1)
    ]
    for t in range(thought_count):
        for tap in range(taps - 1):
            pad_scr[tap : tap + 1, :] = starts[tap][t : t + 1, :]
        pad_scr[taps - 1 : taps - 1 + positions, :] = input_ref[:, t, :].astype(jnp.float32)
        summed = bias_ref[...] + tap_weights[0:1, :] * pad_scr[0:positions, :]
        for offset in range(1, taps):
            summed = summed + tap_weights[offset : offset + 1, :] * pad_scr[
                offset : offset + positions, :
            ]
        driven = jax.nn.silu(summed).astype(jnp.bfloat16)
        driven_ref[t] = driven
        rows_scr[t * positions : (t + 1) * positions, :] = driven.astype(jnp.float32)
    token_rows = rows_scr[...].astype(jnp.bfloat16)
    out_scr[:, :rank] = jnp.dot(token_rows, down_ref[...], preferred_element_type=jnp.float32)
    out_scr[:, rank:] = lax.dot_general(
        token_rows, select_ref[...], (((1,), (1,)), ((), ())),
        preferred_element_type=jnp.float32,
    )
    for t in range(thought_count):
        block = out_scr[t * positions : (t + 1) * positions, :]
        select_part = block[:, rank:]
        select_high = select_part.astype(jnp.bfloat16)
        select_low = (select_part - select_high.astype(jnp.float32)).astype(jnp.bfloat16)
        partial_ref[t, :, :rank] = block[:, :rank].astype(jnp.bfloat16)
        partial_ref[t, :, rank : rank + state_twice] = select_high
        partial_ref[t, :, rank + state_twice :] = select_low


def project(parent_conv, fork_map, mixer_input, conv_weight, conv_bias, rate_down,
            selection_weight):
    thought_count, positions, width_local = mixer_input.shape
    taps = conv_weight.shape[0]
    rank, state_twice = rate_down.shape[1], selection_weight.shape[1]
    conv_view = jnp.transpose(parent_conv, (1, 0, 2))
    input_view = jnp.transpose(mixer_input, (1, 0, 2))
    select_view = jnp.transpose(selection_weight)
    full = lambda shape: pl.BlockSpec(shape, lambda i, fmap: (0,) * len(shape))
    grid_spec = pltpu.PrefetchScalarGridSpec(
        num_scalar_prefetch=1,
        grid=(1,),
        in_specs=[
            full(conv_view.shape),
            full(input_view.shape),
            full(conv_weight.shape),
            full((1, width_local)),
            full(rate_down.shape),
            full(select_view.shape),
        ],
        out_specs=[
            full(mixer_input.shape),
            full((thought_count, positions, rank + 2 * state_twice)),
        ],
        scratch_shapes=[
            pltpu.VMEM((taps - 1 + positions, width_local), jnp.float32),
            pltpu.VMEM((thought_count * positions, width_local), jnp.float32),
            pltpu.VMEM((thought_count * positions, rank + state_twice), jnp.float32),
        ],
    )
    return pl.pallas_call(
        project_kernel,
        grid_spec=grid_spec,
        out_shape=(
            jax.ShapeDtypeStruct(mixer_input.shape, jnp.bfloat16),
            jax.ShapeDtypeStruct((thought_count, positions, rank + 2 * state_twice), jnp.bfloat16),
        ),
    )(fork_map, conv_view, input_view, conv_weight, conv_bias.reshape(1, width_local),
      rate_down, select_view)


def scan_kernel(
    lens_ref, fmap_ref, rate_ref, drive_ref, gate_ref, b_ref, c_ref, *rest
):
    pair = len(rest) - 6
    h0_refs, (a_ref, skip_ref, packed_ref, r_scr, u_scr, y_scr) = rest[:pair], rest[pair:]
    positions = drive_ref.shape[1]
    state_size = h0_refs[0].shape[1]
    decay = a_ref[...]
    states, lives = [], []
    for k in range(pair):
        live = jnp.clip(lens_ref[pl.program_id(0) * pair + k] + GEN, 0, positions)
        inflow = drive_ref[k].astype(jnp.float32)
        alive = lax.broadcasted_iota(jnp.int32, inflow.shape, 0) < live
        rate = jnp.where(alive, rate_ref[k * positions : (k + 1) * positions, :], 0.0)
        r_scr[k] = rate
        u_scr[k] = rate * inflow
        states.append(h0_refs[k][0])
        lives.append(alive)
    for p in range(positions):
        for k in range(pair):
            b_col = b_ref[k][:, p : p + 1]
            c_col = c_ref[k][:, p : p + 1]
            h = states[k]
            rate_rows = r_scr[k, pl.ds(p, state_size, stride=0), :]
            push_rows = u_scr[k, pl.ds(p, state_size, stride=0), :]
            h = jnp.exp2(rate_rows * decay) * h + push_rows * b_col
            y_scr[k, p : p + 1, :] = jnp.sum(c_col * h, axis=0, keepdims=True)
            states[k] = h
    for k in range(pair):
        packed_ref[k, :state_size, :] = states[k].astype(packed_ref.dtype)
        inflow = drive_ref[k].astype(jnp.float32)
        gate = gate_ref[k].astype(jnp.float32)
        result = (y_scr[k] + skip_ref[...] * inflow) * jax.nn.silu(gate)
        packed_ref[k, state_size:, :] = jnp.where(lives[k], result, 0.0).astype(packed_ref.dtype)


def run_scan(judge_lengths, fork_map, step_rate, driven, gate_input, b_t, c_t, parent_state,
             decay_rate, skip_gain):
    thought_count, positions, width_local = driven.shape
    state_size = parent_state.shape[1]
    pair = 4 if thought_count % 4 == 0 else 2
    row_block = lambda t, lens, fmap: (t, 0, 0)
    whole = lambda t, lens, fmap: (0, 0)

    def state_block(k):
        return pl.BlockSpec(
            (1, state_size, width_local), lambda t, lens, fmap: (fmap[t * pair + k], 0, 0)
        )

    grid_spec = pltpu.PrefetchScalarGridSpec(
        num_scalar_prefetch=2,
        grid=(thought_count // pair,),
        in_specs=[
            pl.BlockSpec((pair * positions, width_local), lambda t, lens, fmap: (t, 0)),
            pl.BlockSpec((pair, positions, width_local), row_block),
            pl.BlockSpec((pair, positions, width_local), row_block),
            pl.BlockSpec((pair, state_size, positions), row_block),
            pl.BlockSpec((pair, state_size, positions), row_block),
        ]
        + [state_block(k) for k in range(pair)]
        + [
            pl.BlockSpec((state_size, width_local), whole),
            pl.BlockSpec((1, width_local), whole),
        ],
        out_specs=pl.BlockSpec((pair, state_size + positions, width_local), row_block),
        scratch_shapes=[pltpu.VMEM((pair, positions, width_local), jnp.float32)] * 3,
    )
    return pl.pallas_call(
        scan_kernel,
        grid_spec=grid_spec,
        out_shape=jax.ShapeDtypeStruct(
            (thought_count, state_size + positions, width_local), jnp.bfloat16
        ),
        compiler_params=pltpu.CompilerParams(dimension_semantics=("arbitrary",)),
    )(judge_lengths, fork_map, step_rate, driven, gate_input, b_t, c_t,
      *([parent_state] * pair), decay_rate, skip_gain.reshape(1, width_local))


def body(
    parent_state,
    parent_conv,
    fork_map,
    judge_lengths,
    mixer_input,
    gate_input,
    conv_weight,
    conv_bias,
    rate_down,
    selection_weight,
    rate_up,
    rate_bias,
    decay_log,
    skip_gain,
):
    thought_count, positions, width_local = mixer_input.shape
    state_size = parent_state.shape[1]
    rank = rate_down.shape[1]
    driven, partial = project(
        parent_conv, fork_map, mixer_input, conv_weight, conv_bias, rate_down, selection_weight
    )
    devices = lax.axis_size("chan")
    pieces = lax.all_to_all(
        partial.reshape(devices, -1, partial.shape[2]), "chan", 0, 0, tiled=True
    ).astype(jnp.float32)
    reduced = jnp.sum(pieces, axis=0)
    low_mine = reduced[:, :rank].astype(jnp.bfloat16)
    select_sum = reduced[:, rank : rank + 2 * state_size] + reduced[:, rank + 2 * state_size :]
    select_high = select_sum.astype(jnp.bfloat16)
    select_low = (select_sum - select_high.astype(jnp.float32)).astype(jnp.bfloat16)
    mine = jnp.concatenate([low_mine, select_high, select_low], axis=1)
    gathered = lax.all_to_all(
        jnp.broadcast_to(mine[None], (devices,) + mine.shape), "chan", 0, 0, tiled=True
    ).reshape(-1, mine.shape[1])
    rate_low = gathered[:, :rank]
    selection = (
        gathered[:, rank : rank + 2 * state_size].astype(jnp.float32)
        + gathered[:, rank + 2 * state_size :].astype(jnp.float32)
    ).reshape(thought_count, positions, 2 * state_size)
    step_rate = jax.nn.softplus(
        jnp.dot(rate_low, rate_up, preferred_element_type=jnp.float32) + rate_bias[None, :]
    )
    b_t = jnp.swapaxes(selection[:, :, :state_size], 1, 2)
    c_t = jnp.swapaxes(selection[:, :, state_size:], 1, 2)
    decay_rate = -jnp.exp(decay_log) * 1.4426950408889634
    packed_local = run_scan(
        judge_lengths, fork_map, step_rate, driven, gate_input, b_t, c_t, parent_state,
        decay_rate, skip_gain,
    )
    packed = lax.all_to_all(packed_local, "chan", split_axis=0, concat_axis=2, tiled=True)
    final_state = packed[:, :state_size].astype(jnp.float32)
    mixer_output = packed[:, state_size:]
    return (mixer_output, final_state)


def solution(mesh):
    placed = (
        P("group", None, "chan"),
        P("group", None, "chan"),
        P("group"),
        P("group"),
        P("group", None, "chan"),
        P("group", None, "chan"),
        P(None, "chan"),
        P("chan"),
        P("chan", None),
        P("chan", None),
        P(None, "chan"),
        P("chan"),
        P(None, "chan"),
        P("chan"),
    )
    return jax.shard_map(
        body,
        mesh=mesh,
        in_specs=placed,
        out_specs=(P(("group", "chan"), None, None), P(("group", "chan"), None, None)),
        check_vma=False,
    )
```

```python
import jax
import jax.numpy as jnp
from jax import lax
from jax.experimental import pallas as pl
from jax.experimental.pallas import tpu as pltpu
from jax.sharding import PartitionSpec as P

GEN = 4


def project_kernel(
    fmap_ref, conv_ref, input_ref, weight_ref, bias_ref, down_ref, select_ref,
    driven_ref, partial_ref, pad_scr, rows_scr, out_scr
):
    positions, thought_count, _ = input_ref.shape
    taps = weight_ref.shape[0]
    rank = down_ref.shape[1]
    state_twice = select_ref.shape[0]
    tap_weights = weight_ref[...].astype(jnp.float32)
    parents = conv_ref.shape[1]
    row = lax.broadcasted_iota(jnp.int32, (thought_count, parents), 0)
    col = lax.broadcasted_iota(jnp.int32, (thought_count, parents), 1)
    pick = jnp.zeros((thought_count, parents), jnp.float32)
    for t in range(thought_count):
        pick = jnp.where((row == t) & (col == fmap_ref[t]), 1.0, pick)
    pick = pick.astype(jnp.bfloat16)
    starts = [
        jnp.dot(pick, conv_ref[tap], preferred_element_type=jnp.float32)
        for tap in range(taps - 1)
    ]
    for t in range(thought_count):
        for tap in range(taps - 1):
            pad_scr[tap : tap + 1, :] = starts[tap][t : t + 1, :]
        pad_scr[taps - 1 : taps - 1 + positions, :] = input_ref[:, t, :].astype(jnp.float32)
        summed = bias_ref[...] + tap_weights[0:1, :] * pad_scr[0:positions, :]
        for offset in range(1, taps):
            summed = summed + tap_weights[offset : offset + 1, :] * pad_scr[
                offset : offset + positions, :
            ]
        driven = jax.nn.silu(summed).astype(jnp.bfloat16)
        driven_ref[t] = driven
        rows_scr[t * positions : (t + 1) * positions, :] = driven.astype(jnp.float32)
    token_rows = rows_scr[...].astype(jnp.bfloat16)
    out_scr[:, :rank] = jnp.dot(token_rows, down_ref[...], preferred_element_type=jnp.float32)
    out_scr[:, rank:] = lax.dot_general(
        token_rows, select_ref[...], (((1,), (1,)), ((), ())),
        preferred_element_type=jnp.float32,
    )
    for t in range(thought_count):
        block = out_scr[t * positions : (t + 1) * positions, :]
        select_part = block[:, rank:]
        select_high = select_part.astype(jnp.bfloat16)
        select_low = (select_part - select_high.astype(jnp.float32)).astype(jnp.bfloat16)
        partial_ref[t, :, :rank] = block[:, :rank].astype(jnp.bfloat16)
        partial_ref[t, :, rank : rank + state_twice] = select_high
        partial_ref[t, :, rank + state_twice :] = select_low


def project(parent_conv, fork_map, mixer_input, conv_weight, conv_bias, rate_down,
            selection_weight):
    thought_count, positions, width_local = mixer_input.shape
    taps = conv_weight.shape[0]
    rank, state_twice = rate_down.shape[1], selection_weight.shape[1]
    conv_view = jnp.transpose(parent_conv, (1, 0, 2))
    input_view = jnp.transpose(mixer_input, (1, 0, 2))
    select_view = jnp.transpose(selection_weight)
    full = lambda shape: pl.BlockSpec(shape, lambda i, fmap: (0,) * len(shape))
    grid_spec = pltpu.PrefetchScalarGridSpec(
        num_scalar_prefetch=1,
        grid=(1,),
        in_specs=[
            full(conv_view.shape),
            full(input_view.shape),
            full(conv_weight.shape),
            full((1, width_local)),
            full(rate_down.shape),
            full(select_view.shape),
        ],
        out_specs=[
            full(mixer_input.shape),
            full((thought_count, positions, rank + 2 * state_twice)),
        ],
        scratch_shapes=[
            pltpu.VMEM((taps - 1 + positions, width_local), jnp.float32),
            pltpu.VMEM((thought_count * positions, width_local), jnp.float32),
            pltpu.VMEM((thought_count * positions, rank + state_twice), jnp.float32),
        ],
    )
    return pl.pallas_call(
        project_kernel,
        grid_spec=grid_spec,
        out_shape=(
            jax.ShapeDtypeStruct(mixer_input.shape, jnp.bfloat16),
            jax.ShapeDtypeStruct((thought_count, positions, rank + 2 * state_twice), jnp.bfloat16),
        ),
    )(fork_map, conv_view, input_view, conv_weight, conv_bias.reshape(1, width_local),
      rate_down, select_view)


def scan_kernel(
    lens_ref, fmap_ref, rate_ref, drive_ref, gate_ref, b_ref, c_ref, *rest
):
    pair = len(rest) - 6
    h0_refs, (a_ref, skip_ref, packed_ref, r_scr, u_scr, y_scr) = rest[:pair], rest[pair:]
    positions = drive_ref.shape[1]
    state_size = h0_refs[0].shape[1]
    decay = a_ref[...]
    states, lives = [], []
    for k in range(pair):
        live = jnp.clip(lens_ref[pl.program_id(0) * pair + k] + GEN, 0, positions)
        inflow = drive_ref[k].astype(jnp.float32)
        alive = lax.broadcasted_iota(jnp.int32, inflow.shape, 0) < live
        rate = jnp.where(alive, rate_ref[k * positions : (k + 1) * positions, :], 0.0)
        r_scr[k] = rate
        u_scr[k] = rate * inflow
        states.append(h0_refs[k][0])
        lives.append(alive)
    for p in range(positions):
        for k in range(pair):
            b_col = b_ref[k][:, p : p + 1]
            c_col = c_ref[k][:, p : p + 1]
            h = states[k]
            rate_rows = r_scr[k, pl.ds(p, state_size, stride=0), :]
            push_rows = u_scr[k, pl.ds(p, state_size, stride=0), :]
            h = jnp.exp2(rate_rows * decay) * h + push_rows * b_col
            y_scr[k, p : p + 1, :] = jnp.sum(c_col * h, axis=0, keepdims=True)
            states[k] = h
    for k in range(pair):
        packed_ref[k, :state_size, :] = states[k].astype(packed_ref.dtype)
        inflow = drive_ref[k].astype(jnp.float32)
        gate = gate_ref[k].astype(jnp.float32)
        result = (y_scr[k] + skip_ref[...] * inflow) * jax.nn.silu(gate)
        packed_ref[k, state_size:, :] = jnp.where(lives[k], result, 0.0).astype(packed_ref.dtype)


def run_scan(judge_lengths, fork_map, step_rate, driven, gate_input, b_t, c_t, parent_state,
             decay_rate, skip_gain):
    thought_count, positions, width_local = driven.shape
    state_size = parent_state.shape[1]
    pair = 4 if thought_count % 4 == 0 else 2
    row_block = lambda t, lens, fmap: (t, 0, 0)
    whole = lambda t, lens, fmap: (0, 0)

    def state_block(k):
        return pl.BlockSpec(
            (1, state_size, width_local), lambda t, lens, fmap: (fmap[t * pair + k], 0, 0)
        )

    grid_spec = pltpu.PrefetchScalarGridSpec(
        num_scalar_prefetch=2,
        grid=(thought_count // pair,),
        in_specs=[
            pl.BlockSpec((pair * positions, width_local), lambda t, lens, fmap: (t, 0)),
            pl.BlockSpec((pair, positions, width_local), row_block),
            pl.BlockSpec((pair, positions, width_local), row_block),
            pl.BlockSpec((pair, state_size, positions), row_block),
            pl.BlockSpec((pair, state_size, positions), row_block),
        ]
        + [state_block(k) for k in range(pair)]
        + [
            pl.BlockSpec((state_size, width_local), whole),
            pl.BlockSpec((1, width_local), whole),
        ],
        out_specs=pl.BlockSpec((pair, state_size + positions, width_local), row_block),
        scratch_shapes=[pltpu.VMEM((pair, positions, width_local), jnp.float32)] * 3,
    )
    return pl.pallas_call(
        scan_kernel,
        grid_spec=grid_spec,
        out_shape=jax.ShapeDtypeStruct(
            (thought_count, state_size + positions, width_local), jnp.bfloat16
        ),
        compiler_params=pltpu.CompilerParams(dimension_semantics=("arbitrary",)),
    )(judge_lengths, fork_map, step_rate, driven, gate_input, b_t, c_t,
      *([parent_state] * pair), decay_rate, skip_gain.reshape(1, width_local))


def body(
    parent_state,
    parent_conv,
    fork_map,
    judge_lengths,
    mixer_input,
    gate_input,
    conv_weight,
    conv_bias,
    rate_down,
    selection_weight,
    rate_up,
    rate_bias,
    decay_log,
    skip_gain,
):
    thought_count, positions, width_local = mixer_input.shape
    state_size = parent_state.shape[1]
    rank = rate_down.shape[1]
    driven, partial = project(
        parent_conv, fork_map, mixer_input, conv_weight, conv_bias, rate_down, selection_weight
    )
    devices = lax.axis_size("chan")
    pieces = lax.all_to_all(
        partial.reshape(devices, -1, partial.shape[2]), "chan", 0, 0, tiled=True
    ).astype(jnp.float32)
    reduced = jnp.sum(pieces, axis=0)
    low_mine = reduced[:, :rank].astype(jnp.bfloat16)
    select_sum = reduced[:, rank : rank + 2 * state_size] + reduced[:, rank + 2 * state_size :]
    select_high = select_sum.astype(jnp.bfloat16)
    select_low = (select_sum - select_high.astype(jnp.float32)).astype(jnp.bfloat16)
    mine = jnp.concatenate([low_mine, select_high, select_low], axis=1)
    gathered = lax.all_to_all(
        jnp.broadcast_to(mine[None], (devices,) + mine.shape), "chan", 0, 0, tiled=True
    ).reshape(-1, mine.shape[1])
    rate_low = gathered[:, :rank]
    selection = (
        gathered[:, rank : rank + 2 * state_size].astype(jnp.float32)
        + gathered[:, rank + 2 * state_size :].astype(jnp.float32)
    ).reshape(thought_count, positions, 2 * state_size)
    step_rate = jax.nn.softplus(
        jnp.dot(rate_low, rate_up, preferred_element_type=jnp.float32) + rate_bias[None, :]
    )
    b_t = jnp.swapaxes(selection[:, :, :state_size], 1, 2)
    c_t = jnp.swapaxes(selection[:, :, state_size:], 1, 2)
    decay_rate = -jnp.exp(decay_log) * 1.4426950408889634
    packed_local = run_scan(
        judge_lengths, fork_map, step_rate, driven, gate_input, b_t, c_t, parent_state,
        decay_rate, skip_gain,
    )
    rows = state_size + positions
    lane_rows = packed_local.reshape(thought_count, rows * width_local // 128, 128)
    received = lax.all_to_all(lane_rows, "chan", 0, 0, tiled=True).reshape(
        devices, rows, width_local
    )
    packed = jnp.transpose(received, (1, 0, 2)).reshape(1, rows, devices * width_local)
    final_state = packed[:, :state_size].astype(jnp.float32)
    mixer_output = packed[:, state_size:]
    return (mixer_output, final_state)


def solution(mesh):
    placed = (
        P("group", None, "chan"),
        P("group", None, "chan"),
        P("group"),
        P("group"),
        P("group", None, "chan"),
        P("group", None, "chan"),
        P(None, "chan"),
        P("chan"),
        P("chan", None),
        P("chan", None),
        P(None, "chan"),
        P("chan"),
        P(None, "chan"),
        P("chan"),
    )
    return jax.shard_map(
        body,
        mesh=mesh,
        in_specs=placed,
        out_specs=(P(("group", "chan"), None, None), P(("group", "chan"), None, None)),
        check_vma=False,
    )
```

```python
import jax
import jax.numpy as jnp
from jax import lax
from jax.experimental import pallas as pl
from jax.experimental.pallas import tpu as pltpu
from jax.sharding import PartitionSpec as P

GEN = 4


def project_kernel(
    fmap_ref, conv_ref, input_ref, weight_ref, bias_ref, down_ref, select_ref,
    driven_ref, partial_ref, pad_scr, rows_scr, out_scr
):
    positions, thought_count, _ = input_ref.shape
    taps = weight_ref.shape[0]
    rank = down_ref.shape[1]
    state_twice = select_ref.shape[0]
    tap_weights = weight_ref[...].astype(jnp.float32)
    parents = conv_ref.shape[1]
    row = lax.broadcasted_iota(jnp.int32, (thought_count, parents), 0)
    col = lax.broadcasted_iota(jnp.int32, (thought_count, parents), 1)
    pick = jnp.zeros((thought_count, parents), jnp.float32)
    for t in range(thought_count):
        pick = jnp.where((row == t) & (col == fmap_ref[t]), 1.0, pick)
    pick = pick.astype(jnp.bfloat16)
    starts = [
        jnp.dot(pick, conv_ref[tap], preferred_element_type=jnp.float32)
        for tap in range(taps - 1)
    ]
    for t in range(thought_count):
        for tap in range(taps - 1):
            pad_scr[tap : tap + 1, :] = starts[tap][t : t + 1, :]
        pad_scr[taps - 1 : taps - 1 + positions, :] = input_ref[:, t, :].astype(jnp.float32)
        summed = bias_ref[...] + tap_weights[0:1, :] * pad_scr[0:positions, :]
        for offset in range(1, taps):
            summed = summed + tap_weights[offset : offset + 1, :] * pad_scr[
                offset : offset + positions, :
            ]
        driven = jax.nn.silu(summed).astype(jnp.bfloat16)
        driven_ref[t] = driven
        rows_scr[t * positions : (t + 1) * positions, :] = driven.astype(jnp.float32)
    token_rows = rows_scr[...].astype(jnp.bfloat16)
    out_scr[:, :rank] = jnp.dot(token_rows, down_ref[...], preferred_element_type=jnp.float32)
    out_scr[:, rank:] = lax.dot_general(
        token_rows, select_ref[...], (((1,), (1,)), ((), ())),
        preferred_element_type=jnp.float32,
    )
    for t in range(thought_count):
        block = out_scr[t * positions : (t + 1) * positions, :]
        select_part = block[:, rank:]
        select_high = select_part.astype(jnp.bfloat16)
        select_low = (select_part - select_high.astype(jnp.float32)).astype(jnp.bfloat16)
        partial_ref[t, :, :rank] = block[:, :rank].astype(jnp.bfloat16)
        partial_ref[t, :, rank : rank + state_twice] = select_high
        partial_ref[t, :, rank + state_twice :] = select_low


def project(parent_conv, fork_map, mixer_input, conv_weight, conv_bias, rate_down,
            selection_weight):
    thought_count, positions, width_local = mixer_input.shape
    taps = conv_weight.shape[0]
    rank, state_twice = rate_down.shape[1], selection_weight.shape[1]
    conv_view = jnp.transpose(parent_conv, (1, 0, 2))
    input_view = jnp.transpose(mixer_input, (1, 0, 2))
    select_view = jnp.transpose(selection_weight)
    full = lambda shape: pl.BlockSpec(shape, lambda i, fmap: (0,) * len(shape))
    grid_spec = pltpu.PrefetchScalarGridSpec(
        num_scalar_prefetch=1,
        grid=(1,),
        in_specs=[
            full(conv_view.shape),
            full(input_view.shape),
            full(conv_weight.shape),
            full((1, width_local)),
            full(rate_down.shape),
            full(select_view.shape),
        ],
        out_specs=[
            full(mixer_input.shape),
            full((thought_count, positions, rank + 2 * state_twice)),
        ],
        scratch_shapes=[
            pltpu.VMEM((taps - 1 + positions, width_local), jnp.float32),
            pltpu.VMEM((thought_count * positions, width_local), jnp.float32),
            pltpu.VMEM((thought_count * positions, rank + state_twice), jnp.float32),
        ],
    )
    return pl.pallas_call(
        project_kernel,
        grid_spec=grid_spec,
        out_shape=(
            jax.ShapeDtypeStruct(mixer_input.shape, jnp.bfloat16),
            jax.ShapeDtypeStruct((thought_count, positions, rank + 2 * state_twice), jnp.bfloat16),
        ),
    )(fork_map, conv_view, input_view, conv_weight, conv_bias.reshape(1, width_local),
      rate_down, select_view)


def scan_kernel(
    lens_ref, fmap_ref, rate_ref, drive_ref, gate_ref, b_ref, c_ref, *rest
):
    pair = len(rest) - 6
    h0_refs, (a_ref, skip_ref, packed_ref, r_scr, u_scr, y_scr) = rest[:pair], rest[pair:]
    positions = drive_ref.shape[1]
    state_size = h0_refs[0].shape[1]
    decay = a_ref[...]
    states, lives = [], []
    for k in range(pair):
        live = jnp.clip(lens_ref[pl.program_id(0) * pair + k] + GEN, 0, positions)
        inflow = drive_ref[k].astype(jnp.float32)
        alive = lax.broadcasted_iota(jnp.int32, inflow.shape, 0) < live
        rate = jnp.where(alive, rate_ref[k * positions : (k + 1) * positions, :], 0.0)
        r_scr[k] = rate
        u_scr[k] = rate * inflow
        states.append(h0_refs[k][0])
        lives.append(alive)
    for p in range(positions):
        for k in range(pair):
            b_col = b_ref[k][:, p : p + 1]
            c_col = c_ref[k][:, p : p + 1]
            h = states[k]
            rate_rows = r_scr[k, pl.ds(p, state_size, stride=0), :]
            push_rows = u_scr[k, pl.ds(p, state_size, stride=0), :]
            h = jnp.exp2(rate_rows * decay) * h + push_rows * b_col
            y_scr[k, p : p + 1, :] = jnp.sum(c_col * h, axis=0, keepdims=True)
            states[k] = h
    lanes = packed_ref.shape[2]
    tiles = inflow.shape[1] // lanes
    tail = positions - state_size
    for k in range(pair):
        inflow = drive_ref[k].astype(jnp.float32)
        gate = gate_ref[k].astype(jnp.float32)
        result = (y_scr[k] + skip_ref[...] * inflow) * jax.nn.silu(gate)
        result = jnp.where(lives[k], result, 0.0)
        for j in range(tiles):
            cols = slice(j * lanes, (j + 1) * lanes)
            base = j * state_size
            packed_ref[k, base : base + state_size, :] = states[k][:, cols].astype(
                packed_ref.dtype
            )
            base = tiles * state_size + j * state_size
            packed_ref[k, base : base + state_size, :] = result[:state_size, cols].astype(
                packed_ref.dtype
            )
            base = 2 * tiles * state_size + j * tail
            packed_ref[k, base : base + tail, :] = result[state_size:, cols].astype(
                packed_ref.dtype
            )


def run_scan(judge_lengths, fork_map, step_rate, driven, gate_input, b_t, c_t, parent_state,
             decay_rate, skip_gain):
    thought_count, positions, width_local = driven.shape
    state_size = parent_state.shape[1]
    pair = 4 if thought_count % 4 == 0 else 2
    row_block = lambda t, lens, fmap: (t, 0, 0)
    whole = lambda t, lens, fmap: (0, 0)

    def state_block(k):
        return pl.BlockSpec(
            (1, state_size, width_local), lambda t, lens, fmap: (fmap[t * pair + k], 0, 0)
        )

    grid_spec = pltpu.PrefetchScalarGridSpec(
        num_scalar_prefetch=2,
        grid=(thought_count // pair,),
        in_specs=[
            pl.BlockSpec((pair * positions, width_local), lambda t, lens, fmap: (t, 0)),
            pl.BlockSpec((pair, positions, width_local), row_block),
            pl.BlockSpec((pair, positions, width_local), row_block),
            pl.BlockSpec((pair, state_size, positions), row_block),
            pl.BlockSpec((pair, state_size, positions), row_block),
        ]
        + [state_block(k) for k in range(pair)]
        + [
            pl.BlockSpec((state_size, width_local), whole),
            pl.BlockSpec((1, width_local), whole),
        ],
        out_specs=pl.BlockSpec(
            (pair, (state_size + positions) * width_local // 128, 128), row_block
        ),
        scratch_shapes=[pltpu.VMEM((pair, positions, width_local), jnp.float32)] * 3,
    )
    return pl.pallas_call(
        scan_kernel,
        grid_spec=grid_spec,
        out_shape=jax.ShapeDtypeStruct(
            (thought_count, (state_size + positions) * width_local // 128, 128), jnp.bfloat16
        ),
        compiler_params=pltpu.CompilerParams(dimension_semantics=("arbitrary",)),
    )(judge_lengths, fork_map, step_rate, driven, gate_input, b_t, c_t,
      *([parent_state] * pair), decay_rate, skip_gain.reshape(1, width_local))


def body(
    parent_state,
    parent_conv,
    fork_map,
    judge_lengths,
    mixer_input,
    gate_input,
    conv_weight,
    conv_bias,
    rate_down,
    selection_weight,
    rate_up,
    rate_bias,
    decay_log,
    skip_gain,
):
    thought_count, positions, width_local = mixer_input.shape
    state_size = parent_state.shape[1]
    rank = rate_down.shape[1]
    driven, partial = project(
        parent_conv, fork_map, mixer_input, conv_weight, conv_bias, rate_down, selection_weight
    )
    devices = lax.axis_size("chan")
    pieces = lax.all_to_all(
        partial.reshape(devices, -1, partial.shape[2]), "chan", 0, 0, tiled=True
    ).astype(jnp.float32)
    reduced = jnp.sum(pieces, axis=0)
    low_mine = reduced[:, :rank].astype(jnp.bfloat16)
    select_sum = reduced[:, rank : rank + 2 * state_size] + reduced[:, rank + 2 * state_size :]
    select_high = select_sum.astype(jnp.bfloat16)
    select_low = (select_sum - select_high.astype(jnp.float32)).astype(jnp.bfloat16)
    mine = jnp.concatenate([low_mine, select_high, select_low], axis=1)
    gathered = lax.all_to_all(
        jnp.broadcast_to(mine[None], (devices,) + mine.shape), "chan", 0, 0, tiled=True
    ).reshape(-1, mine.shape[1])
    rate_low = gathered[:, :rank]
    selection = (
        gathered[:, rank : rank + 2 * state_size].astype(jnp.float32)
        + gathered[:, rank + 2 * state_size :].astype(jnp.float32)
    ).reshape(thought_count, positions, 2 * state_size)
    step_rate = jax.nn.softplus(
        jnp.dot(rate_low, rate_up, preferred_element_type=jnp.float32) + rate_bias[None, :]
    )
    b_t = jnp.swapaxes(selection[:, :, :state_size], 1, 2)
    c_t = jnp.swapaxes(selection[:, :, state_size:], 1, 2)
    decay_rate = -jnp.exp(decay_log) * 1.4426950408889634
    packed_local = run_scan(
        judge_lengths, fork_map, step_rate, driven, gate_input, b_t, c_t, parent_state,
        decay_rate, skip_gain,
    )
    received = lax.all_to_all(packed_local, "chan", 0, 0, tiled=True)
    tiles = width_local // 128
    tail = positions - state_size

    def unpack(start, rows):
        block = received[:, start : start + tiles * rows].reshape(devices, tiles, rows, 128)
        return jnp.transpose(block, (2, 0, 1, 3)).reshape(1, rows, devices * width_local)

    final_state = unpack(0, state_size).astype(jnp.float32)
    mixer_output = jnp.concatenate(
        [unpack(tiles * state_size, state_size), unpack(2 * tiles * state_size, tail)], axis=1
    )
    return (mixer_output, final_state)


def solution(mesh):
    placed = (
        P("group", None, "chan"),
        P("group", None, "chan"),
        P("group"),
        P("group"),
        P("group", None, "chan"),
        P("group", None, "chan"),
        P(None, "chan"),
        P("chan"),
        P("chan", None),
        P("chan", None),
        P(None, "chan"),
        P("chan"),
        P(None, "chan"),
        P("chan"),
    )
    return jax.shard_map(
        body,
        mesh=mesh,
        in_specs=placed,
        out_specs=(P(("group", "chan"), None, None), P(("group", "chan"), None, None)),
        check_vma=False,
    )
```

```python
import jax
import jax.numpy as jnp
from jax import lax
from jax.experimental import pallas as pl
from jax.experimental.pallas import tpu as pltpu
from jax.sharding import PartitionSpec as P

GEN = 4


def project_kernel(
    fmap_ref, conv_ref, input_ref, weight_ref, bias_ref, down_ref, select_ref,
    driven_ref, partial_ref, pad_scr, rows_scr, out_scr
):
    positions, thought_count, _ = input_ref.shape
    taps = weight_ref.shape[0]
    rank = down_ref.shape[1]
    state_twice = select_ref.shape[0]
    tap_weights = weight_ref[...].astype(jnp.float32)
    parents = conv_ref.shape[1]
    row = lax.broadcasted_iota(jnp.int32, (thought_count, parents), 0)
    col = lax.broadcasted_iota(jnp.int32, (thought_count, parents), 1)
    pick = jnp.zeros((thought_count, parents), jnp.float32)
    for t in range(thought_count):
        pick = jnp.where((row == t) & (col == fmap_ref[t]), 1.0, pick)
    pick = pick.astype(jnp.bfloat16)
    starts = [
        jnp.dot(pick, conv_ref[tap], preferred_element_type=jnp.float32)
        for tap in range(taps - 1)
    ]
    for t in range(thought_count):
        for tap in range(taps - 1):
            pad_scr[tap : tap + 1, :] = starts[tap][t : t + 1, :]
        pad_scr[taps - 1 : taps - 1 + positions, :] = input_ref[:, t, :].astype(jnp.float32)
        summed = bias_ref[...] + tap_weights[0:1, :] * pad_scr[0:positions, :]
        for offset in range(1, taps):
            summed = summed + tap_weights[offset : offset + 1, :] * pad_scr[
                offset : offset + positions, :
            ]
        driven = jax.nn.silu(summed).astype(jnp.bfloat16)
        driven_ref[t] = driven
        rows_scr[t * positions : (t + 1) * positions, :] = driven.astype(jnp.float32)
    token_rows = rows_scr[...].astype(jnp.bfloat16)
    out_scr[:, :rank] = jnp.dot(token_rows, down_ref[...], preferred_element_type=jnp.float32)
    out_scr[:, rank:] = lax.dot_general(
        token_rows, select_ref[...], (((1,), (1,)), ((), ())),
        preferred_element_type=jnp.float32,
    )
    for t in range(thought_count):
        block = out_scr[t * positions : (t + 1) * positions, :]
        select_part = block[:, rank:]
        select_high = select_part.astype(jnp.bfloat16)
        select_low = (select_part - select_high.astype(jnp.float32)).astype(jnp.bfloat16)
        partial_ref[t, :, :rank] = block[:, :rank].astype(jnp.bfloat16)
        partial_ref[t, :, rank : rank + state_twice] = select_high
        partial_ref[t, :, rank + state_twice :] = select_low


def project(parent_conv, fork_map, mixer_input, conv_weight, conv_bias, rate_down,
            selection_weight):
    thought_count, positions, width_local = mixer_input.shape
    taps = conv_weight.shape[0]
    rank, state_twice = rate_down.shape[1], selection_weight.shape[1]
    conv_view = jnp.transpose(parent_conv, (1, 0, 2))
    input_view = jnp.transpose(mixer_input, (1, 0, 2))
    select_view = jnp.transpose(selection_weight)
    full = lambda shape: pl.BlockSpec(shape, lambda i, fmap: (0,) * len(shape))
    grid_spec = pltpu.PrefetchScalarGridSpec(
        num_scalar_prefetch=1,
        grid=(1,),
        in_specs=[
            full(conv_view.shape),
            full(input_view.shape),
            full(conv_weight.shape),
            full((1, width_local)),
            full(rate_down.shape),
            full(select_view.shape),
        ],
        out_specs=[
            full(mixer_input.shape),
            full((thought_count, positions, rank + 2 * state_twice)),
        ],
        scratch_shapes=[
            pltpu.VMEM((taps - 1 + positions, width_local), jnp.float32),
            pltpu.VMEM((thought_count * positions, width_local), jnp.float32),
            pltpu.VMEM((thought_count * positions, rank + state_twice), jnp.float32),
        ],
    )
    return pl.pallas_call(
        project_kernel,
        grid_spec=grid_spec,
        out_shape=(
            jax.ShapeDtypeStruct(mixer_input.shape, jnp.bfloat16),
            jax.ShapeDtypeStruct((thought_count, positions, rank + 2 * state_twice), jnp.bfloat16),
        ),
    )(fork_map, conv_view, input_view, conv_weight, conv_bias.reshape(1, width_local),
      rate_down, select_view)


def scan_kernel(
    lens_ref, fmap_ref, rate_ref, drive_ref, gate_ref, b_ref, c_ref, *rest
):
    pair = len(rest) - 6
    h0_refs, (a_ref, skip_ref, packed_ref, r_scr, u_scr, y_scr) = rest[:pair], rest[pair:]
    positions = drive_ref.shape[1]
    state_size = h0_refs[0].shape[1]
    decay = a_ref[...]
    states, lives = [], []
    for k in range(pair):
        live = jnp.clip(lens_ref[pl.program_id(0) * pair + k] + GEN, 0, positions)
        inflow = drive_ref[k].astype(jnp.float32)
        alive = lax.broadcasted_iota(jnp.int32, inflow.shape, 0) < live
        rate = jnp.where(alive, rate_ref[k * positions : (k + 1) * positions, :], 0.0)
        r_scr[k] = rate
        u_scr[k] = rate * inflow
        states.append(h0_refs[k][0])
        lives.append(alive)
    for p in range(positions):
        for k in range(pair):
            b_col = b_ref[k][:, p : p + 1]
            c_col = c_ref[k][:, p : p + 1]
            h = states[k]
            rate_rows = r_scr[k, pl.ds(p, state_size, stride=0), :]
            push_rows = u_scr[k, pl.ds(p, state_size, stride=0), :]
            h = jnp.exp2(rate_rows * decay) * h + push_rows * b_col
            y_scr[k, p : p + 1, :] = jnp.sum(c_col * h, axis=0, keepdims=True)
            states[k] = h
    lanes = packed_ref.shape[2]
    tiles = inflow.shape[1] // lanes
    for k in range(pair):
        inflow = drive_ref[k].astype(jnp.float32)
        gate = gate_ref[k].astype(jnp.float32)
        result = (y_scr[k] + skip_ref[...] * inflow) * jax.nn.silu(gate)
        result = jnp.where(lives[k], result, 0.0)
        for j in range(tiles):
            cols = slice(j * lanes, (j + 1) * lanes)
            base = j * state_size
            packed_ref[k, base : base + state_size, :] = states[k][:, cols].astype(
                packed_ref.dtype
            )
            base = tiles * state_size + j * positions
            packed_ref[k, base : base + positions, :] = result[:, cols].astype(packed_ref.dtype)


def run_scan(judge_lengths, fork_map, step_rate, driven, gate_input, b_t, c_t, parent_state,
             decay_rate, skip_gain):
    thought_count, positions, width_local = driven.shape
    state_size = parent_state.shape[1]
    pair = 4 if thought_count % 4 == 0 else 2
    row_block = lambda t, lens, fmap: (t, 0, 0)
    whole = lambda t, lens, fmap: (0, 0)

    def state_block(k):
        return pl.BlockSpec(
            (1, state_size, width_local), lambda t, lens, fmap: (fmap[t * pair + k], 0, 0)
        )

    grid_spec = pltpu.PrefetchScalarGridSpec(
        num_scalar_prefetch=2,
        grid=(thought_count // pair,),
        in_specs=[
            pl.BlockSpec((pair * positions, width_local), lambda t, lens, fmap: (t, 0)),
            pl.BlockSpec((pair, positions, width_local), row_block),
            pl.BlockSpec((pair, positions, width_local), row_block),
            pl.BlockSpec((pair, state_size, positions), row_block),
            pl.BlockSpec((pair, state_size, positions), row_block),
        ]
        + [state_block(k) for k in range(pair)]
        + [
            pl.BlockSpec((state_size, width_local), whole),
            pl.BlockSpec((1, width_local), whole),
        ],
        out_specs=pl.BlockSpec(
            (pair, (state_size + positions) * width_local // 128, 128), row_block
        ),
        scratch_shapes=[pltpu.VMEM((pair, positions, width_local), jnp.float32)] * 3,
    )
    return pl.pallas_call(
        scan_kernel,
        grid_spec=grid_spec,
        out_shape=jax.ShapeDtypeStruct(
            (thought_count, (state_size + positions) * width_local // 128, 128), jnp.bfloat16
        ),
        compiler_params=pltpu.CompilerParams(dimension_semantics=("arbitrary",)),
    )(judge_lengths, fork_map, step_rate, driven, gate_input, b_t, c_t,
      *([parent_state] * pair), decay_rate, skip_gain.reshape(1, width_local))


def body(
    parent_state,
    parent_conv,
    fork_map,
    judge_lengths,
    mixer_input,
    gate_input,
    conv_weight,
    conv_bias,
    rate_down,
    selection_weight,
    rate_up,
    rate_bias,
    decay_log,
    skip_gain,
):
    thought_count, positions, width_local = mixer_input.shape
    state_size = parent_state.shape[1]
    rank = rate_down.shape[1]
    driven, partial = project(
        parent_conv, fork_map, mixer_input, conv_weight, conv_bias, rate_down, selection_weight
    )
    devices = lax.axis_size("chan")
    pieces = lax.all_to_all(
        partial.reshape(devices, -1, partial.shape[2]), "chan", 0, 0, tiled=True
    ).astype(jnp.float32)
    reduced = jnp.sum(pieces, axis=0)
    low_mine = reduced[:, :rank].astype(jnp.bfloat16)
    select_sum = reduced[:, rank : rank + 2 * state_size] + reduced[:, rank + 2 * state_size :]
    select_high = select_sum.astype(jnp.bfloat16)
    select_low = (select_sum - select_high.astype(jnp.float32)).astype(jnp.bfloat16)
    mine = jnp.concatenate([low_mine, select_high, select_low], axis=1)
    gathered = lax.all_to_all(
        jnp.broadcast_to(mine[None], (devices,) + mine.shape), "chan", 0, 0, tiled=True
    ).reshape(-1, mine.shape[1])
    rate_low = gathered[:, :rank]
    selection = (
        gathered[:, rank : rank + 2 * state_size].astype(jnp.float32)
        + gathered[:, rank + 2 * state_size :].astype(jnp.float32)
    ).reshape(thought_count, positions, 2 * state_size)
    step_rate = jax.nn.softplus(
        jnp.dot(rate_low, rate_up, preferred_element_type=jnp.float32) + rate_bias[None, :]
    )
    b_t = jnp.swapaxes(selection[:, :, :state_size], 1, 2)
    c_t = jnp.swapaxes(selection[:, :, state_size:], 1, 2)
    decay_rate = -jnp.exp(decay_log) * 1.4426950408889634
    packed_local = run_scan(
        judge_lengths, fork_map, step_rate, driven, gate_input, b_t, c_t, parent_state,
        decay_rate, skip_gain,
    )
    received = lax.all_to_all(packed_local, "chan", 0, 0, tiled=True)
    tiles = width_local // 128

    def unpack(start, rows):
        block = received[:, start : start + tiles * rows].reshape(devices, tiles, rows, 128)
        return jnp.transpose(block, (2, 0, 1, 3)).reshape(1, rows, devices * width_local)

    final_state = unpack(0, state_size).astype(jnp.float32)
    mixer_output = unpack(tiles * state_size, positions)
    return (mixer_output, final_state)


def solution(mesh):
    placed = (
        P("group", None, "chan"),
        P("group", None, "chan"),
        P("group"),
        P("group"),
        P("group", None, "chan"),
        P("group", None, "chan"),
        P(None, "chan"),
        P("chan"),
        P("chan", None),
        P("chan", None),
        P(None, "chan"),
        P("chan"),
        P(None, "chan"),
        P("chan"),
    )
    return jax.shard_map(
        body,
        mesh=mesh,
        in_specs=placed,
        out_specs=(P(("group", "chan"), None, None), P(("group", "chan"), None, None)),
        check_vma=False,
    )
```

```python
import jax
import jax.numpy as jnp
from jax import lax
from jax.experimental import pallas as pl
from jax.experimental.pallas import tpu as pltpu
from jax.sharding import PartitionSpec as P

GEN = 4


def project_kernel(
    fmap_ref, conv_ref, input_ref, weight_ref, bias_ref, down_ref, select_ref,
    driven_ref, partial_ref, pad_scr, rows_scr, out_scr
):
    positions, thought_count, _ = input_ref.shape
    taps = weight_ref.shape[0]
    rank = down_ref.shape[1]
    state_twice = select_ref.shape[0]
    tap_weights = weight_ref[...].astype(jnp.float32)
    parents = conv_ref.shape[1]
    row = lax.broadcasted_iota(jnp.int32, (thought_count, parents), 0)
    col = lax.broadcasted_iota(jnp.int32, (thought_count, parents), 1)
    pick = jnp.zeros((thought_count, parents), jnp.float32)
    for t in range(thought_count):
        pick = jnp.where((row == t) & (col == fmap_ref[t]), 1.0, pick)
    pick = pick.astype(jnp.bfloat16)
    starts = [
        jnp.dot(pick, conv_ref[tap], preferred_element_type=jnp.float32)
        for tap in range(taps - 1)
    ]
    for t in range(thought_count):
        for tap in range(taps - 1):
            pad_scr[tap : tap + 1, :] = starts[tap][t : t + 1, :]
        pad_scr[taps - 1 : taps - 1 + positions, :] = input_ref[:, t, :].astype(jnp.float32)
        summed = bias_ref[...] + tap_weights[0:1, :] * pad_scr[0:positions, :]
        for offset in range(1, taps):
            summed = summed + tap_weights[offset : offset + 1, :] * pad_scr[
                offset : offset + positions, :
            ]
        driven = jax.nn.silu(summed).astype(jnp.bfloat16)
        driven_ref[t] = driven
        rows_scr[t * positions : (t + 1) * positions, :] = driven.astype(jnp.float32)
    token_rows = rows_scr[...].astype(jnp.bfloat16)
    out_scr[:, :rank] = jnp.dot(token_rows, down_ref[...], preferred_element_type=jnp.float32)
    out_scr[:, rank:] = lax.dot_general(
        token_rows, select_ref[...], (((1,), (1,)), ((), ())),
        preferred_element_type=jnp.float32,
    )
    lanes = partial_ref.shape[2]
    quarters = rank // lanes
    base = quarters * positions
    for t in range(thought_count):
        block = out_scr[t * positions : (t + 1) * positions, :]
        select_part = block[:, rank:]
        select_high = select_part.astype(jnp.bfloat16)
        select_low = (select_part - select_high.astype(jnp.float32)).astype(jnp.bfloat16)
        for j in range(quarters):
            partial_ref[t, j * positions : (j + 1) * positions, :] = block[
                :, j * lanes : (j + 1) * lanes
            ].astype(jnp.bfloat16)
        partial_ref[t, base : base + positions, 2 * state_twice :] = jnp.zeros(
            (positions, lanes - 2 * state_twice), jnp.bfloat16
        )
        partial_ref[t, base : base + positions, :state_twice] = select_high
        partial_ref[t, base : base + positions, state_twice : 2 * state_twice] = select_low


def project(parent_conv, fork_map, mixer_input, conv_weight, conv_bias, rate_down,
            selection_weight):
    thought_count, positions, width_local = mixer_input.shape
    taps = conv_weight.shape[0]
    rank, state_twice = rate_down.shape[1], selection_weight.shape[1]
    conv_view = jnp.transpose(parent_conv, (1, 0, 2))
    input_view = jnp.transpose(mixer_input, (1, 0, 2))
    select_view = jnp.transpose(selection_weight)
    full = lambda shape: pl.BlockSpec(shape, lambda i, fmap: (0,) * len(shape))
    grid_spec = pltpu.PrefetchScalarGridSpec(
        num_scalar_prefetch=1,
        grid=(1,),
        in_specs=[
            full(conv_view.shape),
            full(input_view.shape),
            full(conv_weight.shape),
            full((1, width_local)),
            full(rate_down.shape),
            full(select_view.shape),
        ],
        out_specs=[
            full(mixer_input.shape),
            full((thought_count, (rank // 128 + 1) * positions, 128)),
        ],
        scratch_shapes=[
            pltpu.VMEM((taps - 1 + positions, width_local), jnp.float32),
            pltpu.VMEM((thought_count * positions, width_local), jnp.float32),
            pltpu.VMEM((thought_count * positions, rank + state_twice), jnp.float32),
        ],
    )
    return pl.pallas_call(
        project_kernel,
        grid_spec=grid_spec,
        out_shape=(
            jax.ShapeDtypeStruct(mixer_input.shape, jnp.bfloat16),
            jax.ShapeDtypeStruct(
                (thought_count, (rank // 128 + 1) * positions, 128), jnp.bfloat16
            ),
        ),
    )(fork_map, conv_view, input_view, conv_weight, conv_bias.reshape(1, width_local),
      rate_down, select_view)


def scan_kernel(
    lens_ref, fmap_ref, rate_ref, drive_ref, gate_ref, b_ref, c_ref, *rest
):
    pair = len(rest) - 6
    h0_refs, (a_ref, skip_ref, packed_ref, r_scr, u_scr, y_scr) = rest[:pair], rest[pair:]
    positions = drive_ref.shape[1]
    state_size = h0_refs[0].shape[1]
    decay = a_ref[...]
    states, lives = [], []
    for k in range(pair):
        live = jnp.clip(lens_ref[pl.program_id(0) * pair + k] + GEN, 0, positions)
        inflow = drive_ref[k].astype(jnp.float32)
        alive = lax.broadcasted_iota(jnp.int32, inflow.shape, 0) < live
        rate = jnp.where(alive, rate_ref[k * positions : (k + 1) * positions, :], 0.0)
        r_scr[k] = rate
        u_scr[k] = rate * inflow
        states.append(h0_refs[k][0])
        lives.append(alive)
    for p in range(positions):
        for k in range(pair):
            b_col = b_ref[k][:, p : p + 1]
            c_col = c_ref[k][:, p : p + 1]
            h = states[k]
            rate_rows = r_scr[k, pl.ds(p, state_size, stride=0), :]
            push_rows = u_scr[k, pl.ds(p, state_size, stride=0), :]
            h = jnp.exp2(rate_rows * decay) * h + push_rows * b_col
            y_scr[k, p : p + 1, :] = jnp.sum(c_col * h, axis=0, keepdims=True)
            states[k] = h
    lanes = packed_ref.shape[2]
    tiles = inflow.shape[1] // lanes
    for k in range(pair):
        inflow = drive_ref[k].astype(jnp.float32)
        gate = gate_ref[k].astype(jnp.float32)
        result = (y_scr[k] + skip_ref[...] * inflow) * jax.nn.silu(gate)
        result = jnp.where(lives[k], result, 0.0)
        for j in range(tiles):
            cols = slice(j * lanes, (j + 1) * lanes)
            base = j * state_size
            packed_ref[k, base : base + state_size, :] = states[k][:, cols].astype(
                packed_ref.dtype
            )
            base = tiles * state_size + j * positions
            packed_ref[k, base : base + positions, :] = result[:, cols].astype(packed_ref.dtype)


def run_scan(judge_lengths, fork_map, step_rate, driven, gate_input, b_t, c_t, parent_state,
             decay_rate, skip_gain):
    thought_count, positions, width_local = driven.shape
    state_size = parent_state.shape[1]
    pair = 4 if thought_count % 4 == 0 else 2
    row_block = lambda t, lens, fmap: (t, 0, 0)
    whole = lambda t, lens, fmap: (0, 0)

    def state_block(k):
        return pl.BlockSpec(
            (1, state_size, width_local), lambda t, lens, fmap: (fmap[t * pair + k], 0, 0)
        )

    grid_spec = pltpu.PrefetchScalarGridSpec(
        num_scalar_prefetch=2,
        grid=(thought_count // pair,),
        in_specs=[
            pl.BlockSpec((pair * positions, width_local), lambda t, lens, fmap: (t, 0)),
            pl.BlockSpec((pair, positions, width_local), row_block),
            pl.BlockSpec((pair, positions, width_local), row_block),
            pl.BlockSpec((pair, state_size, positions), row_block),
            pl.BlockSpec((pair, state_size, positions), row_block),
        ]
        + [state_block(k) for k in range(pair)]
        + [
            pl.BlockSpec((state_size, width_local), whole),
            pl.BlockSpec((1, width_local), whole),
        ],
        out_specs=pl.BlockSpec(
            (pair, (state_size + positions) * width_local // 128, 128), row_block
        ),
        scratch_shapes=[pltpu.VMEM((pair, positions, width_local), jnp.float32)] * 3,
    )
    return pl.pallas_call(
        scan_kernel,
        grid_spec=grid_spec,
        out_shape=jax.ShapeDtypeStruct(
            (thought_count, (state_size + positions) * width_local // 128, 128), jnp.bfloat16
        ),
        compiler_params=pltpu.CompilerParams(dimension_semantics=("arbitrary",)),
    )(judge_lengths, fork_map, step_rate, driven, gate_input, b_t, c_t,
      *([parent_state] * pair), decay_rate, skip_gain.reshape(1, width_local))


def body(
    parent_state,
    parent_conv,
    fork_map,
    judge_lengths,
    mixer_input,
    gate_input,
    conv_weight,
    conv_bias,
    rate_down,
    selection_weight,
    rate_up,
    rate_bias,
    decay_log,
    skip_gain,
):
    thought_count, positions, width_local = mixer_input.shape
    state_size = parent_state.shape[1]
    rank = rate_down.shape[1]
    driven, partial = project(
        parent_conv, fork_map, mixer_input, conv_weight, conv_bias, rate_down, selection_weight
    )
    devices = lax.axis_size("chan")
    pieces = lax.all_to_all(partial, "chan", 0, 0, tiled=True).astype(jnp.float32)
    reduced = jnp.sum(pieces, axis=0)
    quarters = rank // 128
    low_mine = jnp.transpose(
        reduced[: quarters * positions].reshape(quarters, positions, 128), (1, 0, 2)
    ).reshape(positions, rank).astype(jnp.bfloat16)
    select_rows = reduced[quarters * positions :]
    select_sum = select_rows[:, : 2 * state_size] + select_rows[:, 2 * state_size : 4 * state_size]
    select_high = select_sum.astype(jnp.bfloat16)
    select_low = (select_sum - select_high.astype(jnp.float32)).astype(jnp.bfloat16)
    mine = jnp.concatenate([low_mine, select_high, select_low], axis=1)
    gathered = lax.all_to_all(
        jnp.broadcast_to(mine[None], (devices,) + mine.shape), "chan", 0, 0, tiled=True
    ).reshape(-1, mine.shape[1])
    rate_low = gathered[:, :rank]
    selection = (
        gathered[:, rank : rank + 2 * state_size].astype(jnp.float32)
        + gathered[:, rank + 2 * state_size :].astype(jnp.float32)
    ).reshape(thought_count, positions, 2 * state_size)
    step_rate = jax.nn.softplus(
        jnp.dot(rate_low, rate_up, preferred_element_type=jnp.float32) + rate_bias[None, :]
    )
    b_t = jnp.swapaxes(selection[:, :, :state_size], 1, 2)
    c_t = jnp.swapaxes(selection[:, :, state_size:], 1, 2)
    decay_rate = -jnp.exp(decay_log) * 1.4426950408889634
    packed_local = run_scan(
        judge_lengths, fork_map, step_rate, driven, gate_input, b_t, c_t, parent_state,
        decay_rate, skip_gain,
    )
    received = lax.all_to_all(packed_local, "chan", 0, 0, tiled=True)
    tiles = width_local // 128

    def unpack(start, rows):
        block = received[:, start : start + tiles * rows].reshape(devices, tiles, rows, 128)
        return jnp.transpose(block, (2, 0, 1, 3)).reshape(1, rows, devices * width_local)

    final_state = unpack(0, state_size).astype(jnp.float32)
    mixer_output = unpack(tiles * state_size, positions)
    return (mixer_output, final_state)


def solution(mesh):
    placed = (
        P("group", None, "chan"),
        P("group", None, "chan"),
        P("group"),
        P("group"),
        P("group", None, "chan"),
        P("group", None, "chan"),
        P(None, "chan"),
        P("chan"),
        P("chan", None),
        P("chan", None),
        P(None, "chan"),
        P("chan"),
        P(None, "chan"),
        P("chan"),
    )
    return jax.shard_map(
        body,
        mesh=mesh,
        in_specs=placed,
        out_specs=(P(("group", "chan"), None, None), P(("group", "chan"), None, None)),
        check_vma=False,
    )
```

```python
import jax
import jax.numpy as jnp
from jax import lax
from jax.experimental import pallas as pl
from jax.experimental.pallas import tpu as pltpu
from jax.sharding import PartitionSpec as P

GEN = 4


def project_kernel(
    fmap_ref, conv_ref, input_ref, weight_ref, bias_ref, down_ref, select_ref,
    driven_ref, partial_ref, pad_scr, rows_scr, out_scr
):
    positions, thought_count, _ = input_ref.shape
    taps = weight_ref.shape[0]
    rank = down_ref.shape[1]
    state_twice = select_ref.shape[0]
    tap_weights = weight_ref[...].astype(jnp.float32)
    parents = conv_ref.shape[1]
    row = lax.broadcasted_iota(jnp.int32, (thought_count, parents), 0)
    col = lax.broadcasted_iota(jnp.int32, (thought_count, parents), 1)
    pick = jnp.zeros((thought_count, parents), jnp.float32)
    for t in range(thought_count):
        pick = jnp.where((row == t) & (col == fmap_ref[t]), 1.0, pick)
    pick = pick.astype(jnp.bfloat16)
    starts = [
        jnp.dot(pick, conv_ref[tap], preferred_element_type=jnp.float32)
        for tap in range(taps - 1)
    ]
    for t in range(thought_count):
        for tap in range(taps - 1):
            pad_scr[tap : tap + 1, :] = starts[tap][t : t + 1, :]
        pad_scr[taps - 1 : taps - 1 + positions, :] = input_ref[:, t, :].astype(jnp.float32)
        summed = bias_ref[...] + tap_weights[0:1, :] * pad_scr[0:positions, :]
        for offset in range(1, taps):
            summed = summed + tap_weights[offset : offset + 1, :] * pad_scr[
                offset : offset + positions, :
            ]
        driven = jax.nn.silu(summed).astype(jnp.bfloat16)
        driven_ref[t] = driven
        rows_scr[t * positions : (t + 1) * positions, :] = driven.astype(jnp.float32)
    token_rows = rows_scr[...].astype(jnp.bfloat16)
    out_scr[:, :rank] = jnp.dot(token_rows, down_ref[...], preferred_element_type=jnp.float32)
    out_scr[:, rank:] = lax.dot_general(
        token_rows, select_ref[...], (((1,), (1,)), ((), ())),
        preferred_element_type=jnp.float32,
    )
    lanes = partial_ref.shape[2]
    quarters = rank // lanes
    base = quarters * positions
    for t in range(thought_count):
        block = out_scr[t * positions : (t + 1) * positions, :]
        select_part = block[:, rank:]
        select_high = select_part.astype(jnp.bfloat16)
        select_low = (select_part - select_high.astype(jnp.float32)).astype(jnp.bfloat16)
        for j in range(quarters):
            partial_ref[t, j * positions : (j + 1) * positions, :] = block[
                :, j * lanes : (j + 1) * lanes
            ].astype(jnp.bfloat16)
        partial_ref[t, base : base + positions, 2 * state_twice :] = jnp.zeros(
            (positions, lanes - 2 * state_twice), jnp.bfloat16
        )
        partial_ref[t, base : base + positions, :state_twice] = select_high
        partial_ref[t, base : base + positions, state_twice : 2 * state_twice] = select_low


def project(parent_conv, fork_map, mixer_input, conv_weight, conv_bias, rate_down,
            selection_weight):
    thought_count, positions, width_local = mixer_input.shape
    taps = conv_weight.shape[0]
    rank, state_twice = rate_down.shape[1], selection_weight.shape[1]
    conv_view = jnp.transpose(parent_conv, (1, 0, 2))
    input_view = jnp.transpose(mixer_input, (1, 0, 2))
    select_view = jnp.transpose(selection_weight)
    full = lambda shape: pl.BlockSpec(shape, lambda i, fmap: (0,) * len(shape))
    grid_spec = pltpu.PrefetchScalarGridSpec(
        num_scalar_prefetch=1,
        grid=(1,),
        in_specs=[
            full(conv_view.shape),
            full(input_view.shape),
            full(conv_weight.shape),
            full((1, width_local)),
            full(rate_down.shape),
            full(select_view.shape),
        ],
        out_specs=[
            full(mixer_input.shape),
            full((thought_count, (rank // 128 + 1) * positions, 128)),
        ],
        scratch_shapes=[
            pltpu.VMEM((taps - 1 + positions, width_local), jnp.float32),
            pltpu.VMEM((thought_count * positions, width_local), jnp.float32),
            pltpu.VMEM((thought_count * positions, rank + state_twice), jnp.float32),
        ],
    )
    return pl.pallas_call(
        project_kernel,
        grid_spec=grid_spec,
        out_shape=(
            jax.ShapeDtypeStruct(mixer_input.shape, jnp.bfloat16),
            jax.ShapeDtypeStruct(
                (thought_count, (rank // 128 + 1) * positions, 128), jnp.bfloat16
            ),
        ),
    )(fork_map, conv_view, input_view, conv_weight, conv_bias.reshape(1, width_local),
      rate_down, select_view)


def scan_kernel(
    lens_ref, fmap_ref, rate_ref, drive_ref, gate_ref, b_ref, c_ref, *rest
):
    pair = len(rest) - 6
    h0_refs, (a_ref, skip_ref, packed_ref, r_scr, u_scr, y_scr) = rest[:pair], rest[pair:]
    positions = drive_ref.shape[1]
    state_size = h0_refs[0].shape[1]
    decay = a_ref[...]
    states, lives = [], []
    for k in range(pair):
        live = jnp.clip(lens_ref[pl.program_id(0) * pair + k] + GEN, 0, positions)
        inflow = drive_ref[k].astype(jnp.float32)
        alive = lax.broadcasted_iota(jnp.int32, inflow.shape, 0) < live
        rate = jnp.where(alive, rate_ref[k * positions : (k + 1) * positions, :], 0.0)
        r_scr[k] = rate
        u_scr[k] = rate * inflow
        states.append(h0_refs[k][0])
        lives.append(alive)
    for p in range(positions):
        for k in range(pair):
            b_col = b_ref[k][:, p : p + 1]
            c_col = c_ref[k][:, p : p + 1]
            h = states[k]
            rate_rows = r_scr[k, pl.ds(p, state_size, stride=0), :]
            push_rows = u_scr[k, pl.ds(p, state_size, stride=0), :]
            h = jnp.exp2(rate_rows * decay) * h + push_rows * b_col
            y_scr[k, p : p + 1, :] = jnp.sum(c_col * h, axis=0, keepdims=True)
            states[k] = h
    lanes = packed_ref.shape[2]
    tiles = inflow.shape[1] // lanes
    for k in range(pair):
        inflow = drive_ref[k].astype(jnp.float32)
        gate = gate_ref[k].astype(jnp.float32)
        result = (y_scr[k] + skip_ref[...] * inflow) * jax.nn.silu(gate)
        result = jnp.where(lives[k], result, 0.0)
        for j in range(tiles):
            cols = slice(j * lanes, (j + 1) * lanes)
            base = j * state_size
            packed_ref[k, base : base + state_size, :] = states[k][:, cols].astype(
                packed_ref.dtype
            )
            base = tiles * state_size + j * positions
            packed_ref[k, base : base + positions, :] = result[:, cols].astype(packed_ref.dtype)


def run_scan(judge_lengths, fork_map, step_rate, driven, gate_input, b_t, c_t, parent_state,
             decay_rate, skip_gain):
    thought_count, positions, width_local = driven.shape
    state_size = parent_state.shape[1]
    pair = 4 if thought_count % 4 == 0 else 2
    row_block = lambda t, lens, fmap: (t, 0, 0)
    whole = lambda t, lens, fmap: (0, 0)

    def state_block(k):
        return pl.BlockSpec(
            (1, state_size, width_local), lambda t, lens, fmap: (fmap[t * pair + k], 0, 0)
        )

    grid_spec = pltpu.PrefetchScalarGridSpec(
        num_scalar_prefetch=2,
        grid=(thought_count // pair,),
        in_specs=[
            pl.BlockSpec((pair * positions, width_local), lambda t, lens, fmap: (t, 0)),
            pl.BlockSpec((pair, positions, width_local), row_block),
            pl.BlockSpec((pair, positions, width_local), row_block),
            pl.BlockSpec((pair, state_size, positions), row_block),
            pl.BlockSpec((pair, state_size, positions), row_block),
        ]
        + [state_block(k) for k in range(pair)]
        + [
            pl.BlockSpec((state_size, width_local), whole),
            pl.BlockSpec((1, width_local), whole),
        ],
        out_specs=pl.BlockSpec(
            (pair, (state_size + positions) * width_local // 128, 128), row_block
        ),
        scratch_shapes=[pltpu.VMEM((pair, positions, width_local), jnp.float32)] * 3,
    )
    return pl.pallas_call(
        scan_kernel,
        grid_spec=grid_spec,
        out_shape=jax.ShapeDtypeStruct(
            (thought_count, (state_size + positions) * width_local // 128, 128), jnp.bfloat16
        ),
        compiler_params=pltpu.CompilerParams(dimension_semantics=("arbitrary",)),
    )(judge_lengths, fork_map, step_rate, driven, gate_input, b_t, c_t,
      *([parent_state] * pair), decay_rate, skip_gain.reshape(1, width_local))


def body(
    parent_state,
    parent_conv,
    fork_map,
    judge_lengths,
    mixer_input,
    gate_input,
    conv_weight,
    conv_bias,
    rate_down,
    selection_weight,
    rate_up,
    rate_bias,
    decay_log,
    skip_gain,
):
    thought_count, positions, width_local = mixer_input.shape
    state_size = parent_state.shape[1]
    rank = rate_down.shape[1]
    driven, partial = project(
        parent_conv, fork_map, mixer_input, conv_weight, conv_bias, rate_down, selection_weight
    )
    devices = lax.axis_size("chan")
    pieces = lax.all_to_all(partial, "chan", 0, 0, tiled=True).astype(jnp.float32)
    reduced = jnp.sum(pieces, axis=0)
    quarters = rank // 128
    low_tiles = reduced[: quarters * positions].astype(jnp.bfloat16)
    select_rows = reduced[quarters * positions :]
    select_sum = select_rows[:, : 2 * state_size] + select_rows[:, 2 * state_size : 4 * state_size]
    select_high = select_sum.astype(jnp.bfloat16)
    select_low = (select_sum - select_high.astype(jnp.float32)).astype(jnp.bfloat16)
    spare = jnp.zeros((positions, 128 - 4 * state_size), jnp.bfloat16)
    mine = jnp.concatenate(
        [low_tiles, jnp.concatenate([select_high, select_low, spare], axis=1)], axis=0
    )
    gathered = lax.all_to_all(
        jnp.broadcast_to(mine[None], (devices,) + mine.shape), "chan", 0, 0, tiled=True
    )
    rate_low = jnp.transpose(
        gathered[:, : quarters * positions].reshape(devices, quarters, positions, 128),
        (0, 2, 1, 3),
    ).reshape(devices * positions, rank)
    select_all = gathered[:, quarters * positions :].astype(jnp.float32)
    selection = select_all[:, :, : 2 * state_size] + select_all[:, :, 2 * state_size : 4 * state_size]
    step_rate = jax.nn.softplus(
        jnp.dot(rate_low, rate_up, preferred_element_type=jnp.float32) + rate_bias[None, :]
    )
    b_t = jnp.swapaxes(selection[:, :, :state_size], 1, 2)
    c_t = jnp.swapaxes(selection[:, :, state_size:], 1, 2)
    decay_rate = -jnp.exp(decay_log) * 1.4426950408889634
    packed_local = run_scan(
        judge_lengths, fork_map, step_rate, driven, gate_input, b_t, c_t, parent_state,
        decay_rate, skip_gain,
    )
    received = lax.all_to_all(packed_local, "chan", 0, 0, tiled=True)
    tiles = width_local // 128

    def unpack(start, rows):
        block = received[:, start : start + tiles * rows].reshape(devices, tiles, rows, 128)
        return jnp.transpose(block, (2, 0, 1, 3)).reshape(1, rows, devices * width_local)

    final_state = unpack(0, state_size).astype(jnp.float32)
    mixer_output = unpack(tiles * state_size, positions)
    return (mixer_output, final_state)


def solution(mesh):
    placed = (
        P("group", None, "chan"),
        P("group", None, "chan"),
        P("group"),
        P("group"),
        P("group", None, "chan"),
        P("group", None, "chan"),
        P(None, "chan"),
        P("chan"),
        P("chan", None),
        P("chan", None),
        P(None, "chan"),
        P("chan"),
        P(None, "chan"),
        P("chan"),
    )
    return jax.shard_map(
        body,
        mesh=mesh,
        in_specs=placed,
        out_specs=(P(("group", "chan"), None, None), P(("group", "chan"), None, None)),
        check_vma=False,
    )
```

```python
import jax
import jax.numpy as jnp
from jax import lax
from jax.experimental import pallas as pl
from jax.experimental.pallas import tpu as pltpu
from jax.sharding import PartitionSpec as P

GEN = 4


def project_kernel(
    fmap_ref, conv_ref, input_ref, weight_ref, bias_ref, down_ref, select_ref,
    driven_ref, partial_ref, pad_scr, rows_scr, out_scr
):
    positions, thought_count, _ = input_ref.shape
    taps = weight_ref.shape[0]
    rank = down_ref.shape[1]
    state_twice = select_ref.shape[0]
    tap_weights = weight_ref[...].astype(jnp.float32)
    parents = conv_ref.shape[1]
    row = lax.broadcasted_iota(jnp.int32, (thought_count, parents), 0)
    col = lax.broadcasted_iota(jnp.int32, (thought_count, parents), 1)
    pick = jnp.zeros((thought_count, parents), jnp.float32)
    for t in range(thought_count):
        pick = jnp.where((row == t) & (col == fmap_ref[t]), 1.0, pick)
    pick = pick.astype(jnp.bfloat16)
    starts = [
        jnp.dot(pick, conv_ref[tap], preferred_element_type=jnp.float32)
        for tap in range(taps - 1)
    ]
    for t in range(thought_count):
        for tap in range(taps - 1):
            pad_scr[tap : tap + 1, :] = starts[tap][t : t + 1, :]
        pad_scr[taps - 1 : taps - 1 + positions, :] = input_ref[:, t, :].astype(jnp.float32)
        summed = bias_ref[...] + tap_weights[0:1, :] * pad_scr[0:positions, :]
        for offset in range(1, taps):
            summed = summed + tap_weights[offset : offset + 1, :] * pad_scr[
                offset : offset + positions, :
            ]
        driven = jax.nn.silu(summed).astype(jnp.bfloat16)
        driven_ref[t] = driven
        rows_scr[t * positions : (t + 1) * positions, :] = driven.astype(jnp.float32)
    token_rows = rows_scr[...].astype(jnp.bfloat16)
    out_scr[:, :rank] = jnp.dot(token_rows, down_ref[...], preferred_element_type=jnp.float32)
    out_scr[:, rank:] = lax.dot_general(
        token_rows, select_ref[...], (((1,), (1,)), ((), ())),
        preferred_element_type=jnp.float32,
    )
    lanes = partial_ref.shape[2]
    quarters = rank // lanes
    base = quarters * positions
    for t in range(thought_count):
        block = out_scr[t * positions : (t + 1) * positions, :]
        select_part = block[:, rank:]
        select_high = select_part.astype(jnp.bfloat16)
        select_low = (select_part - select_high.astype(jnp.float32)).astype(jnp.bfloat16)
        for j in range(quarters):
            partial_ref[t, j * positions : (j + 1) * positions, :] = block[
                :, j * lanes : (j + 1) * lanes
            ].astype(jnp.bfloat16)
        partial_ref[t, base : base + positions, 2 * state_twice :] = jnp.zeros(
            (positions, lanes - 2 * state_twice), jnp.bfloat16
        )
        partial_ref[t, base : base + positions, :state_twice] = select_high
        partial_ref[t, base : base + positions, state_twice : 2 * state_twice] = select_low


def project(parent_conv, fork_map, mixer_input, conv_weight, conv_bias, rate_down,
            selection_weight):
    thought_count, positions, width_local = mixer_input.shape
    taps = conv_weight.shape[0]
    rank, state_twice = rate_down.shape[1], selection_weight.shape[1]
    conv_view = jnp.transpose(parent_conv, (1, 0, 2))
    input_view = jnp.transpose(mixer_input, (1, 0, 2))
    select_view = jnp.transpose(selection_weight)
    full = lambda shape: pl.BlockSpec(shape, lambda i, fmap: (0,) * len(shape))
    grid_spec = pltpu.PrefetchScalarGridSpec(
        num_scalar_prefetch=1,
        grid=(1,),
        in_specs=[
            full(conv_view.shape),
            full(input_view.shape),
            full(conv_weight.shape),
            full((1, width_local)),
            full(rate_down.shape),
            full(select_view.shape),
        ],
        out_specs=[
            full(mixer_input.shape),
            full((thought_count, (rank // 128 + 1) * positions, 128)),
        ],
        scratch_shapes=[
            pltpu.VMEM((taps - 1 + positions, width_local), jnp.float32),
            pltpu.VMEM((thought_count * positions, width_local), jnp.float32),
            pltpu.VMEM((thought_count * positions, rank + state_twice), jnp.float32),
        ],
    )
    return pl.pallas_call(
        project_kernel,
        grid_spec=grid_spec,
        out_shape=(
            jax.ShapeDtypeStruct(mixer_input.shape, jnp.bfloat16),
            jax.ShapeDtypeStruct(
                (thought_count, (rank // 128 + 1) * positions, 128), jnp.bfloat16
            ),
        ),
    )(fork_map, conv_view, input_view, conv_weight, conv_bias.reshape(1, width_local),
      rate_down, select_view)


def scan_kernel(
    lens_ref, fmap_ref, rate_ref, drive_ref, gate_ref, b_ref, c_ref, *rest
):
    pair = len(rest) - 6
    h0_refs, (a_ref, skip_ref, packed_ref, r_scr, u_scr, y_scr) = rest[:pair], rest[pair:]
    positions = drive_ref.shape[1]
    state_size = h0_refs[0].shape[1]
    decay = a_ref[...]
    states, lives = [], []
    for k in range(pair):
        live = jnp.clip(lens_ref[pl.program_id(0) * pair + k] + GEN, 0, positions)
        inflow = drive_ref[k].astype(jnp.float32)
        alive = lax.broadcasted_iota(jnp.int32, inflow.shape, 0) < live
        rate = jnp.where(alive, rate_ref[k * positions : (k + 1) * positions, :], 0.0)
        r_scr[k] = rate
        u_scr[k] = rate * inflow
        states.append(h0_refs[k][0])
        lives.append(alive)
    for p in range(positions):
        for k in range(pair):
            b_col = b_ref[k][:, p : p + 1]
            c_col = c_ref[k][:, p : p + 1]
            h = states[k]
            rate_rows = r_scr[k, pl.ds(p, state_size, stride=0), :]
            push_rows = u_scr[k, pl.ds(p, state_size, stride=0), :]
            h = jnp.exp2(rate_rows * decay) * h + push_rows * b_col
            y_scr[k, p : p + 1, :] = jnp.sum(c_col * h, axis=0, keepdims=True)
            states[k] = h
    lanes = packed_ref.shape[2]
    tiles = inflow.shape[1] // lanes
    for k in range(pair):
        inflow = drive_ref[k].astype(jnp.float32)
        gate = gate_ref[k].astype(jnp.float32)
        result = (y_scr[k] + skip_ref[...] * inflow) * jax.nn.silu(gate)
        result = jnp.where(lives[k], result, 0.0)
        for j in range(tiles):
            cols = slice(j * lanes, (j + 1) * lanes)
            base = j * state_size
            packed_ref[k, base : base + state_size, :] = states[k][:, cols].astype(
                packed_ref.dtype
            )
            base = tiles * state_size + j * positions
            packed_ref[k, base : base + positions, :] = result[:, cols].astype(packed_ref.dtype)


def run_scan(judge_lengths, fork_map, step_rate, driven, gate_input, b_t, c_t, parent_state,
             decay_rate, skip_gain):
    thought_count, positions, width_local = driven.shape
    state_size = parent_state.shape[1]
    pair = 4 if thought_count % 4 == 0 else 2
    row_block = lambda t, lens, fmap: (t, 0, 0)
    whole = lambda t, lens, fmap: (0, 0)

    def state_block(k):
        return pl.BlockSpec(
            (1, state_size, width_local), lambda t, lens, fmap: (fmap[t * pair + k], 0, 0)
        )

    grid_spec = pltpu.PrefetchScalarGridSpec(
        num_scalar_prefetch=2,
        grid=(thought_count // pair,),
        in_specs=[
            pl.BlockSpec((pair * positions, width_local), lambda t, lens, fmap: (t, 0)),
            pl.BlockSpec((pair, positions, width_local), row_block),
            pl.BlockSpec((pair, positions, width_local), row_block),
            pl.BlockSpec((pair, state_size, positions), row_block),
            pl.BlockSpec((pair, state_size, positions), row_block),
        ]
        + [state_block(k) for k in range(pair)]
        + [
            pl.BlockSpec((state_size, width_local), whole),
            pl.BlockSpec((1, width_local), whole),
        ],
        out_specs=pl.BlockSpec(
            (pair, (state_size + positions) * width_local // 128, 128), row_block
        ),
        scratch_shapes=[pltpu.VMEM((pair, positions, width_local), jnp.float32)] * 3,
    )
    return pl.pallas_call(
        scan_kernel,
        grid_spec=grid_spec,
        out_shape=jax.ShapeDtypeStruct(
            (thought_count, (state_size + positions) * width_local // 128, 128), jnp.bfloat16
        ),
        compiler_params=pltpu.CompilerParams(dimension_semantics=("arbitrary",)),
    )(judge_lengths, fork_map, step_rate, driven, gate_input, b_t, c_t,
      *([parent_state] * pair), decay_rate, skip_gain.reshape(1, width_local))


def body(
    parent_state,
    parent_conv,
    fork_map,
    judge_lengths,
    mixer_input,
    gate_input,
    conv_weight,
    conv_bias,
    rate_down,
    selection_weight,
    rate_up,
    rate_bias,
    decay_log,
    skip_gain,
):
    thought_count, positions, width_local = mixer_input.shape
    state_size = parent_state.shape[1]
    rank = rate_down.shape[1]
    driven, partial = project(
        parent_conv, fork_map, mixer_input, conv_weight, conv_bias, rate_down, selection_weight
    )
    devices = lax.axis_size("chan")
    pieces = lax.all_to_all(partial, "chan", 0, 0, tiled=True).astype(jnp.float32)
    reduced = jnp.sum(pieces, axis=0)
    quarters = rank // 128
    low_tiles = reduced[: quarters * positions].astype(jnp.bfloat16)
    select_rows = reduced[quarters * positions :]
    select_sum = select_rows[:, : 2 * state_size] + select_rows[:, 2 * state_size : 4 * state_size]
    select_high = select_sum.astype(jnp.bfloat16)
    select_low = (select_sum - select_high.astype(jnp.float32)).astype(jnp.bfloat16)
    spare = jnp.zeros((positions, 128 - 4 * state_size), jnp.bfloat16)
    mine = jnp.concatenate(
        [low_tiles, jnp.concatenate([select_high, select_low, spare], axis=1)], axis=0
    )
    gathered = lax.all_gather(mine, "chan", axis=0)
    rate_low = jnp.transpose(
        gathered[:, : quarters * positions].reshape(devices, quarters, positions, 128),
        (0, 2, 1, 3),
    ).reshape(devices * positions, rank)
    select_all = gathered[:, quarters * positions :].astype(jnp.float32)
    selection = select_all[:, :, : 2 * state_size] + select_all[:, :, 2 * state_size : 4 * state_size]
    step_rate = jax.nn.softplus(
        jnp.dot(rate_low, rate_up, preferred_element_type=jnp.float32) + rate_bias[None, :]
    )
    b_t = jnp.swapaxes(selection[:, :, :state_size], 1, 2)
    c_t = jnp.swapaxes(selection[:, :, state_size:], 1, 2)
    decay_rate = -jnp.exp(decay_log) * 1.4426950408889634
    packed_local = run_scan(
        judge_lengths, fork_map, step_rate, driven, gate_input, b_t, c_t, parent_state,
        decay_rate, skip_gain,
    )
    received = lax.all_to_all(packed_local, "chan", 0, 0, tiled=True)
    tiles = width_local // 128

    def unpack(start, rows):
        block = received[:, start : start + tiles * rows].reshape(devices, tiles, rows, 128)
        return jnp.transpose(block, (2, 0, 1, 3)).reshape(1, rows, devices * width_local)

    final_state = unpack(0, state_size).astype(jnp.float32)
    mixer_output = unpack(tiles * state_size, positions)
    return (mixer_output, final_state)


def solution(mesh):
    placed = (
        P("group", None, "chan"),
        P("group", None, "chan"),
        P("group"),
        P("group"),
        P("group", None, "chan"),
        P("group", None, "chan"),
        P(None, "chan"),
        P("chan"),
        P("chan", None),
        P("chan", None),
        P(None, "chan"),
        P("chan"),
        P(None, "chan"),
        P("chan"),
    )
    return jax.shard_map(
        body,
        mesh=mesh,
        in_specs=placed,
        out_specs=(P(("group", "chan"), None, None), P(("group", "chan"), None, None)),
        check_vma=False,
    )
```
